32 devices in a mesh: group: 2 (over y), seq: 8 (over z, x), chan: 2 (over core).
Axes of the slice: x: 2, y: 2, z: 4, core: 2. Of those that a mesh axis runs over, the one named last changes fastest.
Arguments:
- fresh: bfloat16 [2048, 3, 2048], P(('group', 'seq'), None, 'chan'), parts along dimension 0, may hold values from -6 to 6
- library: bfloat16 [8, 8, 2048], P('seq', None, 'chan'), may hold values from -6 to 6
- block_slot: int32 [8], replicated, may hold values from 0 to 7, each once
- prefix_blocks: int32 [16, 4], P('group'), parts along dimension 0, may hold values from 0 to 7, all different within a row
- short_taps: float32 [3, 3, 2048], P(None, None, 'chan'), may hold values from -4 to 4
- long_filter: float32 [1024, 2048], P('seq', 'chan'), may hold values from -2 to 2
- skip_gain: float32 [2048], P('chan'), may hold values from -6 to 6
Outputs:
- mixed: bfloat16 [2048, 2048], P(('group', 'seq'), 'chan'), parts along dimension 0
The draws below stay inside these ranges and needn't reach their ends.
There are 2 independent parts, one for each index of `group`. The reference program is written for one: setup_inputs(seed, part) draws one part's arguments, and reference() takes and returns one part's arrays. A program takes and returns all parts, laid end to end along the dimension named above; an argument that names none is the same for every part. Nothing has to cross between parts.
Inputs may be any that keep to these rules, and one draw needn't show every extreme that they name: `block_slot`: each number appears once. `prefix_blocks`: every library block is named at least once; the four entries of a row differ.
All inputs are finite; a program needn't handle non-finite values.
Results may differ from the reference program's by a relative error of at most 0.008.
Values may be sent and summed in bfloat16 or wider, within the bound.
No kernel may reach another device: no remote copies, remote signals or barrier semaphores. Data moves between devices by JAX's collectives and lax.ppermute only.
A program may use at most 64 MiB of HBM per device.

```python
import math
import jax
import jax.numpy as jnp
from jax import lax

CHANNELS = 2048
TAPS = 3
BLK = 8
TOKENS = 1024
LIB_BLOCKS = 8
PREFIX_BLOCKS = 32


def draw_long_filter(key, part):
    share = 0.5
    chooser = jax.random.uniform(jax.random.fold_in(key, 11), (CHANNELS,), jnp.float32)
    slow_level = jax.random.uniform(jax.random.fold_in(key, 12), (CHANNELS,), jnp.float32, math.log(0.3 / TOKENS), math.log(2.0 / TOKENS))
    fast_level = jax.random.uniform(jax.random.fold_in(key, 13), (CHANNELS,), jnp.float32, math.log(1.0 / 48.0), math.log(1.0 / 24.0))
    rate = jnp.where(chooser < share, jnp.exp(slow_level), jnp.exp(fast_level))
    noise = jax.random.uniform(jax.random.fold_in(key, 14), (TOKENS, CHANNELS), jnp.float32, -1.0, 1.0) * math.sqrt(3.0)
    rough = jax.random.uniform(jax.random.fold_in(key, 15), (TOKENS, CHANNELS), jnp.float32, 0.5, 1.5)
    times = jnp.arange(TOKENS).astype(jnp.float32)[:, None]
    envelope = jnp.sqrt(2.0 * rate)[None, :] * jnp.exp(-rate[None, :] * times)
    values = noise * rough * envelope
    return jnp.clip(values, -2.0, 2.0).astype(jnp.float32)


def steps_of(key, shape, shards, low, high):
    level, own = 1.0, jax.random.fold_in(key, 6)
    for dim, shards_of in shards:
        steps = jnp.exp(jax.random.uniform(jax.random.fold_in(own, dim), (shards_of,), jnp.float32, low / len(shards), high / len(shards)))
        level = level * jnp.repeat(steps, shape[dim] // shards_of).reshape([-1 if axis == dim else 1 for axis in range(len(shape))])
    return level


def different_ones(key, rows, number_of, top, lift):
    order = jax.random.permutation(jax.random.fold_in(key, 1), number_of)
    pull = order
    for power in range(3):
        pull = pull * pull // number_of
    pull = pull * lift // number_of
    tickets = jax.random.randint(jax.random.fold_in(key, 2), (rows, number_of), 0, 4096) + pull
    fixed_rows = jax.random.permutation(jax.random.fold_in(key, 3), rows)[jnp.arange(number_of) % rows]
    tickets = jnp.where(jnp.arange(rows)[:, None] == fixed_rows[None, :], 1 << 14, tickets)
    score = tickets * number_of + jnp.arange(number_of)
    return lax.top_k(score.astype(jnp.int32), top)[1].astype(jnp.int32)


def scatter_about(stream_key, extent, spread, limit, shards=(), dtype=jnp.bfloat16):
    entries = spread * jax.random.normal(stream_key, extent, jnp.float32)
    if shards:
        entries = entries * steps_of(stream_key, extent, shards, -0.22, 0.18)
    return jnp.clip(entries, -limit, limit).astype(dtype)


def setup_inputs(seed: int = 0, part: int = 0) -> dict:
    arg_keys = jax.random.split(jax.random.key(seed), 8)
    own_keys = jax.random.split(jax.random.fold_in(arg_keys[7], part), 8)
    return {
        "fresh": scatter_about(own_keys[0], (TOKENS, 3, CHANNELS), 1.0, 6.0, ((0, 8), (2, 2))),
        "library": scatter_about(arg_keys[1], (LIB_BLOCKS, BLK, CHANNELS), 1.0, 6.0, ((0, 8), (2, 2))),
        "block_slot": jax.random.permutation(arg_keys[2], LIB_BLOCKS).astype(jnp.int32),
        "prefix_blocks": different_ones(own_keys[3], (PREFIX_BLOCKS // 4), LIB_BLOCKS, 4, 8192),
        "short_taps": scatter_about(arg_keys[4], (TAPS, 3, CHANNELS), 0.6, 4.0, ((2, 2),), jnp.float32),
        "long_filter": draw_long_filter(jax.random.fold_in(arg_keys[7], 71), part),
        "skip_gain": scatter_about(arg_keys[6], (CHANNELS,), 1.0, 6.0, ((0, 2),), jnp.float32),
    }


def reference(fresh, library, block_slot, prefix_blocks, short_taps, long_filter, skip_gain):
    slot_ids = block_slot[prefix_blocks.reshape(-1)]
    prefix_len = slot_ids.shape[0] * BLK
    cached = library[slot_ids].reshape(prefix_len, CHANNELS)
    values = jnp.concatenate([cached, fresh[prefix_len:, 2]], axis=0)
    stacked = jnp.stack([fresh[:, 0], fresh[:, 1], values], axis=1).astype(jnp.float32)
    shortened = jnp.zeros(stacked.shape, jnp.float32)
    for offset in range(TAPS):
        shifted = jnp.pad(stacked[:TOKENS - offset], ((offset, 0), (0, 0), (0, 0)))
        shortened = shortened + short_taps[offset][None] * shifted
    gating = shortened[:, 0]
    mixed_in = shortened[:, 1] * shortened[:, 2]
    block_width = math.gcd(CHANNELS, 256)
    block_count = CHANNELS // block_width
    fft_length = 2 * TOKENS

    def convolve(operands):
        signal, impulse = operands
        product = jnp.fft.rfft(signal, n=fft_length, axis=0) * jnp.fft.rfft(impulse, n=fft_length, axis=0)
        return jnp.fft.irfft(product, n=fft_length, axis=0)[:TOKENS]

    signals = mixed_in.reshape(TOKENS, block_count, block_width).transpose(1, 0, 2)
    filters = long_filter.reshape(TOKENS, block_count, block_width).transpose(1, 0, 2)
    convolved = lax.map(convolve, (signals, filters))
    convolved = convolved.transpose(1, 0, 2).reshape(TOKENS, CHANNELS)
    output = gating * (convolved + skip_gain[None, :] * mixed_in)
    return output.astype(jnp.bfloat16)
```

```python
import math

import jax
import jax.numpy as jnp
from jax import lax
from jax.sharding import PartitionSpec as P

TAPS = 3
BLK = 8


def from_behind(shard, axis, by):
    count = lax.axis_size(axis)
    pairs = [(i, i + by) for i in range(count) if 0 <= i + by < count]
    return lax.ppermute(shard, axis, pairs)


def exact_dot(pattern, matrix, tensor):
    return jnp.einsum(pattern, matrix, tensor, precision=lax.Precision.HIGHEST)


def turn_angles(numbers, period):
    return (numbers % period).astype(jnp.float32) * (2.0 * math.pi / period)


def ring_body(fresh, library, block_slot, prefix_blocks, short_taps, long_filter, skip_gain):
    row_count = fresh.shape[0]
    channels = fresh.shape[2]
    devices = lax.axis_size("seq")
    seq_index = lax.axis_index("seq")
    group_rows = row_count // devices
    period = 2 * row_count * devices
    block_ids = jnp.arange(devices, dtype=jnp.int32)
    mode_ids = jnp.arange(2 * devices, dtype=jnp.int32)
    coarse = turn_angles(mode_ids[:, None] * block_ids[None, :], 2 * devices)
    cos_q = jnp.cos(coarse)
    sin_q = jnp.sin(coarse)
    local_rows = seq_index * group_rows + jnp.arange(group_rows, dtype=jnp.int32)
    twist = turn_angles(mode_ids[:, None] * local_rows[None, :], period)
    twist_cos = jnp.cos(twist)[:, :, None]
    twist_sin = jnp.sin(twist)[:, :, None]
    row_ids = jnp.arange(row_count, dtype=jnp.int32)
    fine_angles = turn_angles(row_ids[:, None] * row_ids[None, :], row_count)
    cos_m = jnp.cos(fine_angles)
    sin_m = jnp.sin(fine_angles)
    first_modes = 2 * seq_index + jnp.arange(2, dtype=jnp.int32)
    back_twist = turn_angles(first_modes[:, None] * row_ids[None, :], period)
    back_cos = jnp.cos(back_twist)[:, :, None]
    back_sin = jnp.sin(back_twist)[:, :, None]

    def to_modes(column):
        real_part = exact_dot("kq,qgc->kgc", cos_q, column)
        imag_part = -exact_dot("kq,qgc->kgc", sin_q, column)
        return jnp.stack(
            [
                real_part * twist_cos + imag_part * twist_sin,
                imag_part * twist_cos - real_part * twist_sin,
            ]
        )

    def to_spectrum(spread):
        real_part = exact_dot("ki,jic->jkc", cos_m, spread[0]) + exact_dot(
            "ki,jic->jkc", sin_m, spread[1]
        )
        imag_part = exact_dot("ki,jic->jkc", cos_m, spread[1]) - exact_dot(
            "ki,jic->jkc", sin_m, spread[0]
        )
        return (real_part, imag_part)

    blocks_here = row_count // BLK
    flat_ids = prefix_blocks.reshape(-1)
    first_block = jnp.minimum(seq_index * blocks_here, flat_ids.shape[0] - blocks_here)
    own_ids = lax.dynamic_slice_in_dim(flat_ids, first_block, blocks_here)
    matches = own_ids[:, None] == jnp.arange(block_slot.shape[0], dtype=jnp.int32)[None, :]
    wanted = jnp.sum(jnp.where(matches, block_slot[None, :], 0), axis=1)
    shards = lax.all_gather(library, "seq", axis=0, tiled=True)
    picker = (wanted[:, None] == jnp.arange(shards.shape[0], dtype=jnp.int32)[None, :]).astype(
        jnp.bfloat16
    )
    gathered = jnp.einsum("bn,nlc->blc", picker, shards, preferred_element_type=jnp.float32)
    cached = gathered.reshape(row_count, channels).astype(jnp.bfloat16)
    values = jnp.where(seq_index < devices // 4, cached, fresh[:, 2])
    stacked = jnp.concatenate([fresh[:, :2], values[:, None]], axis=1)
    previous = from_behind(stacked[row_count - (TAPS - 1) :], "seq", 1)
    extended = jnp.concatenate([previous, stacked], axis=0)
    shortened = jnp.zeros((row_count, 3, channels), jnp.float32)
    for offset in range(TAPS):
        window_start = TAPS - 1 - offset
        shortened = shortened + short_taps[offset][None] * extended[
            window_start : window_start + row_count
        ].astype(jnp.float32)
    gating = shortened[:, 0]
    signal = shortened[:, 1] * shortened[:, 2]
    spread_signal = to_modes(
        lax.all_to_all(signal[None], "seq", split_axis=1, concat_axis=0, tiled=True)
    )
    spread_taps = to_modes(
        lax.all_to_all(long_filter[None], "seq", split_axis=1, concat_axis=0, tiled=True)
    )
    moved_signal, moved_taps = (
        lax.all_to_all(
            spread_signal.astype(jnp.bfloat16), "seq", split_axis=1, concat_axis=2, tiled=True
        ).astype(spread_signal.dtype),
        lax.all_to_all(
            spread_taps.astype(jnp.bfloat16), "seq", split_axis=1, concat_axis=2, tiled=True
        ).astype(spread_taps.dtype),
    )
    sig_real, sig_imag = to_spectrum(moved_signal)
    tap_real, tap_imag = to_spectrum(moved_taps)
    prod_real = sig_real * tap_real - sig_imag * tap_imag
    prod_imag = sig_real * tap_imag + sig_imag * tap_real
    back_real = exact_dot("ki,jic->jkc", cos_m, prod_real) - exact_dot(
        "ki,jic->jkc", sin_m, prod_imag
    )
    back_imag = exact_dot("ki,jic->jkc", cos_m, prod_imag) + exact_dot(
        "ki,jic->jkc", sin_m, prod_real
    )
    turned = jnp.stack(
        [back_real * back_cos - back_imag * back_sin, back_imag * back_cos + back_real * back_sin]
    )
    spread = lax.all_to_all(turned, "seq", split_axis=2, concat_axis=1, tiled=True)
    positions = (
        exact_dot("kq,kgc->qgc", cos_q, spread[0]) - exact_dot("kq,kgc->qgc", sin_q, spread[1])
    ) / period
    convolved = lax.all_to_all(positions, "seq", split_axis=0, concat_axis=1, tiled=True)[0]
    output = gating * (convolved + skip_gain[None, :] * signal)
    return output.astype(jnp.bfloat16)


def dft_tables(tokens):
    period = 2 * tokens
    width = 1
    while width * width < tokens:
        width *= 2
    outer = tokens // width
    freqs = jnp.arange(tokens + 1, dtype=jnp.int32)[:, None]
    coarse = turn_angles(freqs * (width * jnp.arange(outer, dtype=jnp.int32))[None, :], period)
    fine = turn_angles(freqs * jnp.arange(width, dtype=jnp.int32)[None, :], period)
    c1, s1 = jnp.cos(coarse)[:, :, None], jnp.sin(coarse)[:, :, None]
    c2, s2 = jnp.cos(fine)[:, None, :], jnp.sin(fine)[:, None, :]
    cos_t = (c1 * c2 - s1 * s2).reshape(tokens + 1, tokens)
    sin_t = (s1 * c2 + c1 * s2).reshape(tokens + 1, tokens)
    return cos_t, sin_t


def local_body(fresh, library, block_slot, prefix_blocks, short_taps, long_filter, skip_gain):
    row_count, _, channels = fresh.shape
    devices = lax.axis_size("seq")
    seq_index = lax.axis_index("seq")
    tokens = row_count * devices
    own = channels // devices
    lib_here = library.shape[0]
    lib_rows = lib_here * BLK // 4
    packed = jnp.concatenate([fresh, long_filter.astype(jnp.bfloat16)[:, None, :]], axis=1)
    packed = jnp.concatenate([packed, library.reshape(lib_rows, 4, channels)], axis=0)
    moved = lax.all_to_all(packed, "seq", split_axis=2, concat_axis=0, tiled=True)
    moved = moved.reshape(devices, row_count + lib_rows, 4, own)
    rows = moved[:, :row_count].reshape(tokens, 4, own)
    lib_all = moved[:, row_count:].reshape(devices * lib_here, BLK * own)

    slot_ids = block_slot[prefix_blocks.reshape(-1)]
    prefix_len = slot_ids.shape[0] * BLK
    picker = (slot_ids[:, None] == jnp.arange(lib_all.shape[0], dtype=jnp.int32)[None, :]).astype(
        jnp.bfloat16
    )
    cached = jnp.dot(picker, lib_all, preferred_element_type=jnp.float32)
    cached = cached.reshape(prefix_len, own).astype(jnp.bfloat16)
    values = jnp.concatenate([cached, rows[prefix_len:, 2]], axis=0)
    stacked = jnp.concatenate([rows[:, :2], values[:, None]], axis=1).astype(jnp.float32)

    taps = lax.dynamic_slice_in_dim(short_taps, seq_index * own, own, axis=2)
    gain = lax.dynamic_slice_in_dim(skip_gain, seq_index * own, own, axis=0)
    shortened = jnp.zeros((tokens, 3, own), jnp.float32)
    for offset in range(TAPS):
        shifted = jnp.pad(stacked[: tokens - offset], ((offset, 0), (0, 0), (0, 0)))
        shortened = shortened + taps[offset][None] * shifted
    gating = shortened[:, 0]
    signal = shortened[:, 1] * shortened[:, 2]

    cos_t, sin_t = dft_tables(tokens)
    table = jnp.concatenate([cos_t, sin_t], axis=0).astype(jnp.bfloat16)
    operands = jnp.concatenate([signal.astype(jnp.bfloat16), rows[:, 3]], axis=1)
    spec = jnp.dot(table, operands, preferred_element_type=jnp.float32)
    bins = tokens + 1
    sig_c, tap_c = spec[:bins, :own], spec[:bins, own:]
    sig_s, tap_s = spec[bins:, :own], spec[bins:, own:]
    weight = jnp.where(
        (jnp.arange(bins) == 0) | (jnp.arange(bins) == tokens), 1.0, 2.0
    ).astype(jnp.float32)[:, None] / (2 * tokens)
    real = (sig_c * tap_c - sig_s * tap_s) * weight
    turned = (sig_c * tap_s + sig_s * tap_c) * weight
    back = jnp.concatenate([real, turned], axis=0).astype(jnp.bfloat16)
    convolved = lax.dot_general(
        table, back, (((0,), (0,)), ((), ())), preferred_element_type=jnp.float32
    )
    output = (gating * (convolved + gain[None, :] * signal)).astype(jnp.bfloat16)
    return lax.all_to_all(output, "seq", split_axis=0, concat_axis=1, tiled=True)


def body(fresh, library, *rest):
    devices = lax.axis_size("seq")
    tokens = fresh.shape[0] * devices
    fits = tokens <= 4096 and fresh.shape[2] % devices == 0 and (library.shape[0] * BLK) % 4 == 0
    if fits:
        return local_body(fresh, library, *rest)
    return ring_body(fresh, library, *rest)


def solution(mesh):
    return jax.shard_map(
        body,
        mesh=mesh,
        in_specs=(
            P(("group", "seq"), None, "chan"),
            P("seq", None, "chan"),
            P(),
            P("group", None),
            P(None, None, "chan"),
            P("seq", "chan"),
            P("chan"),
        ),
        out_specs=P(("group", "seq"), "chan"),
        check_vma=False,
    )
```

```python
import math

import jax
import jax.numpy as jnp
from jax import lax
from jax.sharding import PartitionSpec as P

TAPS = 3
BLK = 8


def from_behind(shard, axis, by):
    count = lax.axis_size(axis)
    pairs = [(i, i + by) for i in range(count) if 0 <= i + by < count]
    return lax.ppermute(shard, axis, pairs)


def exact_dot(pattern, matrix, tensor):
    return jnp.einsum(pattern, matrix, tensor, precision=lax.Precision.HIGHEST)


def turn_angles(numbers, period):
    return (numbers % period).astype(jnp.float32) * (2.0 * math.pi / period)


def ring_body(fresh, library, block_slot, prefix_blocks, short_taps, long_filter, skip_gain):
    row_count = fresh.shape[0]
    channels = fresh.shape[2]
    devices = lax.axis_size("seq")
    seq_index = lax.axis_index("seq")
    group_rows = row_count // devices
    period = 2 * row_count * devices
    block_ids = jnp.arange(devices, dtype=jnp.int32)
    mode_ids = jnp.arange(2 * devices, dtype=jnp.int32)
    coarse = turn_angles(mode_ids[:, None] * block_ids[None, :], 2 * devices)
    cos_q = jnp.cos(coarse)
    sin_q = jnp.sin(coarse)
    local_rows = seq_index * group_rows + jnp.arange(group_rows, dtype=jnp.int32)
    twist = turn_angles(mode_ids[:, None] * local_rows[None, :], period)
    twist_cos = jnp.cos(twist)[:, :, None]
    twist_sin = jnp.sin(twist)[:, :, None]
    row_ids = jnp.arange(row_count, dtype=jnp.int32)
    fine_angles = turn_angles(row_ids[:, None] * row_ids[None, :], row_count)
    cos_m = jnp.cos(fine_angles)
    sin_m = jnp.sin(fine_angles)
    first_modes = 2 * seq_index + jnp.arange(2, dtype=jnp.int32)
    back_twist = turn_angles(first_modes[:, None] * row_ids[None, :], period)
    back_cos = jnp.cos(back_twist)[:, :, None]
    back_sin = jnp.sin(back_twist)[:, :, None]

    def to_modes(column):
        real_part = exact_dot("kq,qgc->kgc", cos_q, column)
        imag_part = -exact_dot("kq,qgc->kgc", sin_q, column)
        return jnp.stack(
            [
                real_part * twist_cos + imag_part * twist_sin,
                imag_part * twist_cos - real_part * twist_sin,
            ]
        )

    def to_spectrum(spread):
        real_part = exact_dot("ki,jic->jkc", cos_m, spread[0]) + exact_dot(
            "ki,jic->jkc", sin_m, spread[1]
        )
        imag_part = exact_dot("ki,jic->jkc", cos_m, spread[1]) - exact_dot(
            "ki,jic->jkc", sin_m, spread[0]
        )
        return (real_part, imag_part)

    blocks_here = row_count // BLK
    flat_ids = prefix_blocks.reshape(-1)
    first_block = jnp.minimum(seq_index * blocks_here, flat_ids.shape[0] - blocks_here)
    own_ids = lax.dynamic_slice_in_dim(flat_ids, first_block, blocks_here)
    matches = own_ids[:, None] == jnp.arange(block_slot.shape[0], dtype=jnp.int32)[None, :]
    wanted = jnp.sum(jnp.where(matches, block_slot[None, :], 0), axis=1)
    shards = lax.all_gather(library, "seq", axis=0, tiled=True)
    picker = (wanted[:, None] == jnp.arange(shards.shape[0], dtype=jnp.int32)[None, :]).astype(
        jnp.bfloat16
    )
    gathered = jnp.einsum("bn,nlc->blc", picker, shards, preferred_element_type=jnp.float32)
    cached = gathered.reshape(row_count, channels).astype(jnp.bfloat16)
    values = jnp.where(seq_index < devices // 4, cached, fresh[:, 2])
    stacked = jnp.concatenate([fresh[:, :2], values[:, None]], axis=1)
    previous = from_behind(stacked[row_count - (TAPS - 1) :], "seq", 1)
    extended = jnp.concatenate([previous, stacked], axis=0)
    shortened = jnp.zeros((row_count, 3, channels), jnp.float32)
    for offset in range(TAPS):
        window_start = TAPS - 1 - offset
        shortened = shortened + short_taps[offset][None] * extended[
            window_start : window_start + row_count
        ].astype(jnp.float32)
    gating = shortened[:, 0]
    signal = shortened[:, 1] * shortened[:, 2]
    spread_signal = to_modes(
        lax.all_to_all(signal[None], "seq", split_axis=1, concat_axis=0, tiled=True)
    )
    spread_taps = to_modes(
        lax.all_to_all(long_filter[None], "seq", split_axis=1, concat_axis=0, tiled=True)
    )
    moved_signal, moved_taps = (
        lax.all_to_all(
            spread_signal.astype(jnp.bfloat16), "seq", split_axis=1, concat_axis=2, tiled=True
        ).astype(spread_signal.dtype),
        lax.all_to_all(
            spread_taps.astype(jnp.bfloat16), "seq", split_axis=1, concat_axis=2, tiled=True
        ).astype(spread_taps.dtype),
    )
    sig_real, sig_imag = to_spectrum(moved_signal)
    tap_real, tap_imag = to_spectrum(moved_taps)
    prod_real = sig_real * tap_real - sig_imag * tap_imag
    prod_imag = sig_real * tap_imag + sig_imag * tap_real
    back_real = exact_dot("ki,jic->jkc", cos_m, prod_real) - exact_dot(
        "ki,jic->jkc", sin_m, prod_imag
    )
    back_imag = exact_dot("ki,jic->jkc", cos_m, prod_imag) + exact_dot(
        "ki,jic->jkc", sin_m, prod_real
    )
    turned = jnp.stack(
        [back_real * back_cos - back_imag * back_sin, back_imag * back_cos + back_real * back_sin]
    )
    spread = lax.all_to_all(turned, "seq", split_axis=2, concat_axis=1, tiled=True)
    positions = (
        exact_dot("kq,kgc->qgc", cos_q, spread[0]) - exact_dot("kq,kgc->qgc", sin_q, spread[1])
    ) / period
    convolved = lax.all_to_all(positions, "seq", split_axis=0, concat_axis=1, tiled=True)[0]
    output = gating * (convolved + skip_gain[None, :] * signal)
    return output.astype(jnp.bfloat16)


def dft_tables(tokens):
    period = 2 * tokens
    width = 1
    while width * width < tokens:
        width *= 2
    outer = tokens // width
    freqs = jnp.arange(tokens + 1, dtype=jnp.int32)[:, None]
    coarse = turn_angles(freqs * (width * jnp.arange(outer, dtype=jnp.int32))[None, :], period)
    fine = turn_angles(freqs * jnp.arange(width, dtype=jnp.int32)[None, :], period)
    c1, s1 = jnp.cos(coarse)[:, :, None], jnp.sin(coarse)[:, :, None]
    c2, s2 = jnp.cos(fine)[:, None, :], jnp.sin(fine)[:, None, :]
    cos_t = (c1 * c2 - s1 * s2).reshape(tokens + 1, tokens)
    sin_t = (s1 * c2 + c1 * s2).reshape(tokens + 1, tokens)
    return cos_t, sin_t


def local_body(fresh, library, block_slot, prefix_blocks, short_taps, long_filter, skip_gain):
    row_count, _, channels = fresh.shape
    devices = lax.axis_size("seq")
    seq_index = lax.axis_index("seq")
    tokens = row_count * devices
    own = channels // devices
    lib_here = library.shape[0]
    lib_rows = lib_here * BLK // 4
    packed = jnp.concatenate([fresh, long_filter.astype(jnp.bfloat16)[:, None, :]], axis=1)
    packed = jnp.concatenate([packed, library.reshape(lib_rows, 4, channels)], axis=0)
    packed = packed.reshape(row_count + lib_rows, 4, devices, own).transpose(2, 0, 1, 3)
    moved = lax.all_to_all(packed, "seq", split_axis=0, concat_axis=0, tiled=True)
    rows = moved[:, :row_count].reshape(tokens, 4, own)
    lib_all = moved[:, row_count:].reshape(devices * lib_here, BLK * own)

    slot_ids = block_slot[prefix_blocks.reshape(-1)]
    prefix_len = slot_ids.shape[0] * BLK
    picker = (slot_ids[:, None] == jnp.arange(lib_all.shape[0], dtype=jnp.int32)[None, :]).astype(
        jnp.bfloat16
    )
    cached = jnp.dot(picker, lib_all, preferred_element_type=jnp.float32)
    cached = cached.reshape(prefix_len, own).astype(jnp.bfloat16)
    values = jnp.concatenate([cached, rows[prefix_len:, 2]], axis=0)
    stacked = jnp.concatenate([rows[:, :2], values[:, None]], axis=1).astype(jnp.float32)

    taps = lax.dynamic_slice_in_dim(short_taps, seq_index * own, own, axis=2)
    gain = lax.dynamic_slice_in_dim(skip_gain, seq_index * own, own, axis=0)
    shortened = jnp.zeros((tokens, 3, own), jnp.float32)
    for offset in range(TAPS):
        shifted = jnp.pad(stacked[: tokens - offset], ((offset, 0), (0, 0), (0, 0)))
        shortened = shortened + taps[offset][None] * shifted
    gating = shortened[:, 0]
    signal = shortened[:, 1] * shortened[:, 2]

    cos_t, sin_t = dft_tables(tokens)
    table = jnp.concatenate([cos_t, sin_t], axis=0).astype(jnp.bfloat16)
    operands = jnp.concatenate([signal.astype(jnp.bfloat16), rows[:, 3]], axis=1)
    spec = jnp.dot(table, operands, preferred_element_type=jnp.float32)
    bins = tokens + 1
    sig_c, tap_c = spec[:bins, :own], spec[:bins, own:]
    sig_s, tap_s = spec[bins:, :own], spec[bins:, own:]
    weight = jnp.where(
        (jnp.arange(bins) == 0) | (jnp.arange(bins) == tokens), 1.0, 2.0
    ).astype(jnp.float32)[:, None] / (2 * tokens)
    real = (sig_c * tap_c - sig_s * tap_s) * weight
    turned = (sig_c * tap_s + sig_s * tap_c) * weight
    back = jnp.concatenate([real, turned], axis=0).astype(jnp.bfloat16)
    convolved = lax.dot_general(
        table, back, (((0,), (0,)), ((), ())), preferred_element_type=jnp.float32
    )
    output = (gating * (convolved + gain[None, :] * signal)).astype(jnp.bfloat16)
    output = lax.all_to_all(
        output.reshape(devices, row_count, own), "seq", split_axis=0, concat_axis=0, tiled=True
    )
    return output.transpose(1, 0, 2).reshape(row_count, channels)


def body(fresh, library, *rest):
    devices = lax.axis_size("seq")
    tokens = fresh.shape[0] * devices
    fits = tokens <= 4096 and fresh.shape[2] % devices == 0 and (library.shape[0] * BLK) % 4 == 0
    if fits:
        return local_body(fresh, library, *rest)
    return ring_body(fresh, library, *rest)


def solution(mesh):
    return jax.shard_map(
        body,
        mesh=mesh,
        in_specs=(
            P(("group", "seq"), None, "chan"),
            P("seq", None, "chan"),
            P(),
            P("group", None),
            P(None, None, "chan"),
            P("seq", "chan"),
            P("chan"),
        ),
        out_specs=P(("group", "seq"), "chan"),
        check_vma=False,
    )
```

```python
import math

import jax
import jax.numpy as jnp
from jax import lax
from jax.sharding import PartitionSpec as P

TAPS = 3
BLK = 8


def from_behind(shard, axis, by):
    count = lax.axis_size(axis)
    pairs = [(i, i + by) for i in range(count) if 0 <= i + by < count]
    return lax.ppermute(shard, axis, pairs)


def exact_dot(pattern, matrix, tensor):
    return jnp.einsum(pattern, matrix, tensor, precision=lax.Precision.HIGHEST)


def turn_angles(numbers, period):
    return (numbers % period).astype(jnp.float32) * (2.0 * math.pi / period)


def ring_body(fresh, library, block_slot, prefix_blocks, short_taps, long_filter, skip_gain):
    row_count = fresh.shape[0]
    channels = fresh.shape[2]
    devices = lax.axis_size("seq")
    seq_index = lax.axis_index("seq")
    group_rows = row_count // devices
    period = 2 * row_count * devices
    block_ids = jnp.arange(devices, dtype=jnp.int32)
    mode_ids = jnp.arange(2 * devices, dtype=jnp.int32)
    coarse = turn_angles(mode_ids[:, None] * block_ids[None, :], 2 * devices)
    cos_q = jnp.cos(coarse)
    sin_q = jnp.sin(coarse)
    local_rows = seq_index * group_rows + jnp.arange(group_rows, dtype=jnp.int32)
    twist = turn_angles(mode_ids[:, None] * local_rows[None, :], period)
    twist_cos = jnp.cos(twist)[:, :, None]
    twist_sin = jnp.sin(twist)[:, :, None]
    row_ids = jnp.arange(row_count, dtype=jnp.int32)
    fine_angles = turn_angles(row_ids[:, None] * row_ids[None, :], row_count)
    cos_m = jnp.cos(fine_angles)
    sin_m = jnp.sin(fine_angles)
    first_modes = 2 * seq_index + jnp.arange(2, dtype=jnp.int32)
    back_twist = turn_angles(first_modes[:, None] * row_ids[None, :], period)
    back_cos = jnp.cos(back_twist)[:, :, None]
    back_sin = jnp.sin(back_twist)[:, :, None]

    def to_modes(column):
        real_part = exact_dot("kq,qgc->kgc", cos_q, column)
        imag_part = -exact_dot("kq,qgc->kgc", sin_q, column)
        return jnp.stack(
            [
                real_part * twist_cos + imag_part * twist_sin,
                imag_part * twist_cos - real_part * twist_sin,
            ]
        )

    def to_spectrum(spread):
        real_part = exact_dot("ki,jic->jkc", cos_m, spread[0]) + exact_dot(
            "ki,jic->jkc", sin_m, spread[1]
        )
        imag_part = exact_dot("ki,jic->jkc", cos_m, spread[1]) - exact_dot(
            "ki,jic->jkc", sin_m, spread[0]
        )
        return (real_part, imag_part)

    blocks_here = row_count // BLK
    flat_ids = prefix_blocks.reshape(-1)
    first_block = jnp.minimum(seq_index * blocks_here, flat_ids.shape[0] - blocks_here)
    own_ids = lax.dynamic_slice_in_dim(flat_ids, first_block, blocks_here)
    matches = own_ids[:, None] == jnp.arange(block_slot.shape[0], dtype=jnp.int32)[None, :]
    wanted = jnp.sum(jnp.where(matches, block_slot[None, :], 0), axis=1)
    shards = lax.all_gather(library, "seq", axis=0, tiled=True)
    picker = (wanted[:, None] == jnp.arange(shards.shape[0], dtype=jnp.int32)[None, :]).astype(
        jnp.bfloat16
    )
    gathered = jnp.einsum("bn,nlc->blc", picker, shards, preferred_element_type=jnp.float32)
    cached = gathered.reshape(row_count, channels).astype(jnp.bfloat16)
    values = jnp.where(seq_index < devices // 4, cached, fresh[:, 2])
    stacked = jnp.concatenate([fresh[:, :2], values[:, None]], axis=1)
    previous = from_behind(stacked[row_count - (TAPS - 1) :], "seq", 1)
    extended = jnp.concatenate([previous, stacked], axis=0)
    shortened = jnp.zeros((row_count, 3, channels), jnp.float32)
    for offset in range(TAPS):
        window_start = TAPS - 1 - offset
        shortened = shortened + short_taps[offset][None] * extended[
            window_start : window_start + row_count
        ].astype(jnp.float32)
    gating = shortened[:, 0]
    signal = shortened[:, 1] * shortened[:, 2]
    spread_signal = to_modes(
        lax.all_to_all(signal[None], "seq", split_axis=1, concat_axis=0, tiled=True)
    )
    spread_taps = to_modes(
        lax.all_to_all(long_filter[None], "seq", split_axis=1, concat_axis=0, tiled=True)
    )
    moved_signal, moved_taps = (
        lax.all_to_all(
            spread_signal.astype(jnp.bfloat16), "seq", split_axis=1, concat_axis=2, tiled=True
        ).astype(spread_signal.dtype),
        lax.all_to_all(
            spread_taps.astype(jnp.bfloat16), "seq", split_axis=1, concat_axis=2, tiled=True
        ).astype(spread_taps.dtype),
    )
    sig_real, sig_imag = to_spectrum(moved_signal)
    tap_real, tap_imag = to_spectrum(moved_taps)
    prod_real = sig_real * tap_real - sig_imag * tap_imag
    prod_imag = sig_real * tap_imag + sig_imag * tap_real
    back_real = exact_dot("ki,jic->jkc", cos_m, prod_real) - exact_dot(
        "ki,jic->jkc", sin_m, prod_imag
    )
    back_imag = exact_dot("ki,jic->jkc", cos_m, prod_imag) + exact_dot(
        "ki,jic->jkc", sin_m, prod_real
    )
    turned = jnp.stack(
        [back_real * back_cos - back_imag * back_sin, back_imag * back_cos + back_real * back_sin]
    )
    spread = lax.all_to_all(turned, "seq", split_axis=2, concat_axis=1, tiled=True)
    positions = (
        exact_dot("kq,kgc->qgc", cos_q, spread[0]) - exact_dot("kq,kgc->qgc", sin_q, spread[1])
    ) / period
    convolved = lax.all_to_all(positions, "seq", split_axis=0, concat_axis=1, tiled=True)[0]
    output = gating * (convolved + skip_gain[None, :] * signal)
    return output.astype(jnp.bfloat16)


def exchange(chunk_of, devices):
    seq_index = lax.axis_index("seq")
    arrived = []
    for shift in range(devices):
        block = chunk_of(lax.rem(seq_index + shift, devices))
        if shift:
            block = lax.ppermute(
                block, "seq", [(i, (i + shift) % devices) for i in range(devices)]
            )
        arrived.append(block)
    turned = jnp.stack(arrived[::-1] * 2)
    start = lax.rem(devices - 1 - seq_index + devices, devices)
    return lax.dynamic_slice_in_dim(turned, start, devices, axis=0)


def dft_tables(tokens):
    period = 2 * tokens
    width = 1
    while width * width < tokens:
        width *= 2
    outer = tokens // width
    freqs = jnp.arange(tokens + 1, dtype=jnp.int32)[:, None]
    coarse = turn_angles(freqs * (width * jnp.arange(outer, dtype=jnp.int32))[None, :], period)
    fine = turn_angles(freqs * jnp.arange(width, dtype=jnp.int32)[None, :], period)
    c1, s1 = jnp.cos(coarse)[:, :, None], jnp.sin(coarse)[:, :, None]
    c2, s2 = jnp.cos(fine)[:, None, :], jnp.sin(fine)[:, None, :]
    cos_t = (c1 * c2 - s1 * s2).reshape(tokens + 1, tokens)
    sin_t = (s1 * c2 + c1 * s2).reshape(tokens + 1, tokens)
    return cos_t, sin_t


def local_body(fresh, library, block_slot, prefix_blocks, short_taps, long_filter, skip_gain):
    row_count, _, channels = fresh.shape
    devices = lax.axis_size("seq")
    seq_index = lax.axis_index("seq")
    tokens = row_count * devices
    own = channels // devices
    lib_here = library.shape[0]
    lib_rows = lib_here * BLK // 4
    packed = jnp.concatenate([fresh, long_filter.astype(jnp.bfloat16)[:, None, :]], axis=1)
    packed = jnp.concatenate([packed, library.reshape(lib_rows, 4, channels)], axis=0)
    moved = exchange(
        lambda d: lax.dynamic_slice_in_dim(packed, d * own, own, axis=2), devices
    )
    rows = moved[:, :row_count].reshape(tokens, 4, own)
    lib_all = moved[:, row_count:].reshape(devices * lib_here, BLK * own)

    slot_ids = block_slot[prefix_blocks.reshape(-1)]
    prefix_len = slot_ids.shape[0] * BLK
    picker = (slot_ids[:, None] == jnp.arange(lib_all.shape[0], dtype=jnp.int32)[None, :]).astype(
        jnp.bfloat16
    )
    cached = jnp.dot(picker, lib_all, preferred_element_type=jnp.float32)
    cached = cached.reshape(prefix_len, own).astype(jnp.bfloat16)
    values = jnp.concatenate([cached, rows[prefix_len:, 2]], axis=0)
    stacked = jnp.concatenate([rows[:, :2], values[:, None]], axis=1).astype(jnp.float32)

    taps = lax.dynamic_slice_in_dim(short_taps, seq_index * own, own, axis=2)
    gain = lax.dynamic_slice_in_dim(skip_gain, seq_index * own, own, axis=0)
    shortened = jnp.zeros((tokens, 3, own), jnp.float32)
    for offset in range(TAPS):
        shifted = jnp.pad(stacked[: tokens - offset], ((offset, 0), (0, 0), (0, 0)))
        shortened = shortened + taps[offset][None] * shifted
    gating = shortened[:, 0]
    signal = shortened[:, 1] * shortened[:, 2]

    cos_t, sin_t = dft_tables(tokens)
    table = jnp.concatenate([cos_t, sin_t], axis=0).astype(jnp.bfloat16)
    operands = jnp.concatenate([signal.astype(jnp.bfloat16), rows[:, 3]], axis=1)
    spec = jnp.dot(table, operands, preferred_element_type=jnp.float32)
    bins = tokens + 1
    sig_c, tap_c = spec[:bins, :own], spec[:bins, own:]
    sig_s, tap_s = spec[bins:, :own], spec[bins:, own:]
    weight = jnp.where(
        (jnp.arange(bins) == 0) | (jnp.arange(bins) == tokens), 1.0, 2.0
    ).astype(jnp.float32)[:, None] / (2 * tokens)
    real = (sig_c * tap_c - sig_s * tap_s) * weight
    turned = (sig_c * tap_s + sig_s * tap_c) * weight
    back = jnp.concatenate([real, turned], axis=0).astype(jnp.bfloat16)
    convolved = lax.dot_general(
        table, back, (((0,), (0,)), ((), ())), preferred_element_type=jnp.float32
    )
    output = (gating * (convolved + gain[None, :] * signal)).astype(jnp.bfloat16)
    output = exchange(
        lambda d: lax.dynamic_slice_in_dim(output, d * row_count, row_count, axis=0), devices
    )
    return output.transpose(1, 0, 2).reshape(row_count, channels)


def body(fresh, library, *rest):
    devices = lax.axis_size("seq")
    tokens = fresh.shape[0] * devices
    fits = tokens <= 4096 and fresh.shape[2] % devices == 0 and (library.shape[0] * BLK) % 4 == 0
    if fits:
        return local_body(fresh, library, *rest)
    return ring_body(fresh, library, *rest)


def solution(mesh):
    return jax.shard_map(
        body,
        mesh=mesh,
        in_specs=(
            P(("group", "seq"), None, "chan"),
            P("seq", None, "chan"),
            P(),
            P("group", None),
            P(None, None, "chan"),
            P("seq", "chan"),
            P("chan"),
        ),
        out_specs=P(("group", "seq"), "chan"),
        check_vma=False,
    )
```

```python
import math

import jax
import jax.numpy as jnp
from jax import lax
from jax.sharding import PartitionSpec as P

TAPS = 3
BLK = 8


def from_behind(shard, axis, by):
    count = lax.axis_size(axis)
    pairs = [(i, i + by) for i in range(count) if 0 <= i + by < count]
    return lax.ppermute(shard, axis, pairs)


def exact_dot(pattern, matrix, tensor):
    return jnp.einsum(pattern, matrix, tensor, precision=lax.Precision.HIGHEST)


def turn_angles(numbers, period):
    return (numbers % period).astype(jnp.float32) * (2.0 * math.pi / period)


def ring_body(fresh, library, block_slot, prefix_blocks, short_taps, long_filter, skip_gain):
    row_count = fresh.shape[0]
    channels = fresh.shape[2]
    devices = lax.axis_size("seq")
    seq_index = lax.axis_index("seq")
    group_rows = row_count // devices
    period = 2 * row_count * devices
    block_ids = jnp.arange(devices, dtype=jnp.int32)
    mode_ids = jnp.arange(2 * devices, dtype=jnp.int32)
    coarse = turn_angles(mode_ids[:, None] * block_ids[None, :], 2 * devices)
    cos_q = jnp.cos(coarse)
    sin_q = jnp.sin(coarse)
    local_rows = seq_index * group_rows + jnp.arange(group_rows, dtype=jnp.int32)
    twist = turn_angles(mode_ids[:, None] * local_rows[None, :], period)
    twist_cos = jnp.cos(twist)[:, :, None]
    twist_sin = jnp.sin(twist)[:, :, None]
    row_ids = jnp.arange(row_count, dtype=jnp.int32)
    fine_angles = turn_angles(row_ids[:, None] * row_ids[None, :], row_count)
    cos_m = jnp.cos(fine_angles)
    sin_m = jnp.sin(fine_angles)
    first_modes = 2 * seq_index + jnp.arange(2, dtype=jnp.int32)
    back_twist = turn_angles(first_modes[:, None] * row_ids[None, :], period)
    back_cos = jnp.cos(back_twist)[:, :, None]
    back_sin = jnp.sin(back_twist)[:, :, None]

    def to_modes(column):
        real_part = exact_dot("kq,qgc->kgc", cos_q, column)
        imag_part = -exact_dot("kq,qgc->kgc", sin_q, column)
        return jnp.stack(
            [
                real_part * twist_cos + imag_part * twist_sin,
                imag_part * twist_cos - real_part * twist_sin,
            ]
        )

    def to_spectrum(spread):
        real_part = exact_dot("ki,jic->jkc", cos_m, spread[0]) + exact_dot(
            "ki,jic->jkc", sin_m, spread[1]
        )
        imag_part = exact_dot("ki,jic->jkc", cos_m, spread[1]) - exact_dot(
            "ki,jic->jkc", sin_m, spread[0]
        )
        return (real_part, imag_part)

    blocks_here = row_count // BLK
    flat_ids = prefix_blocks.reshape(-1)
    first_block = jnp.minimum(seq_index * blocks_here, flat_ids.shape[0] - blocks_here)
    own_ids = lax.dynamic_slice_in_dim(flat_ids, first_block, blocks_here)
    matches = own_ids[:, None] == jnp.arange(block_slot.shape[0], dtype=jnp.int32)[None, :]
    wanted = jnp.sum(jnp.where(matches, block_slot[None, :], 0), axis=1)
    shards = lax.all_gather(library, "seq", axis=0, tiled=True)
    picker = (wanted[:, None] == jnp.arange(shards.shape[0], dtype=jnp.int32)[None, :]).astype(
        jnp.bfloat16
    )
    gathered = jnp.einsum("bn,nlc->blc", picker, shards, preferred_element_type=jnp.float32)
    cached = gathered.reshape(row_count, channels).astype(jnp.bfloat16)
    values = jnp.where(seq_index < devices // 4, cached, fresh[:, 2])
    stacked = jnp.concatenate([fresh[:, :2], values[:, None]], axis=1)
    previous = from_behind(stacked[row_count - (TAPS - 1) :], "seq", 1)
    extended = jnp.concatenate([previous, stacked], axis=0)
    shortened = jnp.zeros((row_count, 3, channels), jnp.float32)
    for offset in range(TAPS):
        window_start = TAPS - 1 - offset
        shortened = shortened + short_taps[offset][None] * extended[
            window_start : window_start + row_count
        ].astype(jnp.float32)
    gating = shortened[:, 0]
    signal = shortened[:, 1] * shortened[:, 2]
    spread_signal = to_modes(
        lax.all_to_all(signal[None], "seq", split_axis=1, concat_axis=0, tiled=True)
    )
    spread_taps = to_modes(
        lax.all_to_all(long_filter[None], "seq", split_axis=1, concat_axis=0, tiled=True)
    )
    moved_signal, moved_taps = (
        lax.all_to_all(
            spread_signal.astype(jnp.bfloat16), "seq", split_axis=1, concat_axis=2, tiled=True
        ).astype(spread_signal.dtype),
        lax.all_to_all(
            spread_taps.astype(jnp.bfloat16), "seq", split_axis=1, concat_axis=2, tiled=True
        ).astype(spread_taps.dtype),
    )
    sig_real, sig_imag = to_spectrum(moved_signal)
    tap_real, tap_imag = to_spectrum(moved_taps)
    prod_real = sig_real * tap_real - sig_imag * tap_imag
    prod_imag = sig_real * tap_imag + sig_imag * tap_real
    back_real = exact_dot("ki,jic->jkc", cos_m, prod_real) - exact_dot(
        "ki,jic->jkc", sin_m, prod_imag
    )
    back_imag = exact_dot("ki,jic->jkc", cos_m, prod_imag) + exact_dot(
        "ki,jic->jkc", sin_m, prod_real
    )
    turned = jnp.stack(
        [back_real * back_cos - back_imag * back_sin, back_imag * back_cos + back_real * back_sin]
    )
    spread = lax.all_to_all(turned, "seq", split_axis=2, concat_axis=1, tiled=True)
    positions = (
        exact_dot("kq,kgc->qgc", cos_q, spread[0]) - exact_dot("kq,kgc->qgc", sin_q, spread[1])
    ) / period
    convolved = lax.all_to_all(positions, "seq", split_axis=0, concat_axis=1, tiled=True)[0]
    output = gating * (convolved + skip_gain[None, :] * signal)
    return output.astype(jnp.bfloat16)


def exchange(chunk_of, devices):
    seq_index = lax.axis_index("seq")
    arrived = []
    for shift in range(devices):
        block = chunk_of(lax.rem(seq_index + shift, devices))
        if shift:
            block = lax.ppermute(
                block, "seq", [(i, (i + shift) % devices) for i in range(devices)]
            )
        arrived.append(block)
    turned = jnp.stack(arrived[::-1] * 2)
    start = lax.rem(devices - 1 - seq_index + devices, devices)
    return lax.dynamic_slice_in_dim(turned, start, devices, axis=0)


def dft_tables(tokens):
    period = 2 * tokens
    width = 1
    while width * width < tokens:
        width *= 2
    outer = tokens // width
    freqs = jnp.arange(tokens + 1, dtype=jnp.int32)[:, None]
    coarse = turn_angles(freqs * (width * jnp.arange(outer, dtype=jnp.int32))[None, :], period)
    fine = turn_angles(freqs * jnp.arange(width, dtype=jnp.int32)[None, :], period)
    c1, s1 = jnp.cos(coarse)[:, :, None], jnp.sin(coarse)[:, :, None]
    c2, s2 = jnp.cos(fine)[:, None, :], jnp.sin(fine)[:, None, :]
    cos_t = (c1 * c2 - s1 * s2).reshape(tokens + 1, tokens)
    sin_t = (s1 * c2 + c1 * s2).reshape(tokens + 1, tokens)
    return cos_t, sin_t


def local_body(fresh, library, block_slot, prefix_blocks, short_taps, long_filter, skip_gain):
    row_count, _, channels = fresh.shape
    devices = lax.axis_size("seq")
    seq_index = lax.axis_index("seq")
    tokens = row_count * devices
    own = channels // devices
    lib_here = library.shape[0]
    lib_flat = library.reshape(lib_here * BLK, channels)
    lib_rows = -(-lib_here * BLK // 3)
    lib_flat = jnp.pad(lib_flat, ((0, 3 * lib_rows - lib_here * BLK), (0, 0)))
    packed = jnp.concatenate([fresh[:, 1:], long_filter.astype(jnp.bfloat16)[:, None, :]], axis=1)
    packed = jnp.concatenate([packed, lib_flat.reshape(lib_rows, 3, channels)], axis=0)
    moved = exchange(
        lambda d: lax.dynamic_slice_in_dim(packed, d * own, own, axis=2), devices
    )
    rows = moved[:, :row_count].reshape(tokens, 3, own)
    lib_all = moved[:, row_count:].reshape(devices, 3 * lib_rows, own)[:, : lib_here * BLK]
    lib_all = lib_all.reshape(devices * lib_here, BLK * own)

    gate_in = fresh[:, 0].astype(jnp.float32)
    gate_prev = from_behind(fresh[row_count - (TAPS - 1) :, 0], "seq", 1).astype(jnp.float32)
    gate_ext = jnp.concatenate([gate_prev, gate_in], axis=0)
    gating = jnp.zeros((row_count, channels), jnp.float32)
    for offset in range(TAPS):
        window_start = TAPS - 1 - offset
        gating = gating + short_taps[offset, 0][None] * gate_ext[
            window_start : window_start + row_count
        ]

    slot_ids = block_slot[prefix_blocks.reshape(-1)]
    prefix_len = slot_ids.shape[0] * BLK
    picker = (slot_ids[:, None] == jnp.arange(lib_all.shape[0], dtype=jnp.int32)[None, :]).astype(
        jnp.bfloat16
    )
    cached = jnp.dot(picker, lib_all, preferred_element_type=jnp.float32)
    cached = cached.reshape(prefix_len, own).astype(jnp.bfloat16)
    values = jnp.concatenate([cached, rows[prefix_len:, 1]], axis=0)
    stacked = jnp.stack([rows[:, 0], values], axis=1).astype(jnp.float32)

    taps = lax.dynamic_slice_in_dim(short_taps[:, 1:], seq_index * own, own, axis=2)
    gain = lax.dynamic_slice_in_dim(skip_gain, seq_index * own, own, axis=0)
    shortened = jnp.zeros((tokens, 2, own), jnp.float32)
    for offset in range(TAPS):
        shifted = jnp.pad(stacked[: tokens - offset], ((offset, 0), (0, 0), (0, 0)))
        shortened = shortened + taps[offset][None] * shifted
    signal = shortened[:, 0] * shortened[:, 1]

    cos_t, sin_t = dft_tables(tokens)
    table = jnp.concatenate([cos_t, sin_t], axis=0).astype(jnp.bfloat16)
    operands = jnp.concatenate([signal.astype(jnp.bfloat16), rows[:, 2]], axis=1)
    spec = jnp.dot(table, operands, preferred_element_type=jnp.float32)
    bins = tokens + 1
    sig_c, tap_c = spec[:bins, :own], spec[:bins, own:]
    sig_s, tap_s = spec[bins:, :own], spec[bins:, own:]
    weight = jnp.where(
        (jnp.arange(bins) == 0) | (jnp.arange(bins) == tokens), 1.0, 2.0
    ).astype(jnp.float32)[:, None] / (2 * tokens)
    real = (sig_c * tap_c - sig_s * tap_s) * weight
    turned = (sig_c * tap_s + sig_s * tap_c) * weight
    back = jnp.concatenate([real, turned], axis=0).astype(jnp.bfloat16)
    convolved = lax.dot_general(
        table, back, (((0,), (0,)), ((), ())), preferred_element_type=jnp.float32
    )
    summed = (convolved + gain[None, :] * signal).astype(jnp.bfloat16)
    summed = exchange(
        lambda d: lax.dynamic_slice_in_dim(summed, d * row_count, row_count, axis=0), devices
    )
    summed = summed.transpose(1, 0, 2).reshape(row_count, channels)
    return (gating * summed.astype(jnp.float32)).astype(jnp.bfloat16)


def body(fresh, library, *rest):
    devices = lax.axis_size("seq")
    tokens = fresh.shape[0] * devices
    fits = tokens <= 4096 and fresh.shape[2] % devices == 0
    if fits:
        return local_body(fresh, library, *rest)
    return ring_body(fresh, library, *rest)


def solution(mesh):
    return jax.shard_map(
        body,
        mesh=mesh,
        in_specs=(
            P(("group", "seq"), None, "chan"),
            P("seq", None, "chan"),
            P(),
            P("group", None),
            P(None, None, "chan"),
            P("seq", "chan"),
            P("chan"),
        ),
        out_specs=P(("group", "seq"), "chan"),
        check_vma=False,
    )
```

```python
import math

import jax
import jax.numpy as jnp
from jax import lax
from jax.sharding import PartitionSpec as P

TAPS = 3
BLK = 8


def from_behind(shard, axis, by):
    count = lax.axis_size(axis)
    pairs = [(i, i + by) for i in range(count) if 0 <= i + by < count]
    return lax.ppermute(shard, axis, pairs)


def exact_dot(pattern, matrix, tensor):
    return jnp.einsum(pattern, matrix, tensor, precision=lax.Precision.HIGHEST)


def turn_angles(numbers, period):
    return (numbers % period).astype(jnp.float32) * (2.0 * math.pi / period)


def ring_body(fresh, library, block_slot, prefix_blocks, short_taps, long_filter, skip_gain):
    row_count = fresh.shape[0]
    channels = fresh.shape[2]
    devices = lax.axis_size("seq")
    seq_index = lax.axis_index("seq")
    group_rows = row_count // devices
    period = 2 * row_count * devices
    block_ids = jnp.arange(devices, dtype=jnp.int32)
    mode_ids = jnp.arange(2 * devices, dtype=jnp.int32)
    coarse = turn_angles(mode_ids[:, None] * block_ids[None, :], 2 * devices)
    cos_q = jnp.cos(coarse)
    sin_q = jnp.sin(coarse)
    local_rows = seq_index * group_rows + jnp.arange(group_rows, dtype=jnp.int32)
    twist = turn_angles(mode_ids[:, None] * local_rows[None, :], period)
    twist_cos = jnp.cos(twist)[:, :, None]
    twist_sin = jnp.sin(twist)[:, :, None]
    row_ids = jnp.arange(row_count, dtype=jnp.int32)
    fine_angles = turn_angles(row_ids[:, None] * row_ids[None, :], row_count)
    cos_m = jnp.cos(fine_angles)
    sin_m = jnp.sin(fine_angles)
    first_modes = 2 * seq_index + jnp.arange(2, dtype=jnp.int32)
    back_twist = turn_angles(first_modes[:, None] * row_ids[None, :], period)
    back_cos = jnp.cos(back_twist)[:, :, None]
    back_sin = jnp.sin(back_twist)[:, :, None]

    def to_modes(column):
        real_part = exact_dot("kq,qgc->kgc", cos_q, column)
        imag_part = -exact_dot("kq,qgc->kgc", sin_q, column)
        return jnp.stack(
            [
                real_part * twist_cos + imag_part * twist_sin,
                imag_part * twist_cos - real_part * twist_sin,
            ]
        )

    def to_spectrum(spread):
        real_part = exact_dot("ki,jic->jkc", cos_m, spread[0]) + exact_dot(
            "ki,jic->jkc", sin_m, spread[1]
        )
        imag_part = exact_dot("ki,jic->jkc", cos_m, spread[1]) - exact_dot(
            "ki,jic->jkc", sin_m, spread[0]
        )
        return (real_part, imag_part)

    blocks_here = row_count // BLK
    flat_ids = prefix_blocks.reshape(-1)
    first_block = jnp.minimum(seq_index * blocks_here, flat_ids.shape[0] - blocks_here)
    own_ids = lax.dynamic_slice_in_dim(flat_ids, first_block, blocks_here)
    matches = own_ids[:, None] == jnp.arange(block_slot.shape[0], dtype=jnp.int32)[None, :]
    wanted = jnp.sum(jnp.where(matches, block_slot[None, :], 0), axis=1)
    shards = lax.all_gather(library, "seq", axis=0, tiled=True)
    picker = (wanted[:, None] == jnp.arange(shards.shape[0], dtype=jnp.int32)[None, :]).astype(
        jnp.bfloat16
    )
    gathered = jnp.einsum("bn,nlc->blc", picker, shards, preferred_element_type=jnp.float32)
    cached = gathered.reshape(row_count, channels).astype(jnp.bfloat16)
    values = jnp.where(seq_index < devices // 4, cached, fresh[:, 2])
    stacked = jnp.concatenate([fresh[:, :2], values[:, None]], axis=1)
    previous = from_behind(stacked[row_count - (TAPS - 1) :], "seq", 1)
    extended = jnp.concatenate([previous, stacked], axis=0)
    shortened = jnp.zeros((row_count, 3, channels), jnp.float32)
    for offset in range(TAPS):
        window_start = TAPS - 1 - offset
        shortened = shortened + short_taps[offset][None] * extended[
            window_start : window_start + row_count
        ].astype(jnp.float32)
    gating = shortened[:, 0]
    signal = shortened[:, 1] * shortened[:, 2]
    spread_signal = to_modes(
        lax.all_to_all(signal[None], "seq", split_axis=1, concat_axis=0, tiled=True)
    )
    spread_taps = to_modes(
        lax.all_to_all(long_filter[None], "seq", split_axis=1, concat_axis=0, tiled=True)
    )
    moved_signal, moved_taps = (
        lax.all_to_all(
            spread_signal.astype(jnp.bfloat16), "seq", split_axis=1, concat_axis=2, tiled=True
        ).astype(spread_signal.dtype),
        lax.all_to_all(
            spread_taps.astype(jnp.bfloat16), "seq", split_axis=1, concat_axis=2, tiled=True
        ).astype(spread_taps.dtype),
    )
    sig_real, sig_imag = to_spectrum(moved_signal)
    tap_real, tap_imag = to_spectrum(moved_taps)
    prod_real = sig_real * tap_real - sig_imag * tap_imag
    prod_imag = sig_real * tap_imag + sig_imag * tap_real
    back_real = exact_dot("ki,jic->jkc", cos_m, prod_real) - exact_dot(
        "ki,jic->jkc", sin_m, prod_imag
    )
    back_imag = exact_dot("ki,jic->jkc", cos_m, prod_imag) + exact_dot(
        "ki,jic->jkc", sin_m, prod_real
    )
    turned = jnp.stack(
        [back_real * back_cos - back_imag * back_sin, back_imag * back_cos + back_real * back_sin]
    )
    spread = lax.all_to_all(turned, "seq", split_axis=2, concat_axis=1, tiled=True)
    positions = (
        exact_dot("kq,kgc->qgc", cos_q, spread[0]) - exact_dot("kq,kgc->qgc", sin_q, spread[1])
    ) / period
    convolved = lax.all_to_all(positions, "seq", split_axis=0, concat_axis=1, tiled=True)[0]
    output = gating * (convolved + skip_gain[None, :] * signal)
    return output.astype(jnp.bfloat16)


def exchange(chunk_of, devices):
    seq_index = lax.axis_index("seq")
    arrived = []
    for shift in range(devices):
        block = chunk_of(lax.rem(seq_index + shift, devices))
        if shift:
            block = lax.ppermute(
                block, "seq", [(i, (i + shift) % devices) for i in range(devices)]
            )
        arrived.append(block)
    turned = jnp.stack(arrived[::-1] * 2)
    start = lax.rem(devices - 1 - seq_index + devices, devices)
    return lax.dynamic_slice_in_dim(turned, start, devices, axis=0)


def dft_tables(tokens):
    period = 2 * tokens
    width = 1
    while width * width < tokens:
        width *= 2
    outer = tokens // width
    freqs = jnp.arange(tokens + 1, dtype=jnp.int32)[:, None]
    coarse = turn_angles(freqs * (width * jnp.arange(outer, dtype=jnp.int32))[None, :], period)
    fine = turn_angles(freqs * jnp.arange(width, dtype=jnp.int32)[None, :], period)
    c1, s1 = jnp.cos(coarse)[:, :, None], jnp.sin(coarse)[:, :, None]
    c2, s2 = jnp.cos(fine)[:, None, :], jnp.sin(fine)[:, None, :]
    cos_t = (c1 * c2 - s1 * s2).reshape(tokens + 1, tokens)
    sin_t = (s1 * c2 + c1 * s2).reshape(tokens + 1, tokens)
    return cos_t, sin_t


def local_body(fresh, library, block_slot, prefix_blocks, short_taps, long_filter, skip_gain):
    row_count, _, channels = fresh.shape
    devices = lax.axis_size("seq")
    seq_index = lax.axis_index("seq")
    tokens = row_count * devices
    own = channels // devices
    lib_here = library.shape[0]
    lib_flat = library.reshape(lib_here * BLK, channels)
    lib_rows = -(-lib_here * BLK // 3)
    lib_flat = jnp.pad(lib_flat, ((0, 3 * lib_rows - lib_here * BLK), (0, 0)))
    packed = jnp.concatenate([fresh[:, 1:], long_filter.astype(jnp.bfloat16)[:, None, :]], axis=1)
    packed = jnp.concatenate([packed, lib_flat.reshape(lib_rows, 3, channels)], axis=0)
    moved = exchange(
        lambda d: lax.dynamic_slice_in_dim(packed, d * own, own, axis=2), devices
    )
    rows = moved[:, :row_count].reshape(tokens, 3, own)
    lib_all = moved[:, row_count:].reshape(devices, 3 * lib_rows, own)[:, : lib_here * BLK]
    lib_all = lib_all.reshape(devices * lib_here, BLK * own)

    gate_in = fresh[:, 0].astype(jnp.float32)
    gate_prev = from_behind(fresh[row_count - (TAPS - 1) :, 0], "seq", 1).astype(jnp.float32)
    gate_ext = jnp.concatenate([gate_prev, gate_in], axis=0)
    gating = jnp.zeros((row_count, channels), jnp.float32)
    for offset in range(TAPS):
        window_start = TAPS - 1 - offset
        gating = gating + short_taps[offset, 0][None] * gate_ext[
            window_start : window_start + row_count
        ]

    slot_ids = block_slot[prefix_blocks.reshape(-1)]
    prefix_len = slot_ids.shape[0] * BLK
    picker = (slot_ids[:, None] == jnp.arange(lib_all.shape[0], dtype=jnp.int32)[None, :]).astype(
        jnp.bfloat16
    )
    cached = jnp.dot(picker, lib_all, preferred_element_type=jnp.float32)
    cached = cached.reshape(prefix_len, own).astype(jnp.bfloat16)
    values = jnp.concatenate([cached, rows[prefix_len:, 1]], axis=0)
    stacked = jnp.stack([rows[:, 0], values], axis=1).astype(jnp.float32)

    taps = lax.dynamic_slice_in_dim(short_taps[:, 1:], seq_index * own, own, axis=2)
    gain = lax.dynamic_slice_in_dim(skip_gain, seq_index * own, own, axis=0)
    shortened = jnp.zeros((tokens, 2, own), jnp.float32)
    for offset in range(TAPS):
        shifted = jnp.pad(stacked[: tokens - offset], ((offset, 0), (0, 0), (0, 0)))
        shortened = shortened + taps[offset][None] * shifted
    signal = shortened[:, 0] * shortened[:, 1]

    cos_t, sin_t = dft_tables(tokens)
    table = jnp.concatenate([cos_t, sin_t], axis=0).astype(jnp.bfloat16)
    operands = jnp.concatenate([signal.astype(jnp.bfloat16), rows[:, 2]], axis=1)
    spec = jnp.dot(table, operands, preferred_element_type=jnp.float32)
    bins = tokens + 1
    sig_c, tap_c = spec[:bins, :own], spec[:bins, own:]
    sig_s, tap_s = spec[bins:, :own], spec[bins:, own:]
    weight = jnp.where(
        (jnp.arange(bins) == 0) | (jnp.arange(bins) == tokens), 1.0, 2.0
    ).astype(jnp.float32)[:, None] / (2 * tokens)
    real = (sig_c * tap_c - sig_s * tap_s) * weight
    turned = (sig_c * tap_s + sig_s * tap_c) * weight
    back = jnp.concatenate([real, turned], axis=0).astype(jnp.bfloat16)
    convolved = lax.dot_general(
        table, back, (((0,), (0,)), ((), ())), preferred_element_type=jnp.float32
    )
    summed = (convolved + gain[None, :] * signal).astype(jnp.bfloat16)
    summed = lax.all_to_all(
        summed.reshape(devices, row_count, own), "seq", split_axis=0, concat_axis=0, tiled=True
    )
    summed = summed.transpose(1, 0, 2).reshape(row_count, channels)
    return (gating * summed.astype(jnp.float32)).astype(jnp.bfloat16)


def body(fresh, library, *rest):
    devices = lax.axis_size("seq")
    tokens = fresh.shape[0] * devices
    fits = tokens <= 4096 and fresh.shape[2] % devices == 0
    if fits:
        return local_body(fresh, library, *rest)
    return ring_body(fresh, library, *rest)


def solution(mesh):
    return jax.shard_map(
        body,
        mesh=mesh,
        in_specs=(
            P(("group", "seq"), None, "chan"),
            P("seq", None, "chan"),
            P(),
            P("group", None),
            P(None, None, "chan"),
            P("seq", "chan"),
            P("chan"),
        ),
        out_specs=P(("group", "seq"), "chan"),
        check_vma=False,
    )
```

```python
import math

import jax
import jax.numpy as jnp
from jax import lax
from jax.sharding import PartitionSpec as P

TAPS = 3
BLK = 8


def from_behind(shard, axis, by):
    count = lax.axis_size(axis)
    pairs = [(i, i + by) for i in range(count) if 0 <= i + by < count]
    return lax.ppermute(shard, axis, pairs)


def exact_dot(pattern, matrix, tensor):
    return jnp.einsum(pattern, matrix, tensor, precision=lax.Precision.HIGHEST)


def turn_angles(numbers, period):
    return (numbers % period).astype(jnp.float32) * (2.0 * math.pi / period)


def ring_body(fresh, library, block_slot, prefix_blocks, short_taps, long_filter, skip_gain):
    row_count = fresh.shape[0]
    channels = fresh.shape[2]
    devices = lax.axis_size("seq")
    seq_index = lax.axis_index("seq")
    group_rows = row_count // devices
    period = 2 * row_count * devices
    block_ids = jnp.arange(devices, dtype=jnp.int32)
    mode_ids = jnp.arange(2 * devices, dtype=jnp.int32)
    coarse = turn_angles(mode_ids[:, None] * block_ids[None, :], 2 * devices)
    cos_q = jnp.cos(coarse)
    sin_q = jnp.sin(coarse)
    local_rows = seq_index * group_rows + jnp.arange(group_rows, dtype=jnp.int32)
    twist = turn_angles(mode_ids[:, None] * local_rows[None, :], period)
    twist_cos = jnp.cos(twist)[:, :, None]
    twist_sin = jnp.sin(twist)[:, :, None]
    row_ids = jnp.arange(row_count, dtype=jnp.int32)
    fine_angles = turn_angles(row_ids[:, None] * row_ids[None, :], row_count)
    cos_m = jnp.cos(fine_angles)
    sin_m = jnp.sin(fine_angles)
    first_modes = 2 * seq_index + jnp.arange(2, dtype=jnp.int32)
    back_twist = turn_angles(first_modes[:, None] * row_ids[None, :], period)
    back_cos = jnp.cos(back_twist)[:, :, None]
    back_sin = jnp.sin(back_twist)[:, :, None]

    def to_modes(column):
        real_part = exact_dot("kq,qgc->kgc", cos_q, column)
        imag_part = -exact_dot("kq,qgc->kgc", sin_q, column)
        return jnp.stack(
            [
                real_part * twist_cos + imag_part * twist_sin,
                imag_part * twist_cos - real_part * twist_sin,
            ]
        )

    def to_spectrum(spread):
        real_part = exact_dot("ki,jic->jkc", cos_m, spread[0]) + exact_dot(
            "ki,jic->jkc", sin_m, spread[1]
        )
        imag_part = exact_dot("ki,jic->jkc", cos_m, spread[1]) - exact_dot(
            "ki,jic->jkc", sin_m, spread[0]
        )
        return (real_part, imag_part)

    blocks_here = row_count // BLK
    flat_ids = prefix_blocks.reshape(-1)
    first_block = jnp.minimum(seq_index * blocks_here, flat_ids.shape[0] - blocks_here)
    own_ids = lax.dynamic_slice_in_dim(flat_ids, first_block, blocks_here)
    matches = own_ids[:, None] == jnp.arange(block_slot.shape[0], dtype=jnp.int32)[None, :]
    wanted = jnp.sum(jnp.where(matches, block_slot[None, :], 0), axis=1)
    shards = lax.all_gather(library, "seq", axis=0, tiled=True)
    picker = (wanted[:, None] == jnp.arange(shards.shape[0], dtype=jnp.int32)[None, :]).astype(
        jnp.bfloat16
    )
    gathered = jnp.einsum("bn,nlc->blc", picker, shards, preferred_element_type=jnp.float32)
    cached = gathered.reshape(row_count, channels).astype(jnp.bfloat16)
    values = jnp.where(seq_index < devices // 4, cached, fresh[:, 2])
    stacked = jnp.concatenate([fresh[:, :2], values[:, None]], axis=1)
    previous = from_behind(stacked[row_count - (TAPS - 1) :], "seq", 1)
    extended = jnp.concatenate([previous, stacked], axis=0)
    shortened = jnp.zeros((row_count, 3, channels), jnp.float32)
    for offset in range(TAPS):
        window_start = TAPS - 1 - offset
        shortened = shortened + short_taps[offset][None] * extended[
            window_start : window_start + row_count
        ].astype(jnp.float32)
    gating = shortened[:, 0]
    signal = shortened[:, 1] * shortened[:, 2]
    spread_signal = to_modes(
        lax.all_to_all(signal[None], "seq", split_axis=1, concat_axis=0, tiled=True)
    )
    spread_taps = to_modes(
        lax.all_to_all(long_filter[None], "seq", split_axis=1, concat_axis=0, tiled=True)
    )
    moved_signal, moved_taps = (
        lax.all_to_all(
            spread_signal.astype(jnp.bfloat16), "seq", split_axis=1, concat_axis=2, tiled=True
        ).astype(spread_signal.dtype),
        lax.all_to_all(
            spread_taps.astype(jnp.bfloat16), "seq", split_axis=1, concat_axis=2, tiled=True
        ).astype(spread_taps.dtype),
    )
    sig_real, sig_imag = to_spectrum(moved_signal)
    tap_real, tap_imag = to_spectrum(moved_taps)
    prod_real = sig_real * tap_real - sig_imag * tap_imag
    prod_imag = sig_real * tap_imag + sig_imag * tap_real
    back_real = exact_dot("ki,jic->jkc", cos_m, prod_real) - exact_dot(
        "ki,jic->jkc", sin_m, prod_imag
    )
    back_imag = exact_dot("ki,jic->jkc", cos_m, prod_imag) + exact_dot(
        "ki,jic->jkc", sin_m, prod_real
    )
    turned = jnp.stack(
        [back_real * back_cos - back_imag * back_sin, back_imag * back_cos + back_real * back_sin]
    )
    spread = lax.all_to_all(turned, "seq", split_axis=2, concat_axis=1, tiled=True)
    positions = (
        exact_dot("kq,kgc->qgc", cos_q, spread[0]) - exact_dot("kq,kgc->qgc", sin_q, spread[1])
    ) / period
    convolved = lax.all_to_all(positions, "seq", split_axis=0, concat_axis=1, tiled=True)[0]
    output = gating * (convolved + skip_gain[None, :] * signal)
    return output.astype(jnp.bfloat16)


def exchange(chunk_of, devices):
    seq_index = lax.axis_index("seq")
    arrived = []
    for shift in range(devices):
        block = chunk_of(lax.rem(seq_index + shift, devices))
        if shift:
            block = lax.ppermute(
                block, "seq", [(i, (i + shift) % devices) for i in range(devices)]
            )
        arrived.append(block)
    turned = jnp.stack(arrived[::-1] * 2)
    start = lax.rem(devices - 1 - seq_index + devices, devices)
    return lax.dynamic_slice_in_dim(turned, start, devices, axis=0)


def dft_tables(tokens):
    period = 2 * tokens
    width = 1
    while width * width < tokens:
        width *= 2
    outer = tokens // width
    freqs = jnp.arange(tokens + 1, dtype=jnp.int32)[:, None]
    coarse = turn_angles(freqs * (width * jnp.arange(outer, dtype=jnp.int32))[None, :], period)
    fine = turn_angles(freqs * jnp.arange(width, dtype=jnp.int32)[None, :], period)
    c1, s1 = jnp.cos(coarse)[:, :, None], jnp.sin(coarse)[:, :, None]
    c2, s2 = jnp.cos(fine)[:, None, :], jnp.sin(fine)[:, None, :]
    cos_t = (c1 * c2 - s1 * s2).reshape(tokens + 1, tokens)
    sin_t = (s1 * c2 + c1 * s2).reshape(tokens + 1, tokens)
    return cos_t, sin_t


def local_body(fresh, library, block_slot, prefix_blocks, short_taps, long_filter, skip_gain):
    row_count, _, channels = fresh.shape
    devices = lax.axis_size("seq")
    seq_index = lax.axis_index("seq")
    tokens = row_count * devices
    own = channels // devices
    lib_here = library.shape[0]
    lib_flat = library.reshape(lib_here * BLK, channels)
    lib_rows = -(-lib_here * BLK // 3)
    lib_flat = jnp.pad(lib_flat, ((0, 3 * lib_rows - lib_here * BLK), (0, 0)))
    packed = jnp.concatenate([fresh[:, 1:], long_filter.astype(jnp.bfloat16)[:, None, :]], axis=1)
    packed = jnp.concatenate([packed, lib_flat.reshape(lib_rows, 3, channels)], axis=0)
    moved = exchange(
        lambda d: lax.dynamic_slice_in_dim(packed, d * own, own, axis=2), devices
    )
    rows = moved[:, :row_count].reshape(tokens, 3, own)
    lib_all = moved[:, row_count:].reshape(devices, 3 * lib_rows, own)[:, : lib_here * BLK]
    lib_all = lib_all.reshape(devices * lib_here, BLK * own)

    gate_in = fresh[:, 0].astype(jnp.float32)
    gate_prev = from_behind(fresh[row_count - (TAPS - 1) :, 0], "seq", 1).astype(jnp.float32)
    gate_ext = jnp.concatenate([gate_prev, gate_in], axis=0)
    gating = jnp.zeros((row_count, channels), jnp.float32)
    for offset in range(TAPS):
        window_start = TAPS - 1 - offset
        gating = gating + short_taps[offset, 0][None] * gate_ext[
            window_start : window_start + row_count
        ]

    slot_ids = block_slot[prefix_blocks.reshape(-1)]
    prefix_len = slot_ids.shape[0] * BLK
    picker = (slot_ids[:, None] == jnp.arange(lib_all.shape[0], dtype=jnp.int32)[None, :]).astype(
        jnp.bfloat16
    )
    cached = jnp.dot(picker, lib_all, preferred_element_type=jnp.float32)
    cached = cached.reshape(prefix_len, own).astype(jnp.bfloat16)
    values = jnp.concatenate([cached, rows[prefix_len:, 1]], axis=0)
    stacked = jnp.stack([rows[:, 0], values], axis=1).astype(jnp.float32)

    taps = lax.dynamic_slice_in_dim(short_taps[:, 1:], seq_index * own, own, axis=2)
    gain = lax.dynamic_slice_in_dim(skip_gain, seq_index * own, own, axis=0)
    shortened = jnp.zeros((tokens, 2, own), jnp.float32)
    for offset in range(TAPS):
        shifted = jnp.pad(stacked[: tokens - offset], ((offset, 0), (0, 0), (0, 0)))
        shortened = shortened + taps[offset][None] * shifted
    signal = shortened[:, 0] * shortened[:, 1]

    cos_t, sin_t = dft_tables(tokens)
    table = jnp.concatenate([cos_t, sin_t], axis=0).astype(jnp.bfloat16)
    operands = jnp.concatenate([signal.astype(jnp.bfloat16), rows[:, 2]], axis=1)
    spec = jnp.dot(table, operands, preferred_element_type=jnp.float32)
    bins = tokens + 1
    sig_c, tap_c = spec[:bins, :own], spec[:bins, own:]
    sig_s, tap_s = spec[bins:, :own], spec[bins:, own:]
    weight = jnp.where(
        (jnp.arange(bins) == 0) | (jnp.arange(bins) == tokens), 1.0, 2.0
    ).astype(jnp.float32)[:, None] / (2 * tokens)
    real = (sig_c * tap_c - sig_s * tap_s) * weight
    turned = (sig_c * tap_s + sig_s * tap_c) * weight
    back = jnp.concatenate([real, turned], axis=0).astype(jnp.bfloat16)
    convolved = lax.dot_general(
        table, back, (((0,), (0,)), ((), ())), preferred_element_type=jnp.float32
    )
    summed = (convolved + gain[None, :] * signal).astype(jnp.bfloat16)
    summed = lax.all_to_all(
        summed.reshape(devices, row_count, own), "seq", split_axis=0, concat_axis=0, tiled=True
    )
    summed = summed.transpose(1, 0, 2).reshape(row_count, channels)
    return (gating * summed.astype(jnp.float32)).astype(jnp.bfloat16)


def signal_body(fresh, library, block_slot, prefix_blocks, short_taps, long_filter, skip_gain):
    row_count, _, channels = fresh.shape
    devices = lax.axis_size("seq")
    seq_index = lax.axis_index("seq")
    tokens = row_count * devices
    own = channels // devices
    lib_here = library.shape[0]
    prefix_len = prefix_blocks.size * BLK
    prefix_devices = prefix_len // row_count

    fresh32 = fresh.astype(jnp.float32)
    local = jnp.zeros((row_count, 2, channels), jnp.float32)
    for offset in range(TAPS):
        shifted = jnp.pad(fresh32[: row_count - offset, 1:], ((offset, 0), (0, 0), (0, 0)))
        local = local + short_taps[offset, 1:][None] * shifted
    sent = jnp.where(seq_index < prefix_devices, local[:, 0], local[:, 0] * local[:, 1])
    edges = jnp.concatenate([fresh[: TAPS - 1, 1:], fresh[row_count - (TAPS - 1) :, 1:]], axis=0)
    packed = jnp.stack([sent.astype(jnp.bfloat16), long_filter.astype(jnp.bfloat16)], axis=1)
    lib_rows = lib_here * BLK // 2
    packed = jnp.concatenate(
        [packed, edges, library.reshape(lib_rows, 2, channels)], axis=0
    )
    moved = exchange(
        lambda d: lax.dynamic_slice_in_dim(packed, d * own, own, axis=2), devices
    )
    rows = moved[:, :row_count].reshape(tokens, 2, own)
    edge_rows = moved[:, row_count : row_count + 2 * (TAPS - 1)].astype(jnp.float32)
    lib_all = moved[:, row_count + 2 * (TAPS - 1) :].reshape(devices * lib_here, BLK * own)

    gate_in = fresh32[:, 0]
    gate_prev = from_behind(fresh[row_count - (TAPS - 1) :, 0], "seq", 1).astype(jnp.float32)
    gate_ext = jnp.concatenate([gate_prev, gate_in], axis=0)
    gating = jnp.zeros((row_count, channels), jnp.float32)
    for offset in range(TAPS):
        window_start = TAPS - 1 - offset
        gating = gating + short_taps[offset, 0][None] * gate_ext[
            window_start : window_start + row_count
        ]

    slot_ids = block_slot[prefix_blocks.reshape(-1)]
    picker = (slot_ids[:, None] == jnp.arange(lib_all.shape[0], dtype=jnp.int32)[None, :]).astype(
        jnp.bfloat16
    )
    cached = jnp.dot(picker, lib_all, preferred_element_type=jnp.float32)
    cached = cached.reshape(prefix_len, own).astype(jnp.bfloat16).astype(jnp.float32)

    taps = lax.dynamic_slice_in_dim(short_taps[:, 1:], seq_index * own, own, axis=2)
    gain = lax.dynamic_slice_in_dim(skip_gain, seq_index * own, own, axis=0)
    lib_short = jnp.zeros((prefix_len, own), jnp.float32)
    for offset in range(TAPS):
        lib_short = lib_short + taps[offset, 1][None] * jnp.pad(
            cached[: prefix_len - offset], ((offset, 0), (0, 0))
        )
    arrived = rows[:, 0].astype(jnp.float32)
    signal = jnp.concatenate([arrived[:prefix_len] * lib_short, arrived[prefix_len:]], axis=0)

    head = edge_rows[:, : TAPS - 1]
    tail = jnp.pad(edge_rows[:-1, TAPS - 1 :], ((1, 0), (0, 0), (0, 0), (0, 0)))
    window = jnp.concatenate([tail, head], axis=1)
    positions = (
        jnp.arange(devices)[:, None] * row_count + jnp.arange(2 * (TAPS - 1))[None, :] - (TAPS - 1)
    )
    cached_ext = jnp.pad(cached, ((0, 1), (0, 0)))
    lib_at = cached_ext[jnp.clip(positions, 0, prefix_len)]
    values = jnp.where(
        (positions < prefix_len)[:, :, None], lib_at, window[:, :, 1]
    )
    values = jnp.where((positions >= 0)[:, :, None], values, 0.0)
    ones = jnp.where((positions >= 0)[:, :, None], window[:, :, 0], 0.0)
    edge_signal = []
    for row in range(TAPS - 1):
        first = sum(taps[offset, 0][None] * ones[:, TAPS - 1 + row - offset] for offset in range(TAPS))
        second = sum(
            taps[offset, 1][None] * values[:, TAPS - 1 + row - offset] for offset in range(TAPS)
        )
        edge_signal.append(first * second)
    edge_signal = jnp.stack(edge_signal, axis=1)
    signal = signal.reshape(devices, row_count, own)
    signal = jnp.concatenate([edge_signal, signal[:, TAPS - 1 :]], axis=1).reshape(tokens, own)

    cos_t, sin_t = dft_tables(tokens)
    table = jnp.concatenate([cos_t, sin_t], axis=0).astype(jnp.bfloat16)
    operands = jnp.concatenate([signal.astype(jnp.bfloat16), rows[:, 1]], axis=1)
    spec = jnp.dot(table, operands, preferred_element_type=jnp.float32)
    bins = tokens + 1
    sig_c, tap_c = spec[:bins, :own], spec[:bins, own:]
    sig_s, tap_s = spec[bins:, :own], spec[bins:, own:]
    weight = jnp.where(
        (jnp.arange(bins) == 0) | (jnp.arange(bins) == tokens), 1.0, 2.0
    ).astype(jnp.float32)[:, None] / (2 * tokens)
    real = (sig_c * tap_c - sig_s * tap_s) * weight
    turned = (sig_c * tap_s + sig_s * tap_c) * weight
    back = jnp.concatenate([real, turned], axis=0).astype(jnp.bfloat16)
    convolved = lax.dot_general(
        table, back, (((0,), (0,)), ((), ())), preferred_element_type=jnp.float32
    )
    summed = (convolved + gain[None, :] * signal).astype(jnp.bfloat16)
    summed = exchange(
        lambda d: lax.dynamic_slice_in_dim(summed, d * row_count, row_count, axis=0), devices
    )
    summed = summed.transpose(1, 0, 2).reshape(row_count, channels)
    return (gating * summed.astype(jnp.float32)).astype(jnp.bfloat16)


def body(fresh, library, *rest):
    devices = lax.axis_size("seq")
    tokens = fresh.shape[0] * devices
    fits = tokens <= 4096 and fresh.shape[2] % devices == 0
    prefix_len = rest[1].size * BLK
    aligned = prefix_len % fresh.shape[0] == 0 and prefix_len < tokens and fresh.shape[0] >= 2 * TAPS
    if fits and aligned and (library.shape[0] * BLK) % 2 == 0:
        return signal_body(fresh, library, *rest)
    if fits:
        return local_body(fresh, library, *rest)
    return ring_body(fresh, library, *rest)


def solution(mesh):
    return jax.shard_map(
        body,
        mesh=mesh,
        in_specs=(
            P(("group", "seq"), None, "chan"),
            P("seq", None, "chan"),
            P(),
            P("group", None),
            P(None, None, "chan"),
            P("seq", "chan"),
            P("chan"),
        ),
        out_specs=P(("group", "seq"), "chan"),
        check_vma=False,
    )
```

```python
import math

import jax
import jax.numpy as jnp
from jax import lax
from jax.sharding import PartitionSpec as P

TAPS = 3
BLK = 8


def from_behind(shard, axis, by):
    count = lax.axis_size(axis)
    pairs = [(i, i + by) for i in range(count) if 0 <= i + by < count]
    return lax.ppermute(shard, axis, pairs)


def exact_dot(pattern, matrix, tensor):
    return jnp.einsum(pattern, matrix, tensor, precision=lax.Precision.HIGHEST)


def turn_angles(numbers, period):
    return (numbers % period).astype(jnp.float32) * (2.0 * math.pi / period)


def ring_body(fresh, library, block_slot, prefix_blocks, short_taps, long_filter, skip_gain):
    row_count = fresh.shape[0]
    channels = fresh.shape[2]
    devices = lax.axis_size("seq")
    seq_index = lax.axis_index("seq")
    group_rows = row_count // devices
    period = 2 * row_count * devices
    block_ids = jnp.arange(devices, dtype=jnp.int32)
    mode_ids = jnp.arange(2 * devices, dtype=jnp.int32)
    coarse = turn_angles(mode_ids[:, None] * block_ids[None, :], 2 * devices)
    cos_q = jnp.cos(coarse)
    sin_q = jnp.sin(coarse)
    local_rows = seq_index * group_rows + jnp.arange(group_rows, dtype=jnp.int32)
    twist = turn_angles(mode_ids[:, None] * local_rows[None, :], period)
    twist_cos = jnp.cos(twist)[:, :, None]
    twist_sin = jnp.sin(twist)[:, :, None]
    row_ids = jnp.arange(row_count, dtype=jnp.int32)
    fine_angles = turn_angles(row_ids[:, None] * row_ids[None, :], row_count)
    cos_m = jnp.cos(fine_angles)
    sin_m = jnp.sin(fine_angles)
    first_modes = 2 * seq_index + jnp.arange(2, dtype=jnp.int32)
    back_twist = turn_angles(first_modes[:, None] * row_ids[None, :], period)
    back_cos = jnp.cos(back_twist)[:, :, None]
    back_sin = jnp.sin(back_twist)[:, :, None]

    def to_modes(column):
        real_part = exact_dot("kq,qgc->kgc", cos_q, column)
        imag_part = -exact_dot("kq,qgc->kgc", sin_q, column)
        return jnp.stack(
            [
                real_part * twist_cos + imag_part * twist_sin,
                imag_part * twist_cos - real_part * twist_sin,
            ]
        )

    def to_spectrum(spread):
        real_part = exact_dot("ki,jic->jkc", cos_m, spread[0]) + exact_dot(
            "ki,jic->jkc", sin_m, spread[1]
        )
        imag_part = exact_dot("ki,jic->jkc", cos_m, spread[1]) - exact_dot(
            "ki,jic->jkc", sin_m, spread[0]
        )
        return (real_part, imag_part)

    blocks_here = row_count // BLK
    flat_ids = prefix_blocks.reshape(-1)
    first_block = jnp.minimum(seq_index * blocks_here, flat_ids.shape[0] - blocks_here)
    own_ids = lax.dynamic_slice_in_dim(flat_ids, first_block, blocks_here)
    matches = own_ids[:, None] == jnp.arange(block_slot.shape[0], dtype=jnp.int32)[None, :]
    wanted = jnp.sum(jnp.where(matches, block_slot[None, :], 0), axis=1)
    shards = lax.all_gather(library, "seq", axis=0, tiled=True)
    picker = (wanted[:, None] == jnp.arange(shards.shape[0], dtype=jnp.int32)[None, :]).astype(
        jnp.bfloat16
    )
    gathered = jnp.einsum("bn,nlc->blc", picker, shards, preferred_element_type=jnp.float32)
    cached = gathered.reshape(row_count, channels).astype(jnp.bfloat16)
    values = jnp.where(seq_index < devices // 4, cached, fresh[:, 2])
    stacked = jnp.concatenate([fresh[:, :2], values[:, None]], axis=1)
    previous = from_behind(stacked[row_count - (TAPS - 1) :], "seq", 1)
    extended = jnp.concatenate([previous, stacked], axis=0)
    shortened = jnp.zeros((row_count, 3, channels), jnp.float32)
    for offset in range(TAPS):
        window_start = TAPS - 1 - offset
        shortened = shortened + short_taps[offset][None] * extended[
            window_start : window_start + row_count
        ].astype(jnp.float32)
    gating = shortened[:, 0]
    signal = shortened[:, 1] * shortened[:, 2]
    spread_signal = to_modes(
        lax.all_to_all(signal[None], "seq", split_axis=1, concat_axis=0, tiled=True)
    )
    spread_taps = to_modes(
        lax.all_to_all(long_filter[None], "seq", split_axis=1, concat_axis=0, tiled=True)
    )
    moved_signal, moved_taps = (
        lax.all_to_all(
            spread_signal.astype(jnp.bfloat16), "seq", split_axis=1, concat_axis=2, tiled=True
        ).astype(spread_signal.dtype),
        lax.all_to_all(
            spread_taps.astype(jnp.bfloat16), "seq", split_axis=1, concat_axis=2, tiled=True
        ).astype(spread_taps.dtype),
    )
    sig_real, sig_imag = to_spectrum(moved_signal)
    tap_real, tap_imag = to_spectrum(moved_taps)
    prod_real = sig_real * tap_real - sig_imag * tap_imag
    prod_imag = sig_real * tap_imag + sig_imag * tap_real
    back_real = exact_dot("ki,jic->jkc", cos_m, prod_real) - exact_dot(
        "ki,jic->jkc", sin_m, prod_imag
    )
    back_imag = exact_dot("ki,jic->jkc", cos_m, prod_imag) + exact_dot(
        "ki,jic->jkc", sin_m, prod_real
    )
    turned = jnp.stack(
        [back_real * back_cos - back_imag * back_sin, back_imag * back_cos + back_real * back_sin]
    )
    spread = lax.all_to_all(turned, "seq", split_axis=2, concat_axis=1, tiled=True)
    positions = (
        exact_dot("kq,kgc->qgc", cos_q, spread[0]) - exact_dot("kq,kgc->qgc", sin_q, spread[1])
    ) / period
    convolved = lax.all_to_all(positions, "seq", split_axis=0, concat_axis=1, tiled=True)[0]
    output = gating * (convolved + skip_gain[None, :] * signal)
    return output.astype(jnp.bfloat16)


def exchange(chunk_of, devices):
    seq_index = lax.axis_index("seq")
    arrived = []
    for shift in range(devices):
        block = chunk_of(lax.rem(seq_index + shift, devices))
        if shift:
            block = lax.ppermute(
                block, "seq", [(i, (i + shift) % devices) for i in range(devices)]
            )
        arrived.append(block)
    turned = jnp.stack(arrived[::-1] * 2)
    start = lax.rem(devices - 1 - seq_index + devices, devices)
    return lax.dynamic_slice_in_dim(turned, start, devices, axis=0)


def dft_tables(tokens):
    period = 2 * tokens
    width = 1
    while width * width < tokens:
        width *= 2
    outer = tokens // width
    freqs = jnp.arange(tokens + 1, dtype=jnp.int32)[:, None]
    coarse = turn_angles(freqs * (width * jnp.arange(outer, dtype=jnp.int32))[None, :], period)
    fine = turn_angles(freqs * jnp.arange(width, dtype=jnp.int32)[None, :], period)
    c1, s1 = jnp.cos(coarse)[:, :, None], jnp.sin(coarse)[:, :, None]
    c2, s2 = jnp.cos(fine)[:, None, :], jnp.sin(fine)[:, None, :]
    cos_t = (c1 * c2 - s1 * s2).reshape(tokens + 1, tokens)
    sin_t = (s1 * c2 + c1 * s2).reshape(tokens + 1, tokens)
    return cos_t, sin_t


def local_body(fresh, library, block_slot, prefix_blocks, short_taps, long_filter, skip_gain):
    row_count, _, channels = fresh.shape
    devices = lax.axis_size("seq")
    seq_index = lax.axis_index("seq")
    tokens = row_count * devices
    own = channels // devices
    lib_here = library.shape[0]
    lib_flat = library.reshape(lib_here * BLK, channels)
    lib_rows = -(-lib_here * BLK // 3)
    lib_flat = jnp.pad(lib_flat, ((0, 3 * lib_rows - lib_here * BLK), (0, 0)))
    packed = jnp.concatenate([fresh[:, 1:], long_filter.astype(jnp.bfloat16)[:, None, :]], axis=1)
    packed = jnp.concatenate([packed, lib_flat.reshape(lib_rows, 3, channels)], axis=0)
    moved = exchange(
        lambda d: lax.dynamic_slice_in_dim(packed, d * own, own, axis=2), devices
    )
    rows = moved[:, :row_count].reshape(tokens, 3, own)
    lib_all = moved[:, row_count:].reshape(devices, 3 * lib_rows, own)[:, : lib_here * BLK]
    lib_all = lib_all.reshape(devices * lib_here, BLK * own)

    gate_in = fresh[:, 0].astype(jnp.float32)
    gate_prev = from_behind(fresh[row_count - (TAPS - 1) :, 0], "seq", 1).astype(jnp.float32)
    gate_ext = jnp.concatenate([gate_prev, gate_in], axis=0)
    gating = jnp.zeros((row_count, channels), jnp.float32)
    for offset in range(TAPS):
        window_start = TAPS - 1 - offset
        gating = gating + short_taps[offset, 0][None] * gate_ext[
            window_start : window_start + row_count
        ]

    slot_ids = block_slot[prefix_blocks.reshape(-1)]
    prefix_len = slot_ids.shape[0] * BLK
    picker = (slot_ids[:, None] == jnp.arange(lib_all.shape[0], dtype=jnp.int32)[None, :]).astype(
        jnp.bfloat16
    )
    cached = jnp.dot(picker, lib_all, preferred_element_type=jnp.float32)
    cached = cached.reshape(prefix_len, own).astype(jnp.bfloat16)
    values = jnp.concatenate([cached, rows[prefix_len:, 1]], axis=0)
    stacked = jnp.stack([rows[:, 0], values], axis=1).astype(jnp.float32)

    taps = lax.dynamic_slice_in_dim(short_taps[:, 1:], seq_index * own, own, axis=2)
    gain = lax.dynamic_slice_in_dim(skip_gain, seq_index * own, own, axis=0)
    shortened = jnp.zeros((tokens, 2, own), jnp.float32)
    for offset in range(TAPS):
        shifted = jnp.pad(stacked[: tokens - offset], ((offset, 0), (0, 0), (0, 0)))
        shortened = shortened + taps[offset][None] * shifted
    signal = shortened[:, 0] * shortened[:, 1]

    cos_t, sin_t = dft_tables(tokens)
    table = jnp.concatenate([cos_t, sin_t], axis=0).astype(jnp.bfloat16)
    operands = jnp.concatenate([signal.astype(jnp.bfloat16), rows[:, 2]], axis=1)
    spec = jnp.dot(table, operands, preferred_element_type=jnp.float32)
    bins = tokens + 1
    sig_c, tap_c = spec[:bins, :own], spec[:bins, own:]
    sig_s, tap_s = spec[bins:, :own], spec[bins:, own:]
    weight = jnp.where(
        (jnp.arange(bins) == 0) | (jnp.arange(bins) == tokens), 1.0, 2.0
    ).astype(jnp.float32)[:, None] / (2 * tokens)
    real = (sig_c * tap_c - sig_s * tap_s) * weight
    turned = (sig_c * tap_s + sig_s * tap_c) * weight
    back = jnp.concatenate([real, turned], axis=0).astype(jnp.bfloat16)
    convolved = lax.dot_general(
        table, back, (((0,), (0,)), ((), ())), preferred_element_type=jnp.float32
    )
    summed = (convolved + gain[None, :] * signal).astype(jnp.bfloat16)
    summed = lax.all_to_all(
        summed.reshape(devices, row_count, own), "seq", split_axis=0, concat_axis=0, tiled=True
    )
    summed = summed.transpose(1, 0, 2).reshape(row_count, channels)
    return (gating * summed.astype(jnp.float32)).astype(jnp.bfloat16)


def signal_body(fresh, library, block_slot, prefix_blocks, short_taps, long_filter, skip_gain):
    row_count, _, channels = fresh.shape
    devices = lax.axis_size("seq")
    seq_index = lax.axis_index("seq")
    tokens = row_count * devices
    own = channels // devices
    lib_here = library.shape[0]
    prefix_len = prefix_blocks.size * BLK
    prefix_devices = prefix_len // row_count

    fresh32 = fresh.astype(jnp.float32)
    local = jnp.zeros((row_count, 2, channels), jnp.float32)
    for offset in range(TAPS):
        shifted = jnp.pad(fresh32[: row_count - offset, 1:], ((offset, 0), (0, 0), (0, 0)))
        local = local + short_taps[offset, 1:][None] * shifted
    sent = jnp.where(seq_index < prefix_devices, local[:, 0], local[:, 0] * local[:, 1])
    edges = jnp.concatenate([fresh[: TAPS - 1, 1:], fresh[row_count - (TAPS - 1) :, 1:]], axis=0)
    packed = jnp.stack([sent.astype(jnp.bfloat16), long_filter.astype(jnp.bfloat16)], axis=0)
    lib_rows = lib_here * BLK // 2
    packed = jnp.concatenate(
        [packed, edges.transpose(1, 0, 2), library.reshape(2, lib_rows, channels)], axis=1
    )
    moved = exchange(
        lambda d: lax.dynamic_slice_in_dim(packed, d * own, own, axis=2), devices
    )
    arrived_rows = moved[:, 0, :row_count].reshape(tokens, own)
    filter_rows = moved[:, 1, :row_count].reshape(tokens, own)
    edge_rows = moved[:, :, row_count : row_count + 2 * (TAPS - 1)]
    edge_rows = edge_rows.transpose(0, 2, 1, 3).astype(jnp.float32)
    lib_all = moved[:, :, row_count + 2 * (TAPS - 1) :].reshape(devices * lib_here, BLK * own)

    gate_in = fresh32[:, 0]
    gate_prev = from_behind(fresh[row_count - (TAPS - 1) :, 0], "seq", 1).astype(jnp.float32)
    gate_ext = jnp.concatenate([gate_prev, gate_in], axis=0)
    gating = jnp.zeros((row_count, channels), jnp.float32)
    for offset in range(TAPS):
        window_start = TAPS - 1 - offset
        gating = gating + short_taps[offset, 0][None] * gate_ext[
            window_start : window_start + row_count
        ]

    slot_ids = block_slot[prefix_blocks.reshape(-1)]
    picker = (slot_ids[:, None] == jnp.arange(lib_all.shape[0], dtype=jnp.int32)[None, :]).astype(
        jnp.bfloat16
    )
    cached = jnp.dot(picker, lib_all, preferred_element_type=jnp.float32)
    cached = cached.reshape(prefix_len, own).astype(jnp.bfloat16).astype(jnp.float32)

    taps = lax.dynamic_slice_in_dim(short_taps[:, 1:], seq_index * own, own, axis=2)
    gain = lax.dynamic_slice_in_dim(skip_gain, seq_index * own, own, axis=0)
    lib_short = jnp.zeros((prefix_len, own), jnp.float32)
    for offset in range(TAPS):
        lib_short = lib_short + taps[offset, 1][None] * jnp.pad(
            cached[: prefix_len - offset], ((offset, 0), (0, 0))
        )
    arrived = arrived_rows.astype(jnp.float32)
    signal = jnp.concatenate([arrived[:prefix_len] * lib_short, arrived[prefix_len:]], axis=0)

    head = edge_rows[:, : TAPS - 1]
    tail = jnp.pad(edge_rows[:-1, TAPS - 1 :], ((1, 0), (0, 0), (0, 0), (0, 0)))
    window = jnp.concatenate([tail, head], axis=1)
    positions = (
        jnp.arange(devices)[:, None] * row_count + jnp.arange(2 * (TAPS - 1))[None, :] - (TAPS - 1)
    )
    cached_ext = jnp.pad(cached, ((0, 1), (0, 0)))
    lib_at = cached_ext[jnp.clip(positions, 0, prefix_len)]
    values = jnp.where(
        (positions < prefix_len)[:, :, None], lib_at, window[:, :, 1]
    )
    values = jnp.where((positions >= 0)[:, :, None], values, 0.0)
    ones = jnp.where((positions >= 0)[:, :, None], window[:, :, 0], 0.0)
    edge_signal = []
    for row in range(TAPS - 1):
        first = sum(taps[offset, 0][None] * ones[:, TAPS - 1 + row - offset] for offset in range(TAPS))
        second = sum(
            taps[offset, 1][None] * values[:, TAPS - 1 + row - offset] for offset in range(TAPS)
        )
        edge_signal.append(first * second)
    edge_signal = jnp.stack(edge_signal, axis=1)
    signal = signal.reshape(devices, row_count, own)
    signal = jnp.concatenate([edge_signal, signal[:, TAPS - 1 :]], axis=1).reshape(tokens, own)

    cos_t, sin_t = dft_tables(tokens)
    table = jnp.concatenate([cos_t, sin_t], axis=0).astype(jnp.bfloat16)
    operands = jnp.concatenate([signal.astype(jnp.bfloat16), filter_rows], axis=1)
    spec = jnp.dot(table, operands, preferred_element_type=jnp.float32)
    bins = tokens + 1
    sig_c, tap_c = spec[:bins, :own], spec[:bins, own:]
    sig_s, tap_s = spec[bins:, :own], spec[bins:, own:]
    weight = jnp.where(
        (jnp.arange(bins) == 0) | (jnp.arange(bins) == tokens), 1.0, 2.0
    ).astype(jnp.float32)[:, None] / (2 * tokens)
    real = (sig_c * tap_c - sig_s * tap_s) * weight
    turned = (sig_c * tap_s + sig_s * tap_c) * weight
    back = jnp.concatenate([real, turned], axis=0).astype(jnp.bfloat16)
    convolved = lax.dot_general(
        table, back, (((0,), (0,)), ((), ())), preferred_element_type=jnp.float32
    )
    summed = (convolved + gain[None, :] * signal).astype(jnp.bfloat16)
    summed = exchange(
        lambda d: lax.dynamic_slice_in_dim(summed, d * row_count, row_count, axis=0), devices
    )
    summed = summed.transpose(1, 0, 2).reshape(row_count, channels)
    return (gating * summed.astype(jnp.float32)).astype(jnp.bfloat16)


def body(fresh, library, *rest):
    devices = lax.axis_size("seq")
    tokens = fresh.shape[0] * devices
    fits = tokens <= 4096 and fresh.shape[2] % devices == 0
    prefix_len = rest[1].size * BLK
    aligned = prefix_len % fresh.shape[0] == 0 and prefix_len < tokens and fresh.shape[0] >= 2 * TAPS
    if fits and aligned and (library.shape[0] * BLK) % 2 == 0:
        return signal_body(fresh, library, *rest)
    if fits:
        return local_body(fresh, library, *rest)
    return ring_body(fresh, library, *rest)


def solution(mesh):
    return jax.shard_map(
        body,
        mesh=mesh,
        in_specs=(
            P(("group", "seq"), None, "chan"),
            P("seq", None, "chan"),
            P(),
            P("group", None),
            P(None, None, "chan"),
            P("seq", "chan"),
            P("chan"),
        ),
        out_specs=P(("group", "seq"), "chan"),
        check_vma=False,
    )
```

```python
import math

import jax
import jax.numpy as jnp
from jax import lax
from jax.sharding import PartitionSpec as P

TAPS = 3
BLK = 8


def from_behind(shard, axis, by):
    count = lax.axis_size(axis)
    pairs = [(i, i + by) for i in range(count) if 0 <= i + by < count]
    return lax.ppermute(shard, axis, pairs)


def exact_dot(pattern, matrix, tensor):
    return jnp.einsum(pattern, matrix, tensor, precision=lax.Precision.HIGHEST)


def turn_angles(numbers, period):
    return (numbers % period).astype(jnp.float32) * (2.0 * math.pi / period)


def ring_body(fresh, library, block_slot, prefix_blocks, short_taps, long_filter, skip_gain):
    row_count = fresh.shape[0]
    channels = fresh.shape[2]
    devices = lax.axis_size("seq")
    seq_index = lax.axis_index("seq")
    group_rows = row_count // devices
    period = 2 * row_count * devices
    block_ids = jnp.arange(devices, dtype=jnp.int32)
    mode_ids = jnp.arange(2 * devices, dtype=jnp.int32)
    coarse = turn_angles(mode_ids[:, None] * block_ids[None, :], 2 * devices)
    cos_q = jnp.cos(coarse)
    sin_q = jnp.sin(coarse)
    local_rows = seq_index * group_rows + jnp.arange(group_rows, dtype=jnp.int32)
    twist = turn_angles(mode_ids[:, None] * local_rows[None, :], period)
    twist_cos = jnp.cos(twist)[:, :, None]
    twist_sin = jnp.sin(twist)[:, :, None]
    row_ids = jnp.arange(row_count, dtype=jnp.int32)
    fine_angles = turn_angles(row_ids[:, None] * row_ids[None, :], row_count)
    cos_m = jnp.cos(fine_angles)
    sin_m = jnp.sin(fine_angles)
    first_modes = 2 * seq_index + jnp.arange(2, dtype=jnp.int32)
    back_twist = turn_angles(first_modes[:, None] * row_ids[None, :], period)
    back_cos = jnp.cos(back_twist)[:, :, None]
    back_sin = jnp.sin(back_twist)[:, :, None]

    def to_modes(column):
        real_part = exact_dot("kq,qgc->kgc", cos_q, column)
        imag_part = -exact_dot("kq,qgc->kgc", sin_q, column)
        return jnp.stack(
            [
                real_part * twist_cos + imag_part * twist_sin,
                imag_part * twist_cos - real_part * twist_sin,
            ]
        )

    def to_spectrum(spread):
        real_part = exact_dot("ki,jic->jkc", cos_m, spread[0]) + exact_dot(
            "ki,jic->jkc", sin_m, spread[1]
        )
        imag_part = exact_dot("ki,jic->jkc", cos_m, spread[1]) - exact_dot(
            "ki,jic->jkc", sin_m, spread[0]
        )
        return (real_part, imag_part)

    blocks_here = row_count // BLK
    flat_ids = prefix_blocks.reshape(-1)
    first_block = jnp.minimum(seq_index * blocks_here, flat_ids.shape[0] - blocks_here)
    own_ids = lax.dynamic_slice_in_dim(flat_ids, first_block, blocks_here)
    matches = own_ids[:, None] == jnp.arange(block_slot.shape[0], dtype=jnp.int32)[None, :]
    wanted = jnp.sum(jnp.where(matches, block_slot[None, :], 0), axis=1)
    shards = lax.all_gather(library, "seq", axis=0, tiled=True)
    picker = (wanted[:, None] == jnp.arange(shards.shape[0], dtype=jnp.int32)[None, :]).astype(
        jnp.bfloat16
    )
    gathered = jnp.einsum("bn,nlc->blc", picker, shards, preferred_element_type=jnp.float32)
    cached = gathered.reshape(row_count, channels).astype(jnp.bfloat16)
    values = jnp.where(seq_index < devices // 4, cached, fresh[:, 2])
    stacked = jnp.concatenate([fresh[:, :2], values[:, None]], axis=1)
    previous = from_behind(stacked[row_count - (TAPS - 1) :], "seq", 1)
    extended = jnp.concatenate([previous, stacked], axis=0)
    shortened = jnp.zeros((row_count, 3, channels), jnp.float32)
    for offset in range(TAPS):
        window_start = TAPS - 1 - offset
        shortened = shortened + short_taps[offset][None] * extended[
            window_start : window_start + row_count
        ].astype(jnp.float32)
    gating = shortened[:, 0]
    signal = shortened[:, 1] * shortened[:, 2]
    spread_signal = to_modes(
        lax.all_to_all(signal[None], "seq", split_axis=1, concat_axis=0, tiled=True)
    )
    spread_taps = to_modes(
        lax.all_to_all(long_filter[None], "seq", split_axis=1, concat_axis=0, tiled=True)
    )
    moved_signal, moved_taps = (
        lax.all_to_all(
            spread_signal.astype(jnp.bfloat16), "seq", split_axis=1, concat_axis=2, tiled=True
        ).astype(spread_signal.dtype),
        lax.all_to_all(
            spread_taps.astype(jnp.bfloat16), "seq", split_axis=1, concat_axis=2, tiled=True
        ).astype(spread_taps.dtype),
    )
    sig_real, sig_imag = to_spectrum(moved_signal)
    tap_real, tap_imag = to_spectrum(moved_taps)
    prod_real = sig_real * tap_real - sig_imag * tap_imag
    prod_imag = sig_real * tap_imag + sig_imag * tap_real
    back_real = exact_dot("ki,jic->jkc", cos_m, prod_real) - exact_dot(
        "ki,jic->jkc", sin_m, prod_imag
    )
    back_imag = exact_dot("ki,jic->jkc", cos_m, prod_imag) + exact_dot(
        "ki,jic->jkc", sin_m, prod_real
    )
    turned = jnp.stack(
        [back_real * back_cos - back_imag * back_sin, back_imag * back_cos + back_real * back_sin]
    )
    spread = lax.all_to_all(turned, "seq", split_axis=2, concat_axis=1, tiled=True)
    positions = (
        exact_dot("kq,kgc->qgc", cos_q, spread[0]) - exact_dot("kq,kgc->qgc", sin_q, spread[1])
    ) / period
    convolved = lax.all_to_all(positions, "seq", split_axis=0, concat_axis=1, tiled=True)[0]
    output = gating * (convolved + skip_gain[None, :] * signal)
    return output.astype(jnp.bfloat16)


def exchange(chunk_of, devices):
    seq_index = lax.axis_index("seq")
    arrived = []
    for shift in range(devices):
        block = chunk_of(lax.rem(seq_index + shift, devices))
        if shift:
            block = lax.ppermute(
                block, "seq", [(i, (i + shift) % devices) for i in range(devices)]
            )
        arrived.append(block)
    start = lax.rem(devices - 1 - seq_index + devices, devices)

    def order(*blocks):
        turned = jnp.stack(blocks[::-1] * 2)
        return lax.dynamic_slice_in_dim(turned, start, devices, axis=0)

    return jax.tree.map(order, *arrived)


def dft_tables(tokens):
    period = 2 * tokens
    width = 1
    while width * width < tokens:
        width *= 2
    outer = tokens // width
    freqs = jnp.arange(tokens + 1, dtype=jnp.int32)[:, None]
    coarse = turn_angles(freqs * (width * jnp.arange(outer, dtype=jnp.int32))[None, :], period)
    fine = turn_angles(freqs * jnp.arange(width, dtype=jnp.int32)[None, :], period)
    c1, s1 = jnp.cos(coarse)[:, :, None], jnp.sin(coarse)[:, :, None]
    c2, s2 = jnp.cos(fine)[:, None, :], jnp.sin(fine)[:, None, :]
    cos_t = (c1 * c2 - s1 * s2).reshape(tokens + 1, tokens)
    sin_t = (s1 * c2 + c1 * s2).reshape(tokens + 1, tokens)
    return cos_t, sin_t


def local_body(fresh, library, block_slot, prefix_blocks, short_taps, long_filter, skip_gain):
    row_count, _, channels = fresh.shape
    devices = lax.axis_size("seq")
    seq_index = lax.axis_index("seq")
    tokens = row_count * devices
    own = channels // devices
    lib_here = library.shape[0]
    lib_flat = library.reshape(lib_here * BLK, channels)
    lib_rows = -(-lib_here * BLK // 3)
    lib_flat = jnp.pad(lib_flat, ((0, 3 * lib_rows - lib_here * BLK), (0, 0)))
    packed = jnp.concatenate([fresh[:, 1:], long_filter.astype(jnp.bfloat16)[:, None, :]], axis=1)
    packed = jnp.concatenate([packed, lib_flat.reshape(lib_rows, 3, channels)], axis=0)
    moved = exchange(
        lambda d: lax.dynamic_slice_in_dim(packed, d * own, own, axis=2), devices
    )
    rows = moved[:, :row_count].reshape(tokens, 3, own)
    lib_all = moved[:, row_count:].reshape(devices, 3 * lib_rows, own)[:, : lib_here * BLK]
    lib_all = lib_all.reshape(devices * lib_here, BLK * own)

    gate_in = fresh[:, 0].astype(jnp.float32)
    gate_prev = from_behind(fresh[row_count - (TAPS - 1) :, 0], "seq", 1).astype(jnp.float32)
    gate_ext = jnp.concatenate([gate_prev, gate_in], axis=0)
    gating = jnp.zeros((row_count, channels), jnp.float32)
    for offset in range(TAPS):
        window_start = TAPS - 1 - offset
        gating = gating + short_taps[offset, 0][None] * gate_ext[
            window_start : window_start + row_count
        ]

    slot_ids = block_slot[prefix_blocks.reshape(-1)]
    prefix_len = slot_ids.shape[0] * BLK
    picker = (slot_ids[:, None] == jnp.arange(lib_all.shape[0], dtype=jnp.int32)[None, :]).astype(
        jnp.bfloat16
    )
    cached = jnp.dot(picker, lib_all, preferred_element_type=jnp.float32)
    cached = cached.reshape(prefix_len, own).astype(jnp.bfloat16)
    values = jnp.concatenate([cached, rows[prefix_len:, 1]], axis=0)
    stacked = jnp.stack([rows[:, 0], values], axis=1).astype(jnp.float32)

    taps = lax.dynamic_slice_in_dim(short_taps[:, 1:], seq_index * own, own, axis=2)
    gain = lax.dynamic_slice_in_dim(skip_gain, seq_index * own, own, axis=0)
    shortened = jnp.zeros((tokens, 2, own), jnp.float32)
    for offset in range(TAPS):
        shifted = jnp.pad(stacked[: tokens - offset], ((offset, 0), (0, 0), (0, 0)))
        shortened = shortened + taps[offset][None] * shifted
    signal = shortened[:, 0] * shortened[:, 1]

    cos_t, sin_t = dft_tables(tokens)
    table = jnp.concatenate([cos_t, sin_t], axis=0).astype(jnp.bfloat16)
    operands = jnp.concatenate([signal.astype(jnp.bfloat16), rows[:, 2]], axis=1)
    spec = jnp.dot(table, operands, preferred_element_type=jnp.float32)
    bins = tokens + 1
    sig_c, tap_c = spec[:bins, :own], spec[:bins, own:]
    sig_s, tap_s = spec[bins:, :own], spec[bins:, own:]
    weight = jnp.where(
        (jnp.arange(bins) == 0) | (jnp.arange(bins) == tokens), 1.0, 2.0
    ).astype(jnp.float32)[:, None] / (2 * tokens)
    real = (sig_c * tap_c - sig_s * tap_s) * weight
    turned = (sig_c * tap_s + sig_s * tap_c) * weight
    back = jnp.concatenate([real, turned], axis=0).astype(jnp.bfloat16)
    convolved = lax.dot_general(
        table, back, (((0,), (0,)), ((), ())), preferred_element_type=jnp.float32
    )
    summed = (convolved + gain[None, :] * signal).astype(jnp.bfloat16)
    summed = lax.all_to_all(
        summed.reshape(devices, row_count, own), "seq", split_axis=0, concat_axis=0, tiled=True
    )
    summed = summed.transpose(1, 0, 2).reshape(row_count, channels)
    return (gating * summed.astype(jnp.float32)).astype(jnp.bfloat16)


def signal_body(fresh, library, block_slot, prefix_blocks, short_taps, long_filter, skip_gain):
    row_count, _, channels = fresh.shape
    devices = lax.axis_size("seq")
    seq_index = lax.axis_index("seq")
    tokens = row_count * devices
    own = channels // devices
    lib_here = library.shape[0]
    prefix_len = prefix_blocks.size * BLK
    prefix_devices = prefix_len // row_count

    fresh32 = fresh.astype(jnp.float32)
    local = jnp.zeros((row_count, 2, channels), jnp.float32)
    for offset in range(TAPS):
        shifted = jnp.pad(fresh32[: row_count - offset, 1:], ((offset, 0), (0, 0), (0, 0)))
        local = local + short_taps[offset, 1:][None] * shifted
    sent = jnp.where(seq_index < prefix_devices, local[:, 0], local[:, 0] * local[:, 1])
    edges = jnp.concatenate([fresh[: TAPS - 1, 1:], fresh[row_count - (TAPS - 1) :, 1:]], axis=0)
    edge_count = 2 * (TAPS - 1)
    extra = jnp.concatenate(
        [edges.transpose(1, 0, 2).reshape(2 * edge_count, channels), library.reshape(-1, channels)],
        axis=0,
    )
    payload = jnp.concatenate(
        [sent.astype(jnp.bfloat16), long_filter.astype(jnp.bfloat16), extra], axis=0
    )
    moved = exchange(
        lambda d: lax.dynamic_slice_in_dim(payload, d * own, own, axis=1), devices
    )
    arrived_rows = moved[:, :row_count].reshape(tokens, own)
    filter_rows = moved[:, row_count : 2 * row_count].reshape(tokens, own)
    spare = moved[:, 2 * row_count :]
    edge_rows = spare[:, : 2 * edge_count].reshape(devices, 2, edge_count, own)
    edge_rows = edge_rows.transpose(0, 2, 1, 3).astype(jnp.float32)
    lib_all = spare[:, 2 * edge_count :].reshape(devices * lib_here, BLK * own)

    gate_in = fresh32[:, 0]
    gate_prev = from_behind(fresh[row_count - (TAPS - 1) :, 0], "seq", 1).astype(jnp.float32)
    gate_ext = jnp.concatenate([gate_prev, gate_in], axis=0)
    gating = jnp.zeros((row_count, channels), jnp.float32)
    for offset in range(TAPS):
        window_start = TAPS - 1 - offset
        gating = gating + short_taps[offset, 0][None] * gate_ext[
            window_start : window_start + row_count
        ]

    slot_ids = block_slot[prefix_blocks.reshape(-1)]
    picker = (slot_ids[:, None] == jnp.arange(lib_all.shape[0], dtype=jnp.int32)[None, :]).astype(
        jnp.bfloat16
    )
    cached = jnp.dot(picker, lib_all, preferred_element_type=jnp.float32)
    cached = cached.reshape(prefix_len, own).astype(jnp.bfloat16).astype(jnp.float32)

    taps = lax.dynamic_slice_in_dim(short_taps[:, 1:], seq_index * own, own, axis=2)
    gain = lax.dynamic_slice_in_dim(skip_gain, seq_index * own, own, axis=0)
    lib_short = jnp.zeros((prefix_len, own), jnp.float32)
    for offset in range(TAPS):
        lib_short = lib_short + taps[offset, 1][None] * jnp.pad(
            cached[: prefix_len - offset], ((offset, 0), (0, 0))
        )
    arrived = arrived_rows.astype(jnp.float32)
    signal = jnp.concatenate([arrived[:prefix_len] * lib_short, arrived[prefix_len:]], axis=0)

    head = edge_rows[:, : TAPS - 1]
    tail = jnp.pad(edge_rows[:-1, TAPS - 1 :], ((1, 0), (0, 0), (0, 0), (0, 0)))
    window = jnp.concatenate([tail, head], axis=1)
    positions = (
        jnp.arange(devices)[:, None] * row_count + jnp.arange(2 * (TAPS - 1))[None, :] - (TAPS - 1)
    )
    cached_ext = jnp.pad(cached, ((0, 1), (0, 0)))
    lib_at = cached_ext[jnp.clip(positions, 0, prefix_len)]
    values = jnp.where(
        (positions < prefix_len)[:, :, None], lib_at, window[:, :, 1]
    )
    values = jnp.where((positions >= 0)[:, :, None], values, 0.0)
    ones = jnp.where((positions >= 0)[:, :, None], window[:, :, 0], 0.0)
    edge_signal = []
    for row in range(TAPS - 1):
        first = sum(taps[offset, 0][None] * ones[:, TAPS - 1 + row - offset] for offset in range(TAPS))
        second = sum(
            taps[offset, 1][None] * values[:, TAPS - 1 + row - offset] for offset in range(TAPS)
        )
        edge_signal.append(first * second)
    edge_signal = jnp.stack(edge_signal, axis=1)
    signal = signal.reshape(devices, row_count, own)
    signal = jnp.concatenate([edge_signal, signal[:, TAPS - 1 :]], axis=1).reshape(tokens, own)

    cos_t, sin_t = dft_tables(tokens)
    table = jnp.concatenate([cos_t, sin_t], axis=0).astype(jnp.bfloat16)
    operands = jnp.concatenate([signal.astype(jnp.bfloat16), filter_rows], axis=1)
    spec = jnp.dot(table, operands, preferred_element_type=jnp.float32)
    bins = tokens + 1
    sig_c, tap_c = spec[:bins, :own], spec[:bins, own:]
    sig_s, tap_s = spec[bins:, :own], spec[bins:, own:]
    weight = jnp.where(
        (jnp.arange(bins) == 0) | (jnp.arange(bins) == tokens), 1.0, 2.0
    ).astype(jnp.float32)[:, None] / (2 * tokens)
    real = (sig_c * tap_c - sig_s * tap_s) * weight
    turned = (sig_c * tap_s + sig_s * tap_c) * weight
    back = jnp.concatenate([real, turned], axis=0).astype(jnp.bfloat16)
    convolved = lax.dot_general(
        table, back, (((0,), (0,)), ((), ())), preferred_element_type=jnp.float32
    )
    summed = (convolved + gain[None, :] * signal).astype(jnp.bfloat16)
    summed = exchange(
        lambda d: lax.dynamic_slice_in_dim(summed, d * row_count, row_count, axis=0), devices
    )
    summed = summed.transpose(1, 0, 2).reshape(row_count, channels)
    return (gating * summed.astype(jnp.float32)).astype(jnp.bfloat16)


def body(fresh, library, *rest):
    devices = lax.axis_size("seq")
    tokens = fresh.shape[0] * devices
    fits = tokens <= 4096 and fresh.shape[2] % devices == 0
    prefix_len = rest[1].size * BLK
    aligned = prefix_len % fresh.shape[0] == 0 and prefix_len < tokens and fresh.shape[0] >= 2 * TAPS
    if fits and aligned and (library.shape[0] * BLK) % 2 == 0:
        return signal_body(fresh, library, *rest)
    if fits:
        return local_body(fresh, library, *rest)
    return ring_body(fresh, library, *rest)


def solution(mesh):
    return jax.shard_map(
        body,
        mesh=mesh,
        in_specs=(
            P(("group", "seq"), None, "chan"),
            P("seq", None, "chan"),
            P(),
            P("group", None),
            P(None, None, "chan"),
            P("seq", "chan"),
            P("chan"),
        ),
        out_specs=P(("group", "seq"), "chan"),
        check_vma=False,
    )
```

```python
import math

import jax
import jax.numpy as jnp
from jax import lax
from jax.sharding import PartitionSpec as P

TAPS = 3
BLK = 8


def from_behind(shard, axis, by):
    count = lax.axis_size(axis)
    pairs = [(i, i + by) for i in range(count) if 0 <= i + by < count]
    return lax.ppermute(shard, axis, pairs)


def exact_dot(pattern, matrix, tensor):
    return jnp.einsum(pattern, matrix, tensor, precision=lax.Precision.HIGHEST)


def turn_angles(numbers, period):
    return (numbers % period).astype(jnp.float32) * (2.0 * math.pi / period)


def ring_body(fresh, library, block_slot, prefix_blocks, short_taps, long_filter, skip_gain):
    row_count = fresh.shape[0]
    channels = fresh.shape[2]
    devices = lax.axis_size("seq")
    seq_index = lax.axis_index("seq")
    group_rows = row_count // devices
    period = 2 * row_count * devices
    block_ids = jnp.arange(devices, dtype=jnp.int32)
    mode_ids = jnp.arange(2 * devices, dtype=jnp.int32)
    coarse = turn_angles(mode_ids[:, None] * block_ids[None, :], 2 * devices)
    cos_q = jnp.cos(coarse)
    sin_q = jnp.sin(coarse)
    local_rows = seq_index * group_rows + jnp.arange(group_rows, dtype=jnp.int32)
    twist = turn_angles(mode_ids[:, None] * local_rows[None, :], period)
    twist_cos = jnp.cos(twist)[:, :, None]
    twist_sin = jnp.sin(twist)[:, :, None]
    row_ids = jnp.arange(row_count, dtype=jnp.int32)
    fine_angles = turn_angles(row_ids[:, None] * row_ids[None, :], row_count)
    cos_m = jnp.cos(fine_angles)
    sin_m = jnp.sin(fine_angles)
    first_modes = 2 * seq_index + jnp.arange(2, dtype=jnp.int32)
    back_twist = turn_angles(first_modes[:, None] * row_ids[None, :], period)
    back_cos = jnp.cos(back_twist)[:, :, None]
    back_sin = jnp.sin(back_twist)[:, :, None]

    def to_modes(column):
        real_part = exact_dot("kq,qgc->kgc", cos_q, column)
        imag_part = -exact_dot("kq,qgc->kgc", sin_q, column)
        return jnp.stack(
            [
                real_part * twist_cos + imag_part * twist_sin,
                imag_part * twist_cos - real_part * twist_sin,
            ]
        )

    def to_spectrum(spread):
        real_part = exact_dot("ki,jic->jkc", cos_m, spread[0]) + exact_dot(
            "ki,jic->jkc", sin_m, spread[1]
        )
        imag_part = exact_dot("ki,jic->jkc", cos_m, spread[1]) - exact_dot(
            "ki,jic->jkc", sin_m, spread[0]
        )
        return (real_part, imag_part)

    blocks_here = row_count // BLK
    flat_ids = prefix_blocks.reshape(-1)
    first_block = jnp.minimum(seq_index * blocks_here, flat_ids.shape[0] - blocks_here)
    own_ids = lax.dynamic_slice_in_dim(flat_ids, first_block, blocks_here)
    matches = own_ids[:, None] == jnp.arange(block_slot.shape[0], dtype=jnp.int32)[None, :]
    wanted = jnp.sum(jnp.where(matches, block_slot[None, :], 0), axis=1)
    shards = lax.all_gather(library, "seq", axis=0, tiled=True)
    picker = (wanted[:, None] == jnp.arange(shards.shape[0], dtype=jnp.int32)[None, :]).astype(
        jnp.bfloat16
    )
    gathered = jnp.einsum("bn,nlc->blc", picker, shards, preferred_element_type=jnp.float32)
    cached = gathered.reshape(row_count, channels).astype(jnp.bfloat16)
    values = jnp.where(seq_index < devices // 4, cached, fresh[:, 2])
    stacked = jnp.concatenate([fresh[:, :2], values[:, None]], axis=1)
    previous = from_behind(stacked[row_count - (TAPS - 1) :], "seq", 1)
    extended = jnp.concatenate([previous, stacked], axis=0)
    shortened = jnp.zeros((row_count, 3, channels), jnp.float32)
    for offset in range(TAPS):
        window_start = TAPS - 1 - offset
        shortened = shortened + short_taps[offset][None] * extended[
            window_start : window_start + row_count
        ].astype(jnp.float32)
    gating = shortened[:, 0]
    signal = shortened[:, 1] * shortened[:, 2]
    spread_signal = to_modes(
        lax.all_to_all(signal[None], "seq", split_axis=1, concat_axis=0, tiled=True)
    )
    spread_taps = to_modes(
        lax.all_to_all(long_filter[None], "seq", split_axis=1, concat_axis=0, tiled=True)
    )
    moved_signal, moved_taps = (
        lax.all_to_all(
            spread_signal.astype(jnp.bfloat16), "seq", split_axis=1, concat_axis=2, tiled=True
        ).astype(spread_signal.dtype),
        lax.all_to_all(
            spread_taps.astype(jnp.bfloat16), "seq", split_axis=1, concat_axis=2, tiled=True
        ).astype(spread_taps.dtype),
    )
    sig_real, sig_imag = to_spectrum(moved_signal)
    tap_real, tap_imag = to_spectrum(moved_taps)
    prod_real = sig_real * tap_real - sig_imag * tap_imag
    prod_imag = sig_real * tap_imag + sig_imag * tap_real
    back_real = exact_dot("ki,jic->jkc", cos_m, prod_real) - exact_dot(
        "ki,jic->jkc", sin_m, prod_imag
    )
    back_imag = exact_dot("ki,jic->jkc", cos_m, prod_imag) + exact_dot(
        "ki,jic->jkc", sin_m, prod_real
    )
    turned = jnp.stack(
        [back_real * back_cos - back_imag * back_sin, back_imag * back_cos + back_real * back_sin]
    )
    spread = lax.all_to_all(turned, "seq", split_axis=2, concat_axis=1, tiled=True)
    positions = (
        exact_dot("kq,kgc->qgc", cos_q, spread[0]) - exact_dot("kq,kgc->qgc", sin_q, spread[1])
    ) / period
    convolved = lax.all_to_all(positions, "seq", split_axis=0, concat_axis=1, tiled=True)[0]
    output = gating * (convolved + skip_gain[None, :] * signal)
    return output.astype(jnp.bfloat16)


def exchange(chunk_of, devices, rider=None):
    seq_index = lax.axis_index("seq")
    arrived = []
    carried = None
    for shift in range(devices):
        block = chunk_of(lax.rem(seq_index + shift, devices))
        if shift == 1 and rider is not None:
            size = block.shape[0]
            block = jnp.concatenate([block, rider], axis=0)
            block = lax.ppermute(
                block, "seq", [(i, (i + shift) % devices) for i in range(devices)]
            )
            carried = block[size:]
            arrived.append(block[:size])
            continue
        if shift:
            block = lax.ppermute(
                block, "seq", [(i, (i + shift) % devices) for i in range(devices)]
            )
        arrived.append(block)
    turned = jnp.stack(arrived[::-1] * 2)
    start = lax.rem(devices - 1 - seq_index + devices, devices)
    ordered = lax.dynamic_slice_in_dim(turned, start, devices, axis=0)
    if rider is None:
        return ordered
    return ordered, carried


def dft_tables(tokens):
    period = 2 * tokens
    width = 1
    while width * width < tokens:
        width *= 2
    outer = tokens // width
    freqs = jnp.arange(tokens + 1, dtype=jnp.int32)[:, None]
    coarse = turn_angles(freqs * (width * jnp.arange(outer, dtype=jnp.int32))[None, :], period)
    fine = turn_angles(freqs * jnp.arange(width, dtype=jnp.int32)[None, :], period)
    c1, s1 = jnp.cos(coarse)[:, :, None], jnp.sin(coarse)[:, :, None]
    c2, s2 = jnp.cos(fine)[:, None, :], jnp.sin(fine)[:, None, :]
    cos_t = (c1 * c2 - s1 * s2).reshape(tokens + 1, tokens)
    sin_t = (s1 * c2 + c1 * s2).reshape(tokens + 1, tokens)
    return cos_t, sin_t


def local_body(fresh, library, block_slot, prefix_blocks, short_taps, long_filter, skip_gain):
    row_count, _, channels = fresh.shape
    devices = lax.axis_size("seq")
    seq_index = lax.axis_index("seq")
    tokens = row_count * devices
    own = channels // devices
    lib_here = library.shape[0]
    lib_flat = library.reshape(lib_here * BLK, channels)
    lib_rows = -(-lib_here * BLK // 3)
    lib_flat = jnp.pad(lib_flat, ((0, 3 * lib_rows - lib_here * BLK), (0, 0)))
    packed = jnp.concatenate([fresh[:, 1:], long_filter.astype(jnp.bfloat16)[:, None, :]], axis=1)
    packed = jnp.concatenate([packed, lib_flat.reshape(lib_rows, 3, channels)], axis=0)
    halo = fresh[row_count - (TAPS - 1) :, 0].reshape(-1)
    halo_rows = -(-halo.shape[0] // (3 * own))
    halo = jnp.pad(halo, (0, halo_rows * 3 * own - halo.shape[0])).reshape(halo_rows, 3, own)
    moved, halo = exchange(
        lambda d: lax.dynamic_slice_in_dim(packed, d * own, own, axis=2), devices, halo
    )
    halo = halo.reshape(-1)[: (TAPS - 1) * channels].reshape(TAPS - 1, channels)
    rows = moved[:, :row_count].reshape(tokens, 3, own)
    lib_all = moved[:, row_count:].reshape(devices, 3 * lib_rows, own)[:, : lib_here * BLK]
    lib_all = lib_all.reshape(devices * lib_here, BLK * own)

    gate_in = fresh[:, 0].astype(jnp.float32)
    gate_prev = jnp.where(seq_index > 0, halo.astype(jnp.float32), 0.0)
    gate_ext = jnp.concatenate([gate_prev, gate_in], axis=0)
    gating = jnp.zeros((row_count, channels), jnp.float32)
    for offset in range(TAPS):
        window_start = TAPS - 1 - offset
        gating = gating + short_taps[offset, 0][None] * gate_ext[
            window_start : window_start + row_count
        ]

    slot_ids = block_slot[prefix_blocks.reshape(-1)]
    prefix_len = slot_ids.shape[0] * BLK
    picker = (slot_ids[:, None] == jnp.arange(lib_all.shape[0], dtype=jnp.int32)[None, :]).astype(
        jnp.bfloat16
    )
    cached = jnp.dot(picker, lib_all, preferred_element_type=jnp.float32)
    cached = cached.reshape(prefix_len, own).astype(jnp.bfloat16)
    values = jnp.concatenate([cached, rows[prefix_len:, 1]], axis=0)
    stacked = jnp.stack([rows[:, 0], values], axis=1).astype(jnp.float32)

    taps = lax.dynamic_slice_in_dim(short_taps[:, 1:], seq_index * own, own, axis=2)
    gain = lax.dynamic_slice_in_dim(skip_gain, seq_index * own, own, axis=0)
    shortened = jnp.zeros((tokens, 2, own), jnp.float32)
    for offset in range(TAPS):
        shifted = jnp.pad(stacked[: tokens - offset], ((offset, 0), (0, 0), (0, 0)))
        shortened = shortened + taps[offset][None] * shifted
    signal = shortened[:, 0] * shortened[:, 1]

    cos_t, sin_t = dft_tables(tokens)
    table = jnp.concatenate([cos_t, sin_t], axis=0).astype(jnp.bfloat16)
    operands = jnp.concatenate([signal.astype(jnp.bfloat16), rows[:, 2]], axis=1)
    spec = jnp.dot(table, operands, preferred_element_type=jnp.float32)
    bins = tokens + 1
    sig_c, tap_c = spec[:bins, :own], spec[:bins, own:]
    sig_s, tap_s = spec[bins:, :own], spec[bins:, own:]
    weight = jnp.where(
        (jnp.arange(bins) == 0) | (jnp.arange(bins) == tokens), 1.0, 2.0
    ).astype(jnp.float32)[:, None] / (2 * tokens)
    real = (sig_c * tap_c - sig_s * tap_s) * weight
    turned = (sig_c * tap_s + sig_s * tap_c) * weight
    back = jnp.concatenate([real, turned], axis=0).astype(jnp.bfloat16)
    convolved = lax.dot_general(
        table, back, (((0,), (0,)), ((), ())), preferred_element_type=jnp.float32
    )
    summed = (convolved + gain[None, :] * signal).astype(jnp.bfloat16)
    summed = exchange(
        lambda d: lax.dynamic_slice_in_dim(summed, d * row_count, row_count, axis=0), devices
    )
    summed = summed.transpose(1, 0, 2).reshape(row_count, channels)
    return (gating * summed.astype(jnp.float32)).astype(jnp.bfloat16)


def body(fresh, library, *rest):
    devices = lax.axis_size("seq")
    tokens = fresh.shape[0] * devices
    fits = tokens <= 4096 and fresh.shape[2] % devices == 0
    if fits:
        return local_body(fresh, library, *rest)
    return ring_body(fresh, library, *rest)


def solution(mesh):
    return jax.shard_map(
        body,
        mesh=mesh,
        in_specs=(
            P(("group", "seq"), None, "chan"),
            P("seq", None, "chan"),
            P(),
            P("group", None),
            P(None, None, "chan"),
            P("seq", "chan"),
            P("chan"),
        ),
        out_specs=P(("group", "seq"), "chan"),
        check_vma=False,
    )
```

```python
import math

import jax
import jax.numpy as jnp
from jax import lax
from jax.sharding import PartitionSpec as P

TAPS = 3
BLK = 8


def from_behind(shard, axis, by):
    count = lax.axis_size(axis)
    pairs = [(i, i + by) for i in range(count) if 0 <= i + by < count]
    return lax.ppermute(shard, axis, pairs)


def exact_dot(pattern, matrix, tensor):
    return jnp.einsum(pattern, matrix, tensor, precision=lax.Precision.HIGHEST)


def turn_angles(numbers, period):
    return (numbers % period).astype(jnp.float32) * (2.0 * math.pi / period)


def ring_body(fresh, library, block_slot, prefix_blocks, short_taps, long_filter, skip_gain):
    row_count = fresh.shape[0]
    channels = fresh.shape[2]
    devices = lax.axis_size("seq")
    seq_index = lax.axis_index("seq")
    group_rows = row_count // devices
    period = 2 * row_count * devices
    block_ids = jnp.arange(devices, dtype=jnp.int32)
    mode_ids = jnp.arange(2 * devices, dtype=jnp.int32)
    coarse = turn_angles(mode_ids[:, None] * block_ids[None, :], 2 * devices)
    cos_q = jnp.cos(coarse)
    sin_q = jnp.sin(coarse)
    local_rows = seq_index * group_rows + jnp.arange(group_rows, dtype=jnp.int32)
    twist = turn_angles(mode_ids[:, None] * local_rows[None, :], period)
    twist_cos = jnp.cos(twist)[:, :, None]
    twist_sin = jnp.sin(twist)[:, :, None]
    row_ids = jnp.arange(row_count, dtype=jnp.int32)
    fine_angles = turn_angles(row_ids[:, None] * row_ids[None, :], row_count)
    cos_m = jnp.cos(fine_angles)
    sin_m = jnp.sin(fine_angles)
    first_modes = 2 * seq_index + jnp.arange(2, dtype=jnp.int32)
    back_twist = turn_angles(first_modes[:, None] * row_ids[None, :], period)
    back_cos = jnp.cos(back_twist)[:, :, None]
    back_sin = jnp.sin(back_twist)[:, :, None]

    def to_modes(column):
        real_part = exact_dot("kq,qgc->kgc", cos_q, column)
        imag_part = -exact_dot("kq,qgc->kgc", sin_q, column)
        return jnp.stack(
            [
                real_part * twist_cos + imag_part * twist_sin,
                imag_part * twist_cos - real_part * twist_sin,
            ]
        )

    def to_spectrum(spread):
        real_part = exact_dot("ki,jic->jkc", cos_m, spread[0]) + exact_dot(
            "ki,jic->jkc", sin_m, spread[1]
        )
        imag_part = exact_dot("ki,jic->jkc", cos_m, spread[1]) - exact_dot(
            "ki,jic->jkc", sin_m, spread[0]
        )
        return (real_part, imag_part)

    blocks_here = row_count // BLK
    flat_ids = prefix_blocks.reshape(-1)
    first_block = jnp.minimum(seq_index * blocks_here, flat_ids.shape[0] - blocks_here)
    own_ids = lax.dynamic_slice_in_dim(flat_ids, first_block, blocks_here)
    matches = own_ids[:, None] == jnp.arange(block_slot.shape[0], dtype=jnp.int32)[None, :]
    wanted = jnp.sum(jnp.where(matches, block_slot[None, :], 0), axis=1)
    shards = lax.all_gather(library, "seq", axis=0, tiled=True)
    picker = (wanted[:, None] == jnp.arange(shards.shape[0], dtype=jnp.int32)[None, :]).astype(
        jnp.bfloat16
    )
    gathered = jnp.einsum("bn,nlc->blc", picker, shards, preferred_element_type=jnp.float32)
    cached = gathered.reshape(row_count, channels).astype(jnp.bfloat16)
    values = jnp.where(seq_index < devices // 4, cached, fresh[:, 2])
    stacked = jnp.concatenate([fresh[:, :2], values[:, None]], axis=1)
    previous = from_behind(stacked[row_count - (TAPS - 1) :], "seq", 1)
    extended = jnp.concatenate([previous, stacked], axis=0)
    shortened = jnp.zeros((row_count, 3, channels), jnp.float32)
    for offset in range(TAPS):
        window_start = TAPS - 1 - offset
        shortened = shortened + short_taps[offset][None] * extended[
            window_start : window_start + row_count
        ].astype(jnp.float32)
    gating = shortened[:, 0]
    signal = shortened[:, 1] * shortened[:, 2]
    spread_signal = to_modes(
        lax.all_to_all(signal[None], "seq", split_axis=1, concat_axis=0, tiled=True)
    )
    spread_taps = to_modes(
        lax.all_to_all(long_filter[None], "seq", split_axis=1, concat_axis=0, tiled=True)
    )
    moved_signal, moved_taps = (
        lax.all_to_all(
            spread_signal.astype(jnp.bfloat16), "seq", split_axis=1, concat_axis=2, tiled=True
        ).astype(spread_signal.dtype),
        lax.all_to_all(
            spread_taps.astype(jnp.bfloat16), "seq", split_axis=1, concat_axis=2, tiled=True
        ).astype(spread_taps.dtype),
    )
    sig_real, sig_imag = to_spectrum(moved_signal)
    tap_real, tap_imag = to_spectrum(moved_taps)
    prod_real = sig_real * tap_real - sig_imag * tap_imag
    prod_imag = sig_real * tap_imag + sig_imag * tap_real
    back_real = exact_dot("ki,jic->jkc", cos_m, prod_real) - exact_dot(
        "ki,jic->jkc", sin_m, prod_imag
    )
    back_imag = exact_dot("ki,jic->jkc", cos_m, prod_imag) + exact_dot(
        "ki,jic->jkc", sin_m, prod_real
    )
    turned = jnp.stack(
        [back_real * back_cos - back_imag * back_sin, back_imag * back_cos + back_real * back_sin]
    )
    spread = lax.all_to_all(turned, "seq", split_axis=2, concat_axis=1, tiled=True)
    positions = (
        exact_dot("kq,kgc->qgc", cos_q, spread[0]) - exact_dot("kq,kgc->qgc", sin_q, spread[1])
    ) / period
    convolved = lax.all_to_all(positions, "seq", split_axis=0, concat_axis=1, tiled=True)[0]
    output = gating * (convolved + skip_gain[None, :] * signal)
    return output.astype(jnp.bfloat16)


def exchange(chunk_of, devices, rider=None):
    seq_index = lax.axis_index("seq")
    arrived = []
    carried = None
    for shift in range(devices):
        block = chunk_of(lax.rem(seq_index + shift, devices))
        if shift == 1 and rider is not None:
            size = block.shape[0]
            block = jnp.concatenate([block, rider], axis=0)
            block = lax.ppermute(
                block, "seq", [(i, (i + shift) % devices) for i in range(devices)]
            )
            carried = block[size:]
            arrived.append(block[:size])
            continue
        if shift:
            block = lax.ppermute(
                block, "seq", [(i, (i + shift) % devices) for i in range(devices)]
            )
        arrived.append(block)
    turned = jnp.stack(arrived[::-1] * 2)
    start = lax.rem(devices - 1 - seq_index + devices, devices)
    ordered = lax.dynamic_slice_in_dim(turned, start, devices, axis=0)
    if rider is None:
        return ordered
    return ordered, carried


def two_stage_return(blocks, devices):
    seq_index = lax.axis_index("seq")
    lanes = devices // 2
    lane, side = seq_index // 2, seq_index % 2
    grid = blocks.reshape(lanes, 2, *blocks.shape[1:])
    mine = jnp.where(side == 0, grid[:, 0], grid[:, 1])
    theirs = jnp.where(side == 0, grid[:, 1], grid[:, 0])
    theirs = lax.ppermute(theirs, "seq", [(i, i ^ 1) for i in range(devices)])
    paired = jnp.stack([mine, theirs], axis=1)
    arrived = []
    for shift in range(lanes):
        target = lax.rem(lane + shift, lanes)
        block = lax.dynamic_index_in_dim(paired, target, axis=0, keepdims=False)
        if shift:
            block = lax.ppermute(
                block,
                "seq",
                [(i, 2 * (((i // 2) + shift) % lanes) + i % 2) for i in range(devices)],
            )
        arrived.append(block)
    turned = jnp.stack(arrived[::-1] * 2)
    start = lax.rem(lanes - 1 - lane + lanes, lanes)
    ordered = lax.dynamic_slice_in_dim(turned, start, lanes, axis=0)
    ordered = jnp.where(side == 0, ordered, ordered[:, ::-1])
    return ordered.reshape(devices, *blocks.shape[1:])


def dft_tables(tokens):
    period = 2 * tokens
    width = 1
    while width * width < tokens:
        width *= 2
    outer = tokens // width
    freqs = jnp.arange(tokens + 1, dtype=jnp.int32)[:, None]
    coarse = turn_angles(freqs * (width * jnp.arange(outer, dtype=jnp.int32))[None, :], period)
    fine = turn_angles(freqs * jnp.arange(width, dtype=jnp.int32)[None, :], period)
    c1, s1 = jnp.cos(coarse)[:, :, None], jnp.sin(coarse)[:, :, None]
    c2, s2 = jnp.cos(fine)[:, None, :], jnp.sin(fine)[:, None, :]
    cos_t = (c1 * c2 - s1 * s2).reshape(tokens + 1, tokens)
    sin_t = (s1 * c2 + c1 * s2).reshape(tokens + 1, tokens)
    return cos_t, sin_t


def local_body(fresh, library, block_slot, prefix_blocks, short_taps, long_filter, skip_gain):
    row_count, _, channels = fresh.shape
    devices = lax.axis_size("seq")
    seq_index = lax.axis_index("seq")
    tokens = row_count * devices
    own = channels // devices
    lib_here = library.shape[0]
    lib_flat = library.reshape(lib_here * BLK, channels)
    lib_rows = -(-lib_here * BLK // 3)
    lib_flat = jnp.pad(lib_flat, ((0, 3 * lib_rows - lib_here * BLK), (0, 0)))
    packed = jnp.concatenate([fresh[:, 1:], long_filter.astype(jnp.bfloat16)[:, None, :]], axis=1)
    packed = jnp.concatenate([packed, lib_flat.reshape(lib_rows, 3, channels)], axis=0)
    halo = fresh[row_count - (TAPS - 1) :, 0].reshape(-1)
    halo_rows = -(-halo.shape[0] // (3 * own))
    halo = jnp.pad(halo, (0, halo_rows * 3 * own - halo.shape[0])).reshape(halo_rows, 3, own)
    moved, halo = exchange(
        lambda d: lax.dynamic_slice_in_dim(packed, d * own, own, axis=2), devices, halo
    )
    halo = halo.reshape(-1)[: (TAPS - 1) * channels].reshape(TAPS - 1, channels)
    rows = moved[:, :row_count].reshape(tokens, 3, own)
    lib_all = moved[:, row_count:].reshape(devices, 3 * lib_rows, own)[:, : lib_here * BLK]
    lib_all = lib_all.reshape(devices * lib_here, BLK * own)

    gate_in = fresh[:, 0].astype(jnp.float32)
    gate_prev = jnp.where(seq_index > 0, halo.astype(jnp.float32), 0.0)
    gate_ext = jnp.concatenate([gate_prev, gate_in], axis=0)
    gating = jnp.zeros((row_count, channels), jnp.float32)
    for offset in range(TAPS):
        window_start = TAPS - 1 - offset
        gating = gating + short_taps[offset, 0][None] * gate_ext[
            window_start : window_start + row_count
        ]

    slot_ids = block_slot[prefix_blocks.reshape(-1)]
    prefix_len = slot_ids.shape[0] * BLK
    picker = (slot_ids[:, None] == jnp.arange(lib_all.shape[0], dtype=jnp.int32)[None, :]).astype(
        jnp.bfloat16
    )
    cached = jnp.dot(picker, lib_all, preferred_element_type=jnp.float32)
    cached = cached.reshape(prefix_len, own).astype(jnp.bfloat16)
    values = jnp.concatenate([cached, rows[prefix_len:, 1]], axis=0)
    stacked = jnp.stack([rows[:, 0], values], axis=1).astype(jnp.float32)

    taps = lax.dynamic_slice_in_dim(short_taps[:, 1:], seq_index * own, own, axis=2)
    gain = lax.dynamic_slice_in_dim(skip_gain, seq_index * own, own, axis=0)
    shortened = jnp.zeros((tokens, 2, own), jnp.float32)
    for offset in range(TAPS):
        shifted = jnp.pad(stacked[: tokens - offset], ((offset, 0), (0, 0), (0, 0)))
        shortened = shortened + taps[offset][None] * shifted
    signal = shortened[:, 0] * shortened[:, 1]

    cos_t, sin_t = dft_tables(tokens)
    table = jnp.concatenate([cos_t, sin_t], axis=0).astype(jnp.bfloat16)
    operands = jnp.concatenate([signal.astype(jnp.bfloat16), rows[:, 2]], axis=1)
    spec = jnp.dot(table, operands, preferred_element_type=jnp.float32)
    bins = tokens + 1
    sig_c, tap_c = spec[:bins, :own], spec[:bins, own:]
    sig_s, tap_s = spec[bins:, :own], spec[bins:, own:]
    weight = jnp.where(
        (jnp.arange(bins) == 0) | (jnp.arange(bins) == tokens), 1.0, 2.0
    ).astype(jnp.float32)[:, None] / (2 * tokens)
    real = (sig_c * tap_c - sig_s * tap_s) * weight
    turned = (sig_c * tap_s + sig_s * tap_c) * weight
    back = jnp.concatenate([real, turned], axis=0).astype(jnp.bfloat16)
    convolved = lax.dot_general(
        table, back, (((0,), (0,)), ((), ())), preferred_element_type=jnp.float32
    )
    summed = (convolved + gain[None, :] * signal).astype(jnp.bfloat16)
    if devices % 2 == 0:
        summed = two_stage_return(summed.reshape(devices, row_count, own), devices)
    else:
        summed = exchange(
            lambda d: lax.dynamic_slice_in_dim(summed, d * row_count, row_count, axis=0), devices
        )
    summed = summed.transpose(1, 0, 2).reshape(row_count, channels)
    return (gating * summed.astype(jnp.float32)).astype(jnp.bfloat16)


def body(fresh, library, *rest):
    devices = lax.axis_size("seq")
    tokens = fresh.shape[0] * devices
    fits = tokens <= 4096 and fresh.shape[2] % devices == 0
    if fits:
        return local_body(fresh, library, *rest)
    return ring_body(fresh, library, *rest)


def solution(mesh):
    return jax.shard_map(
        body,
        mesh=mesh,
        in_specs=(
            P(("group", "seq"), None, "chan"),
            P("seq", None, "chan"),
            P(),
            P("group", None),
            P(None, None, "chan"),
            P("seq", "chan"),
            P("chan"),
        ),
        out_specs=P(("group", "seq"), "chan"),
        check_vma=False,
    )
```

```python
import math

import jax
import jax.numpy as jnp
from jax import lax
from jax.sharding import PartitionSpec as P

TAPS = 3
BLK = 8


def from_behind(shard, axis, by):
    count = lax.axis_size(axis)
    pairs = [(i, i + by) for i in range(count) if 0 <= i + by < count]
    return lax.ppermute(shard, axis, pairs)


def exact_dot(pattern, matrix, tensor):
    return jnp.einsum(pattern, matrix, tensor, precision=lax.Precision.HIGHEST)


def turn_angles(numbers, period):
    return (numbers % period).astype(jnp.float32) * (2.0 * math.pi / period)


def ring_body(fresh, library, block_slot, prefix_blocks, short_taps, long_filter, skip_gain):
    row_count = fresh.shape[0]
    channels = fresh.shape[2]
    devices = lax.axis_size("seq")
    seq_index = lax.axis_index("seq")
    group_rows = row_count // devices
    period = 2 * row_count * devices
    block_ids = jnp.arange(devices, dtype=jnp.int32)
    mode_ids = jnp.arange(2 * devices, dtype=jnp.int32)
    coarse = turn_angles(mode_ids[:, None] * block_ids[None, :], 2 * devices)
    cos_q = jnp.cos(coarse)
    sin_q = jnp.sin(coarse)
    local_rows = seq_index * group_rows + jnp.arange(group_rows, dtype=jnp.int32)
    twist = turn_angles(mode_ids[:, None] * local_rows[None, :], period)
    twist_cos = jnp.cos(twist)[:, :, None]
    twist_sin = jnp.sin(twist)[:, :, None]
    row_ids = jnp.arange(row_count, dtype=jnp.int32)
    fine_angles = turn_angles(row_ids[:, None] * row_ids[None, :], row_count)
    cos_m = jnp.cos(fine_angles)
    sin_m = jnp.sin(fine_angles)
    first_modes = 2 * seq_index + jnp.arange(2, dtype=jnp.int32)
    back_twist = turn_angles(first_modes[:, None] * row_ids[None, :], period)
    back_cos = jnp.cos(back_twist)[:, :, None]
    back_sin = jnp.sin(back_twist)[:, :, None]

    def to_modes(column):
        real_part = exact_dot("kq,qgc->kgc", cos_q, column)
        imag_part = -exact_dot("kq,qgc->kgc", sin_q, column)
        return jnp.stack(
            [
                real_part * twist_cos + imag_part * twist_sin,
                imag_part * twist_cos - real_part * twist_sin,
            ]
        )

    def to_spectrum(spread):
        real_part = exact_dot("ki,jic->jkc", cos_m, spread[0]) + exact_dot(
            "ki,jic->jkc", sin_m, spread[1]
        )
        imag_part = exact_dot("ki,jic->jkc", cos_m, spread[1]) - exact_dot(
            "ki,jic->jkc", sin_m, spread[0]
        )
        return (real_part, imag_part)

    blocks_here = row_count // BLK
    flat_ids = prefix_blocks.reshape(-1)
    first_block = jnp.minimum(seq_index * blocks_here, flat_ids.shape[0] - blocks_here)
    own_ids = lax.dynamic_slice_in_dim(flat_ids, first_block, blocks_here)
    matches = own_ids[:, None] == jnp.arange(block_slot.shape[0], dtype=jnp.int32)[None, :]
    wanted = jnp.sum(jnp.where(matches, block_slot[None, :], 0), axis=1)
    shards = lax.all_gather(library, "seq", axis=0, tiled=True)
    picker = (wanted[:, None] == jnp.arange(shards.shape[0], dtype=jnp.int32)[None, :]).astype(
        jnp.bfloat16
    )
    gathered = jnp.einsum("bn,nlc->blc", picker, shards, preferred_element_type=jnp.float32)
    cached = gathered.reshape(row_count, channels).astype(jnp.bfloat16)
    values = jnp.where(seq_index < devices // 4, cached, fresh[:, 2])
    stacked = jnp.concatenate([fresh[:, :2], values[:, None]], axis=1)
    previous = from_behind(stacked[row_count - (TAPS - 1) :], "seq", 1)
    extended = jnp.concatenate([previous, stacked], axis=0)
    shortened = jnp.zeros((row_count, 3, channels), jnp.float32)
    for offset in range(TAPS):
        window_start = TAPS - 1 - offset
        shortened = shortened + short_taps[offset][None] * extended[
            window_start : window_start + row_count
        ].astype(jnp.float32)
    gating = shortened[:, 0]
    signal = shortened[:, 1] * shortened[:, 2]
    spread_signal = to_modes(
        lax.all_to_all(signal[None], "seq", split_axis=1, concat_axis=0, tiled=True)
    )
    spread_taps = to_modes(
        lax.all_to_all(long_filter[None], "seq", split_axis=1, concat_axis=0, tiled=True)
    )
    moved_signal, moved_taps = (
        lax.all_to_all(
            spread_signal.astype(jnp.bfloat16), "seq", split_axis=1, concat_axis=2, tiled=True
        ).astype(spread_signal.dtype),
        lax.all_to_all(
            spread_taps.astype(jnp.bfloat16), "seq", split_axis=1, concat_axis=2, tiled=True
        ).astype(spread_taps.dtype),
    )
    sig_real, sig_imag = to_spectrum(moved_signal)
    tap_real, tap_imag = to_spectrum(moved_taps)
    prod_real = sig_real * tap_real - sig_imag * tap_imag
    prod_imag = sig_real * tap_imag + sig_imag * tap_real
    back_real = exact_dot("ki,jic->jkc", cos_m, prod_real) - exact_dot(
        "ki,jic->jkc", sin_m, prod_imag
    )
    back_imag = exact_dot("ki,jic->jkc", cos_m, prod_imag) + exact_dot(
        "ki,jic->jkc", sin_m, prod_real
    )
    turned = jnp.stack(
        [back_real * back_cos - back_imag * back_sin, back_imag * back_cos + back_real * back_sin]
    )
    spread = lax.all_to_all(turned, "seq", split_axis=2, concat_axis=1, tiled=True)
    positions = (
        exact_dot("kq,kgc->qgc", cos_q, spread[0]) - exact_dot("kq,kgc->qgc", sin_q, spread[1])
    ) / period
    convolved = lax.all_to_all(positions, "seq", split_axis=0, concat_axis=1, tiled=True)[0]
    output = gating * (convolved + skip_gain[None, :] * signal)
    return output.astype(jnp.bfloat16)


def exchange(chunk_of, devices, rider=None, by_source=True):
    seq_index = lax.axis_index("seq")
    arrived = []
    carried = None
    for shift in range(devices):
        block = chunk_of(lax.rem(seq_index + shift, devices), shift)
        if shift == 1 and rider is not None:
            size = block.shape[0]
            block = jnp.concatenate([block, rider], axis=0)
            block = lax.ppermute(
                block, "seq", [(i, (i + shift) % devices) for i in range(devices)]
            )
            carried = block[size:]
            arrived.append(block[:size])
            continue
        if shift:
            block = lax.ppermute(
                block, "seq", [(i, (i + shift) % devices) for i in range(devices)]
            )
        arrived.append(block)
    if by_source:
        turned = jnp.stack(arrived[::-1] * 2)
        start = lax.rem(devices - 1 - seq_index + devices, devices)
        ordered = lax.dynamic_slice_in_dim(turned, start, devices, axis=0)
    else:
        ordered = jnp.stack(arrived)
    if rider is None:
        return ordered
    return ordered, carried


def dft_tables(tokens, starts=None, block=None):
    period = 2 * tokens
    width = 1
    while width * width < tokens:
        width *= 2
    outer = tokens // width
    freqs = jnp.arange(tokens + 1, dtype=jnp.int32)[:, None]
    if starts is None:
        coarse_ids = jnp.arange(outer, dtype=jnp.int32)
    else:
        per = block // width
        coarse_ids = (starts[:, None] * per + jnp.arange(per, dtype=jnp.int32)[None, :]).reshape(-1)
    coarse = turn_angles(freqs * (width * coarse_ids)[None, :], period)
    fine = turn_angles(freqs * jnp.arange(width, dtype=jnp.int32)[None, :], period)
    c1, s1 = jnp.cos(coarse)[:, :, None], jnp.sin(coarse)[:, :, None]
    c2, s2 = jnp.cos(fine)[:, None, :], jnp.sin(fine)[:, None, :]
    cos_t = (c1 * c2 - s1 * s2).reshape(tokens + 1, tokens)
    sin_t = (s1 * c2 + c1 * s2).reshape(tokens + 1, tokens)
    return cos_t, sin_t


def local_body(fresh, library, block_slot, prefix_blocks, short_taps, long_filter, skip_gain):
    row_count, _, channels = fresh.shape
    devices = lax.axis_size("seq")
    seq_index = lax.axis_index("seq")
    tokens = row_count * devices
    own = channels // devices
    lib_here = library.shape[0]
    lib_flat = library.reshape(lib_here * BLK, channels)
    lib_rows = -(-lib_here * BLK // 3)
    lib_flat = jnp.pad(lib_flat, ((0, 3 * lib_rows - lib_here * BLK), (0, 0)))
    packed = jnp.concatenate([fresh[:, 1:], long_filter.astype(jnp.bfloat16)[:, None, :]], axis=1)
    packed = jnp.concatenate([packed, lib_flat.reshape(lib_rows, 3, channels)], axis=0)
    halo = fresh[row_count - (TAPS - 1) :, 0].reshape(-1)
    halo_rows = -(-halo.shape[0] // (3 * own))
    halo = jnp.pad(halo, (0, halo_rows * 3 * own - halo.shape[0])).reshape(halo_rows, 3, own)
    moved, halo = exchange(
        lambda d, shift: lax.dynamic_slice_in_dim(packed, d * own, own, axis=2),
        devices,
        halo,
        by_source=False,
    )
    halo = halo.reshape(-1)[: (TAPS - 1) * channels].reshape(TAPS - 1, channels)
    sources = lax.rem(seq_index - jnp.arange(devices, dtype=jnp.int32) + devices, devices)
    rows = moved[:, :row_count]
    lib_all = moved[:, row_count:].reshape(devices, 3 * lib_rows, own)[:, : lib_here * BLK]
    lib_all = lib_all.reshape(devices * lib_here, BLK * own)
    lib_ids = (sources[:, None] * lib_here + jnp.arange(lib_here, dtype=jnp.int32)[None, :]).reshape(-1)

    gate_in = fresh[:, 0].astype(jnp.float32)
    gate_prev = jnp.where(seq_index > 0, halo.astype(jnp.float32), 0.0)
    gate_ext = jnp.concatenate([gate_prev, gate_in], axis=0)
    gating = jnp.zeros((row_count, channels), jnp.float32)
    for offset in range(TAPS):
        window_start = TAPS - 1 - offset
        gating = gating + short_taps[offset, 0][None] * gate_ext[
            window_start : window_start + row_count
        ]

    flat_ids = prefix_blocks.reshape(-1)
    prefix_count = flat_ids.shape[0]
    prefix_len = prefix_count * BLK
    per_block = row_count // BLK
    pos_blocks = sources[:, None] * per_block + jnp.arange(per_block, dtype=jnp.int32)[None, :]
    pos_slots = block_slot[flat_ids[jnp.clip(pos_blocks, 0, prefix_count - 1)]]
    picker = (pos_slots.reshape(-1)[:, None] == lib_ids[None, :]).astype(jnp.bfloat16)
    cached = jnp.dot(picker, lib_all, preferred_element_type=jnp.float32)
    cached = cached.reshape(devices, row_count, own).astype(jnp.bfloat16)
    positions = sources[:, None] * row_count + jnp.arange(row_count, dtype=jnp.int32)[None, :]
    values = jnp.where((positions < prefix_len)[:, :, None], cached, rows[:, :, 1])
    stacked = jnp.stack([rows[:, :, 0], values], axis=2).astype(jnp.float32)

    taps = lax.dynamic_slice_in_dim(short_taps[:, 1:], seq_index * own, own, axis=2)
    gain = lax.dynamic_slice_in_dim(skip_gain, seq_index * own, own, axis=0)
    previous = jnp.roll(stacked[:, row_count - (TAPS - 1) :], -1, axis=0)
    previous = jnp.where((sources == 0)[:, None, None, None], 0.0, previous)
    extended = jnp.concatenate([previous, stacked], axis=1)
    shortened = jnp.zeros((devices, row_count, 2, own), jnp.float32)
    for offset in range(TAPS):
        window_start = TAPS - 1 - offset
        shortened = shortened + taps[offset][None, None] * extended[
            :, window_start : window_start + row_count
        ]
    signal = (shortened[:, :, 0] * shortened[:, :, 1]).reshape(tokens, own)

    cos_t, sin_t = dft_tables(tokens, sources, row_count)
    table = jnp.concatenate([cos_t, sin_t], axis=0).astype(jnp.bfloat16)
    operands = jnp.concatenate([signal.astype(jnp.bfloat16), rows[:, :, 2].reshape(tokens, own)], axis=1)
    spec = jnp.dot(table, operands, preferred_element_type=jnp.float32)
    bins = tokens + 1
    sig_c, tap_c = spec[:bins, :own], spec[:bins, own:]
    sig_s, tap_s = spec[bins:, :own], spec[bins:, own:]
    weight = jnp.where(
        (jnp.arange(bins) == 0) | (jnp.arange(bins) == tokens), 1.0, 2.0
    ).astype(jnp.float32)[:, None] / (2 * tokens)
    real = (sig_c * tap_c - sig_s * tap_s) * weight
    turned = (sig_c * tap_s + sig_s * tap_c) * weight
    back = jnp.concatenate([real, turned], axis=0).astype(jnp.bfloat16)
    convolved = lax.dot_general(
        table, back, (((0,), (0,)), ((), ())), preferred_element_type=jnp.float32
    )
    summed = (convolved + gain[None, :] * signal).astype(jnp.bfloat16)
    summed = summed.reshape(devices, row_count, own)
    summed = exchange(lambda d, shift: summed[(devices - shift) % devices], devices)
    summed = summed.transpose(1, 0, 2).reshape(row_count, channels)
    return (gating * summed.astype(jnp.float32)).astype(jnp.bfloat16)


def body(fresh, library, *rest):
    devices = lax.axis_size("seq")
    tokens = fresh.shape[0] * devices
    width = 1
    while width * width < tokens:
        width *= 2
    fits = tokens <= 4096 and fresh.shape[2] % devices == 0 and fresh.shape[0] % width == 0
    fits = fits and fresh.shape[0] % BLK == 0 and fresh.shape[0] >= TAPS
    if fits:
        return local_body(fresh, library, *rest)
    return ring_body(fresh, library, *rest)


def solution(mesh):
    return jax.shard_map(
        body,
        mesh=mesh,
        in_specs=(
            P(("group", "seq"), None, "chan"),
            P("seq", None, "chan"),
            P(),
            P("group", None),
            P(None, None, "chan"),
            P("seq", "chan"),
            P("chan"),
        ),
        out_specs=P(("group", "seq"), "chan"),
        check_vma=False,
    )
```

```python
import math

import jax
import jax.numpy as jnp
from jax import lax
from jax.sharding import PartitionSpec as P

TAPS = 3
BLK = 8


def from_behind(shard, axis, by):
    count = lax.axis_size(axis)
    pairs = [(i, i + by) for i in range(count) if 0 <= i + by < count]
    return lax.ppermute(shard, axis, pairs)


def exact_dot(pattern, matrix, tensor):
    return jnp.einsum(pattern, matrix, tensor, precision=lax.Precision.HIGHEST)


def turn_angles(numbers, period):
    return (numbers % period).astype(jnp.float32) * (2.0 * math.pi / period)


def ring_body(fresh, library, block_slot, prefix_blocks, short_taps, long_filter, skip_gain):
    row_count = fresh.shape[0]
    channels = fresh.shape[2]
    devices = lax.axis_size("seq")
    seq_index = lax.axis_index("seq")
    group_rows = row_count // devices
    period = 2 * row_count * devices
    block_ids = jnp.arange(devices, dtype=jnp.int32)
    mode_ids = jnp.arange(2 * devices, dtype=jnp.int32)
    coarse = turn_angles(mode_ids[:, None] * block_ids[None, :], 2 * devices)
    cos_q = jnp.cos(coarse)
    sin_q = jnp.sin(coarse)
    local_rows = seq_index * group_rows + jnp.arange(group_rows, dtype=jnp.int32)
    twist = turn_angles(mode_ids[:, None] * local_rows[None, :], period)
    twist_cos = jnp.cos(twist)[:, :, None]
    twist_sin = jnp.sin(twist)[:, :, None]
    row_ids = jnp.arange(row_count, dtype=jnp.int32)
    fine_angles = turn_angles(row_ids[:, None] * row_ids[None, :], row_count)
    cos_m = jnp.cos(fine_angles)
    sin_m = jnp.sin(fine_angles)
    first_modes = 2 * seq_index + jnp.arange(2, dtype=jnp.int32)
    back_twist = turn_angles(first_modes[:, None] * row_ids[None, :], period)
    back_cos = jnp.cos(back_twist)[:, :, None]
    back_sin = jnp.sin(back_twist)[:, :, None]

    def to_modes(column):
        real_part = exact_dot("kq,qgc->kgc", cos_q, column)
        imag_part = -exact_dot("kq,qgc->kgc", sin_q, column)
        return jnp.stack(
            [
                real_part * twist_cos + imag_part * twist_sin,
                imag_part * twist_cos - real_part * twist_sin,
            ]
        )

    def to_spectrum(spread):
        real_part = exact_dot("ki,jic->jkc", cos_m, spread[0]) + exact_dot(
            "ki,jic->jkc", sin_m, spread[1]
        )
        imag_part = exact_dot("ki,jic->jkc", cos_m, spread[1]) - exact_dot(
            "ki,jic->jkc", sin_m, spread[0]
        )
        return (real_part, imag_part)

    blocks_here = row_count // BLK
    flat_ids = prefix_blocks.reshape(-1)
    first_block = jnp.minimum(seq_index * blocks_here, flat_ids.shape[0] - blocks_here)
    own_ids = lax.dynamic_slice_in_dim(flat_ids, first_block, blocks_here)
    matches = own_ids[:, None] == jnp.arange(block_slot.shape[0], dtype=jnp.int32)[None, :]
    wanted = jnp.sum(jnp.where(matches, block_slot[None, :], 0), axis=1)
    shards = lax.all_gather(library, "seq", axis=0, tiled=True)
    picker = (wanted[:, None] == jnp.arange(shards.shape[0], dtype=jnp.int32)[None, :]).astype(
        jnp.bfloat16
    )
    gathered = jnp.einsum("bn,nlc->blc", picker, shards, preferred_element_type=jnp.float32)
    cached = gathered.reshape(row_count, channels).astype(jnp.bfloat16)
    values = jnp.where(seq_index < devices // 4, cached, fresh[:, 2])
    stacked = jnp.concatenate([fresh[:, :2], values[:, None]], axis=1)
    previous = from_behind(stacked[row_count - (TAPS - 1) :], "seq", 1)
    extended = jnp.concatenate([previous, stacked], axis=0)
    shortened = jnp.zeros((row_count, 3, channels), jnp.float32)
    for offset in range(TAPS):
        window_start = TAPS - 1 - offset
        shortened = shortened + short_taps[offset][None] * extended[
            window_start : window_start + row_count
        ].astype(jnp.float32)
    gating = shortened[:, 0]
    signal = shortened[:, 1] * shortened[:, 2]
    spread_signal = to_modes(
        lax.all_to_all(signal[None], "seq", split_axis=1, concat_axis=0, tiled=True)
    )
    spread_taps = to_modes(
        lax.all_to_all(long_filter[None], "seq", split_axis=1, concat_axis=0, tiled=True)
    )
    moved_signal, moved_taps = (
        lax.all_to_all(
            spread_signal.astype(jnp.bfloat16), "seq", split_axis=1, concat_axis=2, tiled=True
        ).astype(spread_signal.dtype),
        lax.all_to_all(
            spread_taps.astype(jnp.bfloat16), "seq", split_axis=1, concat_axis=2, tiled=True
        ).astype(spread_taps.dtype),
    )
    sig_real, sig_imag = to_spectrum(moved_signal)
    tap_real, tap_imag = to_spectrum(moved_taps)
    prod_real = sig_real * tap_real - sig_imag * tap_imag
    prod_imag = sig_real * tap_imag + sig_imag * tap_real
    back_real = exact_dot("ki,jic->jkc", cos_m, prod_real) - exact_dot(
        "ki,jic->jkc", sin_m, prod_imag
    )
    back_imag = exact_dot("ki,jic->jkc", cos_m, prod_imag) + exact_dot(
        "ki,jic->jkc", sin_m, prod_real
    )
    turned = jnp.stack(
        [back_real * back_cos - back_imag * back_sin, back_imag * back_cos + back_real * back_sin]
    )
    spread = lax.all_to_all(turned, "seq", split_axis=2, concat_axis=1, tiled=True)
    positions = (
        exact_dot("kq,kgc->qgc", cos_q, spread[0]) - exact_dot("kq,kgc->qgc", sin_q, spread[1])
    ) / period
    convolved = lax.all_to_all(positions, "seq", split_axis=0, concat_axis=1, tiled=True)[0]
    output = gating * (convolved + skip_gain[None, :] * signal)
    return output.astype(jnp.bfloat16)


def exchange(chunk_of, devices, rider=None):
    seq_index = lax.axis_index("seq")
    arrived = []
    carried = None
    for shift in range(devices):
        block = chunk_of(lax.rem(seq_index + shift, devices))
        if shift == 1 and rider is not None:
            size = block.shape[0]
            block = jnp.concatenate([block, rider], axis=0)
            block = lax.ppermute(
                block, "seq", [(i, (i + shift) % devices) for i in range(devices)]
            )
            carried = block[size:]
            arrived.append(block[:size])
            continue
        if shift:
            block = lax.ppermute(
                block, "seq", [(i, (i + shift) % devices) for i in range(devices)]
            )
        arrived.append(block)
    picks = lax.rem(seq_index - jnp.arange(devices, dtype=jnp.int32) + devices, devices)
    ordered = jnp.take(jnp.stack(arrived), picks, axis=0, mode="clip")
    if rider is None:
        return ordered
    return ordered, carried


def dft_tables(tokens):
    period = 2 * tokens
    width = 1
    while width * width < tokens:
        width *= 2
    outer = tokens // width
    freqs = jnp.arange(tokens + 1, dtype=jnp.int32)[:, None]
    coarse = turn_angles(freqs * (width * jnp.arange(outer, dtype=jnp.int32))[None, :], period)
    fine = turn_angles(freqs * jnp.arange(width, dtype=jnp.int32)[None, :], period)
    c1, s1 = jnp.cos(coarse)[:, :, None], jnp.sin(coarse)[:, :, None]
    c2, s2 = jnp.cos(fine)[:, None, :], jnp.sin(fine)[:, None, :]
    cos_t = (c1 * c2 - s1 * s2).reshape(tokens + 1, tokens)
    sin_t = (s1 * c2 + c1 * s2).reshape(tokens + 1, tokens)
    return cos_t, sin_t


def local_body(fresh, library, block_slot, prefix_blocks, short_taps, long_filter, skip_gain):
    row_count, _, channels = fresh.shape
    devices = lax.axis_size("seq")
    seq_index = lax.axis_index("seq")
    tokens = row_count * devices
    own = channels // devices
    lib_here = library.shape[0]
    lib_flat = library.reshape(lib_here * BLK, channels)
    lib_rows = -(-lib_here * BLK // 3)
    lib_flat = jnp.pad(lib_flat, ((0, 3 * lib_rows - lib_here * BLK), (0, 0)))
    packed = jnp.concatenate([fresh[:, 1:], long_filter.astype(jnp.bfloat16)[:, None, :]], axis=1)
    packed = jnp.concatenate([packed, lib_flat.reshape(lib_rows, 3, channels)], axis=0)
    halo = fresh[row_count - (TAPS - 1) :, 0].reshape(-1)
    halo_rows = -(-halo.shape[0] // (3 * own))
    halo = jnp.pad(halo, (0, halo_rows * 3 * own - halo.shape[0])).reshape(halo_rows, 3, own)
    moved, halo = exchange(
        lambda d: lax.dynamic_slice_in_dim(packed, d * own, own, axis=2), devices, halo
    )
    halo = halo.reshape(-1)[: (TAPS - 1) * channels].reshape(TAPS - 1, channels)
    rows = moved[:, :row_count].reshape(tokens, 3, own)
    lib_all = moved[:, row_count:].reshape(devices, 3 * lib_rows, own)[:, : lib_here * BLK]
    lib_all = lib_all.reshape(devices * lib_here, BLK * own)

    gate_in = fresh[:, 0].astype(jnp.float32)
    gate_prev = jnp.where(seq_index > 0, halo.astype(jnp.float32), 0.0)
    gate_ext = jnp.concatenate([gate_prev, gate_in], axis=0)
    gating = jnp.zeros((row_count, channels), jnp.float32)
    for offset in range(TAPS):
        window_start = TAPS - 1 - offset
        gating = gating + short_taps[offset, 0][None] * gate_ext[
            window_start : window_start + row_count
        ]

    slot_ids = block_slot[prefix_blocks.reshape(-1)]
    prefix_len = slot_ids.shape[0] * BLK
    picker = (slot_ids[:, None] == jnp.arange(lib_all.shape[0], dtype=jnp.int32)[None, :]).astype(
        jnp.bfloat16
    )
    cached = jnp.dot(picker, lib_all, preferred_element_type=jnp.float32)
    cached = cached.reshape(prefix_len, own).astype(jnp.bfloat16)
    values = jnp.concatenate([cached, rows[prefix_len:, 1]], axis=0)
    stacked = jnp.stack([rows[:, 0], values], axis=1).astype(jnp.float32)

    taps = lax.dynamic_slice_in_dim(short_taps[:, 1:], seq_index * own, own, axis=2)
    gain = lax.dynamic_slice_in_dim(skip_gain, seq_index * own, own, axis=0)
    shortened = jnp.zeros((tokens, 2, own), jnp.float32)
    for offset in range(TAPS):
        shifted = jnp.pad(stacked[: tokens - offset], ((offset, 0), (0, 0), (0, 0)))
        shortened = shortened + taps[offset][None] * shifted
    signal = shortened[:, 0] * shortened[:, 1]

    cos_t, sin_t = dft_tables(tokens)
    table = jnp.concatenate([cos_t, sin_t], axis=0).astype(jnp.bfloat16)
    operands = jnp.concatenate([signal.astype(jnp.bfloat16), rows[:, 2]], axis=1)
    spec = jnp.dot(table, operands, preferred_element_type=jnp.float32)
    bins = tokens + 1
    sig_c, tap_c = spec[:bins, :own], spec[:bins, own:]
    sig_s, tap_s = spec[bins:, :own], spec[bins:, own:]
    weight = jnp.where(
        (jnp.arange(bins) == 0) | (jnp.arange(bins) == tokens), 1.0, 2.0
    ).astype(jnp.float32)[:, None] / (2 * tokens)
    real = (sig_c * tap_c - sig_s * tap_s) * weight
    turned = (sig_c * tap_s + sig_s * tap_c) * weight
    back = jnp.concatenate([real, turned], axis=0).astype(jnp.bfloat16)
    convolved = lax.dot_general(
        table, back, (((0,), (0,)), ((), ())), preferred_element_type=jnp.float32
    )
    summed = (convolved + gain[None, :] * signal).astype(jnp.bfloat16)
    summed = exchange(
        lambda d: lax.dynamic_slice_in_dim(summed, d * row_count, row_count, axis=0), devices
    )
    summed = summed.transpose(1, 0, 2).reshape(row_count, channels)
    return (gating * summed.astype(jnp.float32)).astype(jnp.bfloat16)


def body(fresh, library, *rest):
    devices = lax.axis_size("seq")
    tokens = fresh.shape[0] * devices
    fits = tokens <= 4096 and fresh.shape[2] % devices == 0
    if fits:
        return local_body(fresh, library, *rest)
    return ring_body(fresh, library, *rest)


def solution(mesh):
    return jax.shard_map(
        body,
        mesh=mesh,
        in_specs=(
            P(("group", "seq"), None, "chan"),
            P("seq", None, "chan"),
            P(),
            P("group", None),
            P(None, None, "chan"),
            P("seq", "chan"),
            P("chan"),
        ),
        out_specs=P(("group", "seq"), "chan"),
        check_vma=False,
    )
```

```python
import math

import jax
import jax.numpy as jnp
from jax import lax
from jax.sharding import PartitionSpec as P

TAPS = 3
BLK = 8


def from_behind(shard, axis, by):
    count = lax.axis_size(axis)
    pairs = [(i, i + by) for i in range(count) if 0 <= i + by < count]
    return lax.ppermute(shard, axis, pairs)


def exact_dot(pattern, matrix, tensor):
    return jnp.einsum(pattern, matrix, tensor, precision=lax.Precision.HIGHEST)


def turn_angles(numbers, period):
    return (numbers % period).astype(jnp.float32) * (2.0 * math.pi / period)


def ring_body(fresh, library, block_slot, prefix_blocks, short_taps, long_filter, skip_gain):
    row_count = fresh.shape[0]
    channels = fresh.shape[2]
    devices = lax.axis_size("seq")
    seq_index = lax.axis_index("seq")
    group_rows = row_count // devices
    period = 2 * row_count * devices
    block_ids = jnp.arange(devices, dtype=jnp.int32)
    mode_ids = jnp.arange(2 * devices, dtype=jnp.int32)
    coarse = turn_angles(mode_ids[:, None] * block_ids[None, :], 2 * devices)
    cos_q = jnp.cos(coarse)
    sin_q = jnp.sin(coarse)
    local_rows = seq_index * group_rows + jnp.arange(group_rows, dtype=jnp.int32)
    twist = turn_angles(mode_ids[:, None] * local_rows[None, :], period)
    twist_cos = jnp.cos(twist)[:, :, None]
    twist_sin = jnp.sin(twist)[:, :, None]
    row_ids = jnp.arange(row_count, dtype=jnp.int32)
    fine_angles = turn_angles(row_ids[:, None] * row_ids[None, :], row_count)
    cos_m = jnp.cos(fine_angles)
    sin_m = jnp.sin(fine_angles)
    first_modes = 2 * seq_index + jnp.arange(2, dtype=jnp.int32)
    back_twist = turn_angles(first_modes[:, None] * row_ids[None, :], period)
    back_cos = jnp.cos(back_twist)[:, :, None]
    back_sin = jnp.sin(back_twist)[:, :, None]

    def to_modes(column):
        real_part = exact_dot("kq,qgc->kgc", cos_q, column)
        imag_part = -exact_dot("kq,qgc->kgc", sin_q, column)
        return jnp.stack(
            [
                real_part * twist_cos + imag_part * twist_sin,
                imag_part * twist_cos - real_part * twist_sin,
            ]
        )

    def to_spectrum(spread):
        real_part = exact_dot("ki,jic->jkc", cos_m, spread[0]) + exact_dot(
            "ki,jic->jkc", sin_m, spread[1]
        )
        imag_part = exact_dot("ki,jic->jkc", cos_m, spread[1]) - exact_dot(
            "ki,jic->jkc", sin_m, spread[0]
        )
        return (real_part, imag_part)

    blocks_here = row_count // BLK
    flat_ids = prefix_blocks.reshape(-1)
    first_block = jnp.minimum(seq_index * blocks_here, flat_ids.shape[0] - blocks_here)
    own_ids = lax.dynamic_slice_in_dim(flat_ids, first_block, blocks_here)
    matches = own_ids[:, None] == jnp.arange(block_slot.shape[0], dtype=jnp.int32)[None, :]
    wanted = jnp.sum(jnp.where(matches, block_slot[None, :], 0), axis=1)
    shards = lax.all_gather(library, "seq", axis=0, tiled=True)
    picker = (wanted[:, None] == jnp.arange(shards.shape[0], dtype=jnp.int32)[None, :]).astype(
        jnp.bfloat16
    )
    gathered = jnp.einsum("bn,nlc->blc", picker, shards, preferred_element_type=jnp.float32)
    cached = gathered.reshape(row_count, channels).astype(jnp.bfloat16)
    values = jnp.where(seq_index < devices // 4, cached, fresh[:, 2])
    stacked = jnp.concatenate([fresh[:, :2], values[:, None]], axis=1)
    previous = from_behind(stacked[row_count - (TAPS - 1) :], "seq", 1)
    extended = jnp.concatenate([previous, stacked], axis=0)
    shortened = jnp.zeros((row_count, 3, channels), jnp.float32)
    for offset in range(TAPS):
        window_start = TAPS - 1 - offset
        shortened = shortened + short_taps[offset][None] * extended[
            window_start : window_start + row_count
        ].astype(jnp.float32)
    gating = shortened[:, 0]
    signal = shortened[:, 1] * shortened[:, 2]
    spread_signal = to_modes(
        lax.all_to_all(signal[None], "seq", split_axis=1, concat_axis=0, tiled=True)
    )
    spread_taps = to_modes(
        lax.all_to_all(long_filter[None], "seq", split_axis=1, concat_axis=0, tiled=True)
    )
    moved_signal, moved_taps = (
        lax.all_to_all(
            spread_signal.astype(jnp.bfloat16), "seq", split_axis=1, concat_axis=2, tiled=True
        ).astype(spread_signal.dtype),
        lax.all_to_all(
            spread_taps.astype(jnp.bfloat16), "seq", split_axis=1, concat_axis=2, tiled=True
        ).astype(spread_taps.dtype),
    )
    sig_real, sig_imag = to_spectrum(moved_signal)
    tap_real, tap_imag = to_spectrum(moved_taps)
    prod_real = sig_real * tap_real - sig_imag * tap_imag
    prod_imag = sig_real * tap_imag + sig_imag * tap_real
    back_real = exact_dot("ki,jic->jkc", cos_m, prod_real) - exact_dot(
        "ki,jic->jkc", sin_m, prod_imag
    )
    back_imag = exact_dot("ki,jic->jkc", cos_m, prod_imag) + exact_dot(
        "ki,jic->jkc", sin_m, prod_real
    )
    turned = jnp.stack(
        [back_real * back_cos - back_imag * back_sin, back_imag * back_cos + back_real * back_sin]
    )
    spread = lax.all_to_all(turned, "seq", split_axis=2, concat_axis=1, tiled=True)
    positions = (
        exact_dot("kq,kgc->qgc", cos_q, spread[0]) - exact_dot("kq,kgc->qgc", sin_q, spread[1])
    ) / period
    convolved = lax.all_to_all(positions, "seq", split_axis=0, concat_axis=1, tiled=True)[0]
    output = gating * (convolved + skip_gain[None, :] * signal)
    return output.astype(jnp.bfloat16)


def exchange(chunk_of, devices, rider=None):
    seq_index = lax.axis_index("seq")
    arrived = []
    carried = None
    for shift in range(devices):
        block = chunk_of(lax.rem(seq_index + shift, devices))
        if shift == 1 and rider is not None:
            size = block.shape[0]
            block = jnp.concatenate([block, rider], axis=0)
            block = lax.ppermute(
                block, "seq", [(i, (i + shift) % devices) for i in range(devices)]
            )
            carried = block[size:]
            arrived.append(block[:size])
            continue
        if shift:
            block = lax.ppermute(
                block, "seq", [(i, (i + shift) % devices) for i in range(devices)]
            )
        arrived.append(block)
    turned = jnp.stack(arrived[::-1] * 2)
    start = lax.rem(devices - 1 - seq_index + devices, devices)
    ordered = lax.dynamic_slice_in_dim(turned, start, devices, axis=0)
    if rider is None:
        return ordered
    return ordered, carried


def dft_tables(tokens):
    period = 2 * tokens
    width = 1
    while width * width < tokens:
        width *= 2
    outer = tokens // width
    freqs = jnp.arange(tokens + 1, dtype=jnp.int32)[:, None]
    coarse = turn_angles(freqs * (width * jnp.arange(outer, dtype=jnp.int32))[None, :], period)
    fine = turn_angles(freqs * jnp.arange(width, dtype=jnp.int32)[None, :], period)
    c1, s1 = jnp.cos(coarse)[:, :, None], jnp.sin(coarse)[:, :, None]
    c2, s2 = jnp.cos(fine)[:, None, :], jnp.sin(fine)[:, None, :]
    cos_t = (c1 * c2 - s1 * s2).reshape(tokens + 1, tokens)
    sin_t = (s1 * c2 + c1 * s2).reshape(tokens + 1, tokens)
    return cos_t, sin_t


def local_body(fresh, library, block_slot, prefix_blocks, short_taps, long_filter, skip_gain):
    row_count, _, channels = fresh.shape
    devices = lax.axis_size("seq")
    seq_index = lax.axis_index("seq")
    tokens = row_count * devices
    own = channels // devices
    lib_here = library.shape[0]
    lib_flat = library.reshape(lib_here * BLK, channels)
    lib_rows = -(-lib_here * BLK // 3)
    lib_flat = jnp.pad(lib_flat, ((0, 3 * lib_rows - lib_here * BLK), (0, 0)))
    lib_packed = lib_flat.reshape(lib_rows, 3, channels)

    def chunk_for(d):
        start = d * own
        streams = lax.dynamic_slice_in_dim(fresh[:, 1:], start, own, axis=2)
        taps_here = lax.dynamic_slice_in_dim(long_filter, start, own, axis=1)
        lib_here_rows = lax.dynamic_slice_in_dim(lib_packed, start, own, axis=2)
        block = jnp.concatenate([streams, taps_here.astype(jnp.bfloat16)[:, None, :]], axis=1)
        return jnp.concatenate([block, lib_here_rows], axis=0)

    halo = fresh[row_count - (TAPS - 1) :, 0].reshape(-1)
    halo_rows = -(-halo.shape[0] // (3 * own))
    halo = jnp.pad(halo, (0, halo_rows * 3 * own - halo.shape[0])).reshape(halo_rows, 3, own)
    moved, halo = exchange(chunk_for, devices, halo)
    halo = halo.reshape(-1)[: (TAPS - 1) * channels].reshape(TAPS - 1, channels)
    rows = moved[:, :row_count].reshape(tokens, 3, own)
    lib_all = moved[:, row_count:].reshape(devices, 3 * lib_rows, own)[:, : lib_here * BLK]
    lib_all = lib_all.reshape(devices * lib_here, BLK * own)

    gate_in = fresh[:, 0].astype(jnp.float32)
    gate_prev = jnp.where(seq_index > 0, halo.astype(jnp.float32), 0.0)
    gate_ext = jnp.concatenate([gate_prev, gate_in], axis=0)
    gating = jnp.zeros((row_count, channels), jnp.float32)
    for offset in range(TAPS):
        window_start = TAPS - 1 - offset
        gating = gating + short_taps[offset, 0][None] * gate_ext[
            window_start : window_start + row_count
        ]

    slot_ids = block_slot[prefix_blocks.reshape(-1)]
    prefix_len = slot_ids.shape[0] * BLK
    picker = (slot_ids[:, None] == jnp.arange(lib_all.shape[0], dtype=jnp.int32)[None, :]).astype(
        jnp.bfloat16
    )
    cached = jnp.dot(picker, lib_all, preferred_element_type=jnp.float32)
    cached = cached.reshape(prefix_len, own).astype(jnp.bfloat16)
    values = jnp.concatenate([cached, rows[prefix_len:, 1]], axis=0)
    stacked = jnp.stack([rows[:, 0], values], axis=1).astype(jnp.float32)

    taps = lax.dynamic_slice_in_dim(short_taps[:, 1:], seq_index * own, own, axis=2)
    gain = lax.dynamic_slice_in_dim(skip_gain, seq_index * own, own, axis=0)
    shortened = jnp.zeros((tokens, 2, own), jnp.float32)
    for offset in range(TAPS):
        shifted = jnp.pad(stacked[: tokens - offset], ((offset, 0), (0, 0), (0, 0)))
        shortened = shortened + taps[offset][None] * shifted
    signal = shortened[:, 0] * shortened[:, 1]

    cos_t, sin_t = dft_tables(tokens)
    table = jnp.concatenate([cos_t, sin_t], axis=0).astype(jnp.bfloat16)
    operands = jnp.concatenate([signal.astype(jnp.bfloat16), rows[:, 2]], axis=1)
    spec = jnp.dot(table, operands, preferred_element_type=jnp.float32)
    bins = tokens + 1
    sig_c, tap_c = spec[:bins, :own], spec[:bins, own:]
    sig_s, tap_s = spec[bins:, :own], spec[bins:, own:]
    weight = jnp.where(
        (jnp.arange(bins) == 0) | (jnp.arange(bins) == tokens), 1.0, 2.0
    ).astype(jnp.float32)[:, None] / (2 * tokens)
    real = (sig_c * tap_c - sig_s * tap_s) * weight
    turned = (sig_c * tap_s + sig_s * tap_c) * weight
    back = jnp.concatenate([real, turned], axis=0).astype(jnp.bfloat16)
    convolved = lax.dot_general(
        table, back, (((0,), (0,)), ((), ())), preferred_element_type=jnp.float32
    )
    summed = (convolved + gain[None, :] * signal).astype(jnp.bfloat16)
    summed = exchange(
        lambda d: lax.dynamic_slice_in_dim(summed, d * row_count, row_count, axis=0), devices
    )
    summed = summed.transpose(1, 0, 2).reshape(row_count, channels)
    return (gating * summed.astype(jnp.float32)).astype(jnp.bfloat16)


def body(fresh, library, *rest):
    devices = lax.axis_size("seq")
    tokens = fresh.shape[0] * devices
    fits = tokens <= 4096 and fresh.shape[2] % devices == 0
    if fits:
        return local_body(fresh, library, *rest)
    return ring_body(fresh, library, *rest)


def solution(mesh):
    return jax.shard_map(
        body,
        mesh=mesh,
        in_specs=(
            P(("group", "seq"), None, "chan"),
            P("seq", None, "chan"),
            P(),
            P("group", None),
            P(None, None, "chan"),
            P("seq", "chan"),
            P("chan"),
        ),
        out_specs=P(("group", "seq"), "chan"),
        check_vma=False,
    )
```

```python
import math

import jax
import jax.numpy as jnp
from jax import lax
from jax.sharding import PartitionSpec as P

TAPS = 3
BLK = 8


def from_behind(shard, axis, by):
    count = lax.axis_size(axis)
    pairs = [(i, i + by) for i in range(count) if 0 <= i + by < count]
    return lax.ppermute(shard, axis, pairs)


def exact_dot(pattern, matrix, tensor):
    return jnp.einsum(pattern, matrix, tensor, precision=lax.Precision.HIGHEST)


def turn_angles(numbers, period):
    return (numbers % period).astype(jnp.float32) * (2.0 * math.pi / period)


def ring_body(fresh, library, block_slot, prefix_blocks, short_taps, long_filter, skip_gain):
    row_count = fresh.shape[0]
    channels = fresh.shape[2]
    devices = lax.axis_size("seq")
    seq_index = lax.axis_index("seq")
    group_rows = row_count // devices
    period = 2 * row_count * devices
    block_ids = jnp.arange(devices, dtype=jnp.int32)
    mode_ids = jnp.arange(2 * devices, dtype=jnp.int32)
    coarse = turn_angles(mode_ids[:, None] * block_ids[None, :], 2 * devices)
    cos_q = jnp.cos(coarse)
    sin_q = jnp.sin(coarse)
    local_rows = seq_index * group_rows + jnp.arange(group_rows, dtype=jnp.int32)
    twist = turn_angles(mode_ids[:, None] * local_rows[None, :], period)
    twist_cos = jnp.cos(twist)[:, :, None]
    twist_sin = jnp.sin(twist)[:, :, None]
    row_ids = jnp.arange(row_count, dtype=jnp.int32)
    fine_angles = turn_angles(row_ids[:, None] * row_ids[None, :], row_count)
    cos_m = jnp.cos(fine_angles)
    sin_m = jnp.sin(fine_angles)
    first_modes = 2 * seq_index + jnp.arange(2, dtype=jnp.int32)
    back_twist = turn_angles(first_modes[:, None] * row_ids[None, :], period)
    back_cos = jnp.cos(back_twist)[:, :, None]
    back_sin = jnp.sin(back_twist)[:, :, None]

    def to_modes(column):
        real_part = exact_dot("kq,qgc->kgc", cos_q, column)
        imag_part = -exact_dot("kq,qgc->kgc", sin_q, column)
        return jnp.stack(
            [
                real_part * twist_cos + imag_part * twist_sin,
                imag_part * twist_cos - real_part * twist_sin,
            ]
        )

    def to_spectrum(spread):
        real_part = exact_dot("ki,jic->jkc", cos_m, spread[0]) + exact_dot(
            "ki,jic->jkc", sin_m, spread[1]
        )
        imag_part = exact_dot("ki,jic->jkc", cos_m, spread[1]) - exact_dot(
            "ki,jic->jkc", sin_m, spread[0]
        )
        return (real_part, imag_part)

    blocks_here = row_count // BLK
    flat_ids = prefix_blocks.reshape(-1)
    first_block = jnp.minimum(seq_index * blocks_here, flat_ids.shape[0] - blocks_here)
    own_ids = lax.dynamic_slice_in_dim(flat_ids, first_block, blocks_here)
    matches = own_ids[:, None] == jnp.arange(block_slot.shape[0], dtype=jnp.int32)[None, :]
    wanted = jnp.sum(jnp.where(matches, block_slot[None, :], 0), axis=1)
    shards = lax.all_gather(library, "seq", axis=0, tiled=True)
    picker = (wanted[:, None] == jnp.arange(shards.shape[0], dtype=jnp.int32)[None, :]).astype(
        jnp.bfloat16
    )
    gathered = jnp.einsum("bn,nlc->blc", picker, shards, preferred_element_type=jnp.float32)
    cached = gathered.reshape(row_count, channels).astype(jnp.bfloat16)
    values = jnp.where(seq_index < devices // 4, cached, fresh[:, 2])
    stacked = jnp.concatenate([fresh[:, :2], values[:, None]], axis=1)
    previous = from_behind(stacked[row_count - (TAPS - 1) :], "seq", 1)
    extended = jnp.concatenate([previous, stacked], axis=0)
    shortened = jnp.zeros((row_count, 3, channels), jnp.float32)
    for offset in range(TAPS):
        window_start = TAPS - 1 - offset
        shortened = shortened + short_taps[offset][None] * extended[
            window_start : window_start + row_count
        ].astype(jnp.float32)
    gating = shortened[:, 0]
    signal = shortened[:, 1] * shortened[:, 2]
    spread_signal = to_modes(
        lax.all_to_all(signal[None], "seq", split_axis=1, concat_axis=0, tiled=True)
    )
    spread_taps = to_modes(
        lax.all_to_all(long_filter[None], "seq", split_axis=1, concat_axis=0, tiled=True)
    )
    moved_signal, moved_taps = (
        lax.all_to_all(
            spread_signal.astype(jnp.bfloat16), "seq", split_axis=1, concat_axis=2, tiled=True
        ).astype(spread_signal.dtype),
        lax.all_to_all(
            spread_taps.astype(jnp.bfloat16), "seq", split_axis=1, concat_axis=2, tiled=True
        ).astype(spread_taps.dtype),
    )
    sig_real, sig_imag = to_spectrum(moved_signal)
    tap_real, tap_imag = to_spectrum(moved_taps)
    prod_real = sig_real * tap_real - sig_imag * tap_imag
    prod_imag = sig_real * tap_imag + sig_imag * tap_real
    back_real = exact_dot("ki,jic->jkc", cos_m, prod_real) - exact_dot(
        "ki,jic->jkc", sin_m, prod_imag
    )
    back_imag = exact_dot("ki,jic->jkc", cos_m, prod_imag) + exact_dot(
        "ki,jic->jkc", sin_m, prod_real
    )
    turned = jnp.stack(
        [back_real * back_cos - back_imag * back_sin, back_imag * back_cos + back_real * back_sin]
    )
    spread = lax.all_to_all(turned, "seq", split_axis=2, concat_axis=1, tiled=True)
    positions = (
        exact_dot("kq,kgc->qgc", cos_q, spread[0]) - exact_dot("kq,kgc->qgc", sin_q, spread[1])
    ) / period
    convolved = lax.all_to_all(positions, "seq", split_axis=0, concat_axis=1, tiled=True)[0]
    output = gating * (convolved + skip_gain[None, :] * signal)
    return output.astype(jnp.bfloat16)


def exchange(chunk_of, devices, rider=None):
    seq_index = lax.axis_index("seq")
    arrived = []
    carried = None
    for shift in range(devices):
        block = chunk_of(lax.rem(seq_index + shift, devices))
        if shift == 1 and rider is not None:
            size = block.shape[0]
            block = jnp.concatenate([block, rider], axis=0)
            block = lax.ppermute(
                block, "seq", [(i, (i + shift) % devices) for i in range(devices)]
            )
            carried = block[size:]
            arrived.append(block[:size])
            continue
        if shift:
            block = lax.ppermute(
                block, "seq", [(i, (i + shift) % devices) for i in range(devices)]
            )
        arrived.append(block)
    turned = jnp.stack(arrived[::-1] * 2)
    start = lax.rem(devices - 1 - seq_index + devices, devices)
    ordered = lax.dynamic_slice_in_dim(turned, start, devices, axis=0)
    if rider is None:
        return ordered
    return ordered, carried


def dft_tables(tokens):
    period = 2 * tokens
    width = 1
    while width * width < tokens:
        width *= 2
    outer = tokens // width
    freqs = jnp.arange(tokens + 1, dtype=jnp.int32)[:, None]
    coarse = turn_angles(freqs * (width * jnp.arange(outer, dtype=jnp.int32))[None, :], period)
    fine = turn_angles(freqs * jnp.arange(width, dtype=jnp.int32)[None, :], period)
    c1, s1 = jnp.cos(coarse)[:, :, None], jnp.sin(coarse)[:, :, None]
    c2, s2 = jnp.cos(fine)[:, None, :], jnp.sin(fine)[:, None, :]
    cos_t = (c1 * c2 - s1 * s2).reshape(tokens + 1, tokens)
    sin_t = (s1 * c2 + c1 * s2).reshape(tokens + 1, tokens)
    return cos_t, sin_t


def local_body(fresh, library, block_slot, prefix_blocks, short_taps, long_filter, skip_gain):
    row_count, _, channels = fresh.shape
    devices = lax.axis_size("seq")
    seq_index = lax.axis_index("seq")
    tokens = row_count * devices
    own = channels // devices
    lib_here = library.shape[0]
    lib_flat = library.reshape(lib_here * BLK, channels)
    lib_rows = -(-lib_here * BLK // 3)
    lib_flat = jnp.pad(lib_flat, ((0, 3 * lib_rows - lib_here * BLK), (0, 0)))
    lib_packed = lib_flat.reshape(lib_rows, 3, channels)

    def chunk_for(d):
        start = d * own
        streams = lax.dynamic_slice(fresh, (0, 1, start), (row_count, 2, own))
        taps_here = lax.dynamic_slice_in_dim(long_filter, start, own, axis=1)
        lib_here_rows = lax.dynamic_slice_in_dim(lib_packed, start, own, axis=2)
        block = jnp.concatenate([streams, taps_here.astype(jnp.bfloat16)[:, None, :]], axis=1)
        return jnp.concatenate([block, lib_here_rows], axis=0)

    halo = fresh[row_count - (TAPS - 1) :, 0].reshape(-1)
    halo_rows = -(-halo.shape[0] // (3 * own))
    halo = jnp.pad(halo, (0, halo_rows * 3 * own - halo.shape[0])).reshape(halo_rows, 3, own)
    moved, halo = exchange(chunk_for, devices, halo)
    halo = halo.reshape(-1)[: (TAPS - 1) * channels].reshape(TAPS - 1, channels)
    rows = moved[:, :row_count].reshape(tokens, 3, own)
    lib_all = moved[:, row_count:].reshape(devices, 3 * lib_rows, own)[:, : lib_here * BLK]
    lib_all = lib_all.reshape(devices * lib_here, BLK * own)

    gate_in = fresh[:, 0].astype(jnp.float32)
    gate_prev = jnp.where(seq_index > 0, halo.astype(jnp.float32), 0.0)
    gate_ext = jnp.concatenate([gate_prev, gate_in], axis=0)
    gating = jnp.zeros((row_count, channels), jnp.float32)
    for offset in range(TAPS):
        window_start = TAPS - 1 - offset
        gating = gating + short_taps[offset, 0][None] * gate_ext[
            window_start : window_start + row_count
        ]

    slot_ids = block_slot[prefix_blocks.reshape(-1)]
    prefix_len = slot_ids.shape[0] * BLK
    picker = (slot_ids[:, None] == jnp.arange(lib_all.shape[0], dtype=jnp.int32)[None, :]).astype(
        jnp.bfloat16
    )
    cached = jnp.dot(picker, lib_all, preferred_element_type=jnp.float32)
    cached = cached.reshape(prefix_len, own).astype(jnp.bfloat16)
    values = jnp.concatenate([cached, rows[prefix_len:, 1]], axis=0)
    stacked = jnp.stack([rows[:, 0], values], axis=1).astype(jnp.float32)

    taps = lax.dynamic_slice_in_dim(short_taps[:, 1:], seq_index * own, own, axis=2)
    gain = lax.dynamic_slice_in_dim(skip_gain, seq_index * own, own, axis=0)
    shortened = jnp.zeros((tokens, 2, own), jnp.float32)
    for offset in range(TAPS):
        shifted = jnp.pad(stacked[: tokens - offset], ((offset, 0), (0, 0), (0, 0)))
        shortened = shortened + taps[offset][None] * shifted
    signal = shortened[:, 0] * shortened[:, 1]

    cos_t, sin_t = dft_tables(tokens)
    table = jnp.concatenate([cos_t, sin_t], axis=0).astype(jnp.bfloat16)
    operands = jnp.concatenate([signal.astype(jnp.bfloat16), rows[:, 2]], axis=1)
    spec = jnp.dot(table, operands, preferred_element_type=jnp.float32)
    bins = tokens + 1
    sig_c, tap_c = spec[:bins, :own], spec[:bins, own:]
    sig_s, tap_s = spec[bins:, :own], spec[bins:, own:]
    weight = jnp.where(
        (jnp.arange(bins) == 0) | (jnp.arange(bins) == tokens), 1.0, 2.0
    ).astype(jnp.float32)[:, None] / (2 * tokens)
    real = (sig_c * tap_c - sig_s * tap_s) * weight
    turned = (sig_c * tap_s + sig_s * tap_c) * weight
    back = jnp.concatenate([real, turned], axis=0).astype(jnp.bfloat16)
    convolved = lax.dot_general(
        table, back, (((0,), (0,)), ((), ())), preferred_element_type=jnp.float32
    )
    summed = (convolved + gain[None, :] * signal).astype(jnp.bfloat16)
    summed = exchange(
        lambda d: lax.dynamic_slice_in_dim(summed, d * row_count, row_count, axis=0), devices
    )
    summed = summed.transpose(1, 0, 2).reshape(row_count, channels)
    return (gating * summed.astype(jnp.float32)).astype(jnp.bfloat16)


def body(fresh, library, *rest):
    devices = lax.axis_size("seq")
    tokens = fresh.shape[0] * devices
    fits = tokens <= 4096 and fresh.shape[2] % devices == 0
    if fits:
        return local_body(fresh, library, *rest)
    return ring_body(fresh, library, *rest)


def solution(mesh):
    return jax.shard_map(
        body,
        mesh=mesh,
        in_specs=(
            P(("group", "seq"), None, "chan"),
            P("seq", None, "chan"),
            P(),
            P("group", None),
            P(None, None, "chan"),
            P("seq", "chan"),
            P("chan"),
        ),
        out_specs=P(("group", "seq"), "chan"),
        check_vma=False,
    )
```

```python
import math

import jax
import jax.numpy as jnp
from jax import lax
from jax.sharding import PartitionSpec as P

TAPS = 3
BLK = 8


def from_behind(shard, axis, by):
    count = lax.axis_size(axis)
    pairs = [(i, i + by) for i in range(count) if 0 <= i + by < count]
    return lax.ppermute(shard, axis, pairs)


def exact_dot(pattern, matrix, tensor):
    return jnp.einsum(pattern, matrix, tensor, precision=lax.Precision.HIGHEST)


def turn_angles(numbers, period):
    return (numbers % period).astype(jnp.float32) * (2.0 * math.pi / period)


def ring_body(fresh, library, block_slot, prefix_blocks, short_taps, long_filter, skip_gain):
    row_count = fresh.shape[0]
    channels = fresh.shape[2]
    devices = lax.axis_size("seq")
    seq_index = lax.axis_index("seq")
    group_rows = row_count // devices
    period = 2 * row_count * devices
    block_ids = jnp.arange(devices, dtype=jnp.int32)
    mode_ids = jnp.arange(2 * devices, dtype=jnp.int32)
    coarse = turn_angles(mode_ids[:, None] * block_ids[None, :], 2 * devices)
    cos_q = jnp.cos(coarse)
    sin_q = jnp.sin(coarse)
    local_rows = seq_index * group_rows + jnp.arange(group_rows, dtype=jnp.int32)
    twist = turn_angles(mode_ids[:, None] * local_rows[None, :], period)
    twist_cos = jnp.cos(twist)[:, :, None]
    twist_sin = jnp.sin(twist)[:, :, None]
    row_ids = jnp.arange(row_count, dtype=jnp.int32)
    fine_angles = turn_angles(row_ids[:, None] * row_ids[None, :], row_count)
    cos_m = jnp.cos(fine_angles)
    sin_m = jnp.sin(fine_angles)
    first_modes = 2 * seq_index + jnp.arange(2, dtype=jnp.int32)
    back_twist = turn_angles(first_modes[:, None] * row_ids[None, :], period)
    back_cos = jnp.cos(back_twist)[:, :, None]
    back_sin = jnp.sin(back_twist)[:, :, None]

    def to_modes(column):
        real_part = exact_dot("kq,qgc->kgc", cos_q, column)
        imag_part = -exact_dot("kq,qgc->kgc", sin_q, column)
        return jnp.stack(
            [
                real_part * twist_cos + imag_part * twist_sin,
                imag_part * twist_cos - real_part * twist_sin,
            ]
        )

    def to_spectrum(spread):
        real_part = exact_dot("ki,jic->jkc", cos_m, spread[0]) + exact_dot(
            "ki,jic->jkc", sin_m, spread[1]
        )
        imag_part = exact_dot("ki,jic->jkc", cos_m, spread[1]) - exact_dot(
            "ki,jic->jkc", sin_m, spread[0]
        )
        return (real_part, imag_part)

    blocks_here = row_count // BLK
    flat_ids = prefix_blocks.reshape(-1)
    first_block = jnp.minimum(seq_index * blocks_here, flat_ids.shape[0] - blocks_here)
    own_ids = lax.dynamic_slice_in_dim(flat_ids, first_block, blocks_here)
    matches = own_ids[:, None] == jnp.arange(block_slot.shape[0], dtype=jnp.int32)[None, :]
    wanted = jnp.sum(jnp.where(matches, block_slot[None, :], 0), axis=1)
    shards = lax.all_gather(library, "seq", axis=0, tiled=True)
    picker = (wanted[:, None] == jnp.arange(shards.shape[0], dtype=jnp.int32)[None, :]).astype(
        jnp.bfloat16
    )
    gathered = jnp.einsum("bn,nlc->blc", picker, shards, preferred_element_type=jnp.float32)
    cached = gathered.reshape(row_count, channels).astype(jnp.bfloat16)
    values = jnp.where(seq_index < devices // 4, cached, fresh[:, 2])
    stacked = jnp.concatenate([fresh[:, :2], values[:, None]], axis=1)
    previous = from_behind(stacked[row_count - (TAPS - 1) :], "seq", 1)
    extended = jnp.concatenate([previous, stacked], axis=0)
    shortened = jnp.zeros((row_count, 3, channels), jnp.float32)
    for offset in range(TAPS):
        window_start = TAPS - 1 - offset
        shortened = shortened + short_taps[offset][None] * extended[
            window_start : window_start + row_count
        ].astype(jnp.float32)
    gating = shortened[:, 0]
    signal = shortened[:, 1] * shortened[:, 2]
    spread_signal = to_modes(
        lax.all_to_all(signal[None], "seq", split_axis=1, concat_axis=0, tiled=True)
    )
    spread_taps = to_modes(
        lax.all_to_all(long_filter[None], "seq", split_axis=1, concat_axis=0, tiled=True)
    )
    moved_signal, moved_taps = (
        lax.all_to_all(
            spread_signal.astype(jnp.bfloat16), "seq", split_axis=1, concat_axis=2, tiled=True
        ).astype(spread_signal.dtype),
        lax.all_to_all(
            spread_taps.astype(jnp.bfloat16), "seq", split_axis=1, concat_axis=2, tiled=True
        ).astype(spread_taps.dtype),
    )
    sig_real, sig_imag = to_spectrum(moved_signal)
    tap_real, tap_imag = to_spectrum(moved_taps)
    prod_real = sig_real * tap_real - sig_imag * tap_imag
    prod_imag = sig_real * tap_imag + sig_imag * tap_real
    back_real = exact_dot("ki,jic->jkc", cos_m, prod_real) - exact_dot(
        "ki,jic->jkc", sin_m, prod_imag
    )
    back_imag = exact_dot("ki,jic->jkc", cos_m, prod_imag) + exact_dot(
        "ki,jic->jkc", sin_m, prod_real
    )
    turned = jnp.stack(
        [back_real * back_cos - back_imag * back_sin, back_imag * back_cos + back_real * back_sin]
    )
    spread = lax.all_to_all(turned, "seq", split_axis=2, concat_axis=1, tiled=True)
    positions = (
        exact_dot("kq,kgc->qgc", cos_q, spread[0]) - exact_dot("kq,kgc->qgc", sin_q, spread[1])
    ) / period
    convolved = lax.all_to_all(positions, "seq", split_axis=0, concat_axis=1, tiled=True)[0]
    output = gating * (convolved + skip_gain[None, :] * signal)
    return output.astype(jnp.bfloat16)


def exchange(chunk_of, devices, rider=None):
    seq_index = lax.axis_index("seq")
    arrived = []
    carried = None
    for shift in range(devices):
        block = chunk_of(lax.rem(seq_index + shift, devices))
        if shift == 1 and rider is not None:
            size = block.shape[0]
            block = jnp.concatenate([block, rider], axis=0)
            block = lax.ppermute(
                block, "seq", [(i, (i + shift) % devices) for i in range(devices)]
            )
            carried = block[size:]
            arrived.append(block[:size])
            continue
        if shift:
            block = lax.ppermute(
                block, "seq", [(i, (i + shift) % devices) for i in range(devices)]
            )
        arrived.append(block)
    turned = jnp.stack(arrived[::-1] * 2)
    start = lax.rem(devices - 1 - seq_index + devices, devices)
    ordered = lax.dynamic_slice_in_dim(turned, start, devices, axis=0)
    if rider is None:
        return ordered
    return ordered, carried


def dft_tables(tokens):
    period = 2 * tokens
    width = 1
    while width * width < tokens:
        width *= 2
    outer = tokens // width
    freqs = jnp.arange(tokens + 1, dtype=jnp.int32)[:, None]
    coarse = turn_angles(freqs * (width * jnp.arange(outer, dtype=jnp.int32))[None, :], period)
    fine = turn_angles(freqs * jnp.arange(width, dtype=jnp.int32)[None, :], period)
    c1, s1 = jnp.cos(coarse)[:, :, None], jnp.sin(coarse)[:, :, None]
    c2, s2 = jnp.cos(fine)[:, None, :], jnp.sin(fine)[:, None, :]
    cos_t = (c1 * c2 - s1 * s2).reshape(tokens + 1, tokens)
    sin_t = (s1 * c2 + c1 * s2).reshape(tokens + 1, tokens)
    return cos_t, sin_t


def local_body(fresh, library, block_slot, prefix_blocks, short_taps, long_filter, skip_gain):
    row_count, _, channels = fresh.shape
    devices = lax.axis_size("seq")
    seq_index = lax.axis_index("seq")
    tokens = row_count * devices
    own = channels // devices
    lib_here = library.shape[0]
    lib_flat = library.reshape(lib_here * BLK, channels)
    lib_rows = -(-lib_here * BLK // 3)
    lib_flat = jnp.pad(lib_flat, ((0, 3 * lib_rows - lib_here * BLK), (0, 0)))
    lib_packed = lib_flat.reshape(lib_rows, 3, channels)

    def chunk_for(d):
        start = d * own
        streams = lax.dynamic_slice_in_dim(fresh[:, 1:], start, own, axis=2)
        taps_here = lax.dynamic_slice_in_dim(long_filter, start, own, axis=1)
        lib_here_rows = lax.dynamic_slice_in_dim(lib_packed, start, own, axis=2)
        block = jnp.concatenate([streams, taps_here.astype(jnp.bfloat16)[:, None, :]], axis=1)
        return jnp.concatenate([block, lib_here_rows], axis=0)

    halo = fresh[row_count - (TAPS - 1) :, 0].reshape(-1)
    halo_rows = -(-halo.shape[0] // (3 * own))
    halo = jnp.pad(halo, (0, halo_rows * 3 * own - halo.shape[0])).reshape(halo_rows, 3, own)
    moved, halo = exchange(chunk_for, devices, halo)
    halo = halo.reshape(-1)[: (TAPS - 1) * channels].reshape(TAPS - 1, channels)
    rows = moved[:, :row_count].reshape(tokens, 3, own)
    lib_all = moved[:, row_count:].reshape(devices, 3 * lib_rows, own)[:, : lib_here * BLK]
    lib_all = lib_all.reshape(devices * lib_here, BLK * own)

    gate_in = fresh[:, 0].astype(jnp.float32)
    gate_prev = jnp.where(seq_index > 0, halo.astype(jnp.float32), 0.0)
    gate_ext = jnp.concatenate([gate_prev, gate_in], axis=0)
    gating = jnp.zeros((row_count, channels), jnp.float32)
    for offset in range(TAPS):
        window_start = TAPS - 1 - offset
        gating = gating + short_taps[offset, 0][None] * gate_ext[
            window_start : window_start + row_count
        ]

    slot_ids = block_slot[prefix_blocks.reshape(-1)]
    prefix_len = slot_ids.shape[0] * BLK
    picker = (slot_ids[:, None] == jnp.arange(lib_all.shape[0], dtype=jnp.int32)[None, :]).astype(
        jnp.bfloat16
    )
    cached = jnp.dot(picker, lib_all, preferred_element_type=jnp.float32)
    cached = cached.reshape(prefix_len, own).astype(jnp.bfloat16)
    values = jnp.concatenate([cached, rows[prefix_len:, 1]], axis=0)
    stacked = jnp.stack([rows[:, 0], values], axis=1).astype(jnp.float32)

    taps = lax.dynamic_slice_in_dim(short_taps[:, 1:], seq_index * own, own, axis=2)
    gain = lax.dynamic_slice_in_dim(skip_gain, seq_index * own, own, axis=0)
    shortened = jnp.zeros((tokens, 2, own), jnp.float32)
    for offset in range(TAPS):
        shifted = jnp.pad(stacked[: tokens - offset], ((offset, 0), (0, 0), (0, 0)))
        shortened = shortened + taps[offset][None] * shifted
    signal = shortened[:, 0] * shortened[:, 1]

    cos_t, sin_t = dft_tables(tokens)
    table = jnp.concatenate([cos_t, sin_t], axis=0).astype(jnp.bfloat16)
    operands = jnp.concatenate([signal.astype(jnp.bfloat16), rows[:, 2]], axis=1)
    spec = jnp.dot(table, operands, preferred_element_type=jnp.float32)
    bins = tokens + 1
    sig_c, tap_c = spec[:bins, :own], spec[:bins, own:]
    sig_s, tap_s = spec[bins:, :own], spec[bins:, own:]
    weight = jnp.where(
        (jnp.arange(bins) == 0) | (jnp.arange(bins) == tokens), 1.0, 2.0
    ).astype(jnp.float32)[:, None] / (2 * tokens)
    real = (sig_c * tap_c - sig_s * tap_s) * weight
    turned = (sig_c * tap_s + sig_s * tap_c) * weight
    back = jnp.concatenate([real, turned], axis=0).astype(jnp.bfloat16)
    convolved = lax.dot_general(
        table, back, (((0,), (0,)), ((), ())), preferred_element_type=jnp.float32
    )
    def summed_for(d):
        conv_rows = lax.dynamic_slice_in_dim(convolved, d * row_count, row_count, axis=0)
        sig_rows = lax.dynamic_slice_in_dim(signal, d * row_count, row_count, axis=0)
        return (conv_rows + gain[None, :] * sig_rows).astype(jnp.bfloat16)

    summed = exchange(summed_for, devices)
    summed = summed.transpose(1, 0, 2).reshape(row_count, channels)
    return (gating * summed.astype(jnp.float32)).astype(jnp.bfloat16)


def body(fresh, library, *rest):
    devices = lax.axis_size("seq")
    tokens = fresh.shape[0] * devices
    fits = tokens <= 4096 and fresh.shape[2] % devices == 0
    if fits:
        return local_body(fresh, library, *rest)
    return ring_body(fresh, library, *rest)


def solution(mesh):
    return jax.shard_map(
        body,
        mesh=mesh,
        in_specs=(
            P(("group", "seq"), None, "chan"),
            P("seq", None, "chan"),
            P(),
            P("group", None),
            P(None, None, "chan"),
            P("seq", "chan"),
            P("chan"),
        ),
        out_specs=P(("group", "seq"), "chan"),
        check_vma=False,
    )
```

```python
import math

import jax
import jax.numpy as jnp
from jax import lax
from jax.sharding import PartitionSpec as P

TAPS = 3
BLK = 8


def from_behind(shard, axis, by):
    count = lax.axis_size(axis)
    pairs = [(i, i + by) for i in range(count) if 0 <= i + by < count]
    return lax.ppermute(shard, axis, pairs)


def exact_dot(pattern, matrix, tensor):
    return jnp.einsum(pattern, matrix, tensor, precision=lax.Precision.HIGHEST)


def turn_angles(numbers, period):
    return (numbers % period).astype(jnp.float32) * (2.0 * math.pi / period)


def ring_body(fresh, library, block_slot, prefix_blocks, short_taps, long_filter, skip_gain):
    row_count = fresh.shape[0]
    channels = fresh.shape[2]
    devices = lax.axis_size("seq")
    seq_index = lax.axis_index("seq")
    group_rows = row_count // devices
    period = 2 * row_count * devices
    block_ids = jnp.arange(devices, dtype=jnp.int32)
    mode_ids = jnp.arange(2 * devices, dtype=jnp.int32)
    coarse = turn_angles(mode_ids[:, None] * block_ids[None, :], 2 * devices)
    cos_q = jnp.cos(coarse)
    sin_q = jnp.sin(coarse)
    local_rows = seq_index * group_rows + jnp.arange(group_rows, dtype=jnp.int32)
    twist = turn_angles(mode_ids[:, None] * local_rows[None, :], period)
    twist_cos = jnp.cos(twist)[:, :, None]
    twist_sin = jnp.sin(twist)[:, :, None]
    row_ids = jnp.arange(row_count, dtype=jnp.int32)
    fine_angles = turn_angles(row_ids[:, None] * row_ids[None, :], row_count)
    cos_m = jnp.cos(fine_angles)
    sin_m = jnp.sin(fine_angles)
    first_modes = 2 * seq_index + jnp.arange(2, dtype=jnp.int32)
    back_twist = turn_angles(first_modes[:, None] * row_ids[None, :], period)
    back_cos = jnp.cos(back_twist)[:, :, None]
    back_sin = jnp.sin(back_twist)[:, :, None]

    def to_modes(column):
        real_part = exact_dot("kq,qgc->kgc", cos_q, column)
        imag_part = -exact_dot("kq,qgc->kgc", sin_q, column)
        return jnp.stack(
            [
                real_part * twist_cos + imag_part * twist_sin,
                imag_part * twist_cos - real_part * twist_sin,
            ]
        )

    def to_spectrum(spread):
        real_part = exact_dot("ki,jic->jkc", cos_m, spread[0]) + exact_dot(
            "ki,jic->jkc", sin_m, spread[1]
        )
        imag_part = exact_dot("ki,jic->jkc", cos_m, spread[1]) - exact_dot(
            "ki,jic->jkc", sin_m, spread[0]
        )
        return (real_part, imag_part)

    blocks_here = row_count // BLK
    flat_ids = prefix_blocks.reshape(-1)
    first_block = jnp.minimum(seq_index * blocks_here, flat_ids.shape[0] - blocks_here)
    own_ids = lax.dynamic_slice_in_dim(flat_ids, first_block, blocks_here)
    matches = own_ids[:, None] == jnp.arange(block_slot.shape[0], dtype=jnp.int32)[None, :]
    wanted = jnp.sum(jnp.where(matches, block_slot[None, :], 0), axis=1)
    shards = lax.all_gather(library, "seq", axis=0, tiled=True)
    picker = (wanted[:, None] == jnp.arange(shards.shape[0], dtype=jnp.int32)[None, :]).astype(
        jnp.bfloat16
    )
    gathered = jnp.einsum("bn,nlc->blc", picker, shards, preferred_element_type=jnp.float32)
    cached = gathered.reshape(row_count, channels).astype(jnp.bfloat16)
    values = jnp.where(seq_index < devices // 4, cached, fresh[:, 2])
    stacked = jnp.concatenate([fresh[:, :2], values[:, None]], axis=1)
    previous = from_behind(stacked[row_count - (TAPS - 1) :], "seq", 1)
    extended = jnp.concatenate([previous, stacked], axis=0)
    shortened = jnp.zeros((row_count, 3, channels), jnp.float32)
    for offset in range(TAPS):
        window_start = TAPS - 1 - offset
        shortened = shortened + short_taps[offset][None] * extended[
            window_start : window_start + row_count
        ].astype(jnp.float32)
    gating = shortened[:, 0]
    signal = shortened[:, 1] * shortened[:, 2]
    spread_signal = to_modes(
        lax.all_to_all(signal[None], "seq", split_axis=1, concat_axis=0, tiled=True)
    )
    spread_taps = to_modes(
        lax.all_to_all(long_filter[None], "seq", split_axis=1, concat_axis=0, tiled=True)
    )
    moved_signal, moved_taps = (
        lax.all_to_all(
            spread_signal.astype(jnp.bfloat16), "seq", split_axis=1, concat_axis=2, tiled=True
        ).astype(spread_signal.dtype),
        lax.all_to_all(
            spread_taps.astype(jnp.bfloat16), "seq", split_axis=1, concat_axis=2, tiled=True
        ).astype(spread_taps.dtype),
    )
    sig_real, sig_imag = to_spectrum(moved_signal)
    tap_real, tap_imag = to_spectrum(moved_taps)
    prod_real = sig_real * tap_real - sig_imag * tap_imag
    prod_imag = sig_real * tap_imag + sig_imag * tap_real
    back_real = exact_dot("ki,jic->jkc", cos_m, prod_real) - exact_dot(
        "ki,jic->jkc", sin_m, prod_imag
    )
    back_imag = exact_dot("ki,jic->jkc", cos_m, prod_imag) + exact_dot(
        "ki,jic->jkc", sin_m, prod_real
    )
    turned = jnp.stack(
        [back_real * back_cos - back_imag * back_sin, back_imag * back_cos + back_real * back_sin]
    )
    spread = lax.all_to_all(turned, "seq", split_axis=2, concat_axis=1, tiled=True)
    positions = (
        exact_dot("kq,kgc->qgc", cos_q, spread[0]) - exact_dot("kq,kgc->qgc", sin_q, spread[1])
    ) / period
    convolved = lax.all_to_all(positions, "seq", split_axis=0, concat_axis=1, tiled=True)[0]
    output = gating * (convolved + skip_gain[None, :] * signal)
    return output.astype(jnp.bfloat16)


def exchange(chunk_of, devices, rider=None):
    seq_index = lax.axis_index("seq")
    arrived = []
    carried = None
    for shift in range(devices):
        block = chunk_of(lax.rem(seq_index + shift, devices))
        if shift == 1 and rider is not None:
            size = block.shape[0]
            block = jnp.concatenate([block, rider], axis=0)
            block = lax.ppermute(
                block, "seq", [(i, (i + shift) % devices) for i in range(devices)]
            )
            carried = block[size:]
            arrived.append(block[:size])
            continue
        if shift:
            block = lax.ppermute(
                block, "seq", [(i, (i + shift) % devices) for i in range(devices)]
            )
        arrived.append(block)
    turned = jnp.stack(arrived[::-1] * 2)
    start = lax.rem(devices - 1 - seq_index + devices, devices)
    ordered = lax.dynamic_slice_in_dim(turned, start, devices, axis=0)
    if rider is None:
        return ordered
    return ordered, carried


def dft_tables(tokens):
    period = 2 * tokens
    width = 1
    while width * width < tokens:
        width *= 2
    outer = tokens // width
    freqs = jnp.arange(tokens + 1, dtype=jnp.int32)[:, None]
    coarse = turn_angles(freqs * (width * jnp.arange(outer, dtype=jnp.int32))[None, :], period)
    fine = turn_angles(freqs * jnp.arange(width, dtype=jnp.int32)[None, :], period)
    c1, s1 = jnp.cos(coarse)[:, :, None], jnp.sin(coarse)[:, :, None]
    c2, s2 = jnp.cos(fine)[:, None, :], jnp.sin(fine)[:, None, :]
    c1, s1 = jnp.stack([c1, s1]), jnp.stack([s1, c1])
    both = (c1 * c2[None] + jnp.stack([-s1[0], s1[1]]) * s2[None]).astype(jnp.bfloat16)
    return both.reshape(2 * (tokens + 1), tokens)


def local_body(fresh, library, block_slot, prefix_blocks, short_taps, long_filter, skip_gain):
    row_count, _, channels = fresh.shape
    devices = lax.axis_size("seq")
    seq_index = lax.axis_index("seq")
    tokens = row_count * devices
    own = channels // devices
    lib_here = library.shape[0]
    lib_flat = library.reshape(lib_here * BLK, channels)
    lib_rows = -(-lib_here * BLK // 3)
    lib_flat = jnp.pad(lib_flat, ((0, 3 * lib_rows - lib_here * BLK), (0, 0)))
    lib_packed = lib_flat.reshape(lib_rows, 3, channels)

    def chunk_for(d):
        start = d * own
        streams = lax.dynamic_slice_in_dim(fresh[:, 1:], start, own, axis=2)
        taps_here = lax.dynamic_slice_in_dim(long_filter, start, own, axis=1)
        lib_here_rows = lax.dynamic_slice_in_dim(lib_packed, start, own, axis=2)
        block = jnp.concatenate([streams, taps_here.astype(jnp.bfloat16)[:, None, :]], axis=1)
        return jnp.concatenate([block, lib_here_rows], axis=0)

    halo = fresh[row_count - (TAPS - 1) :, 0].reshape(-1)
    halo_rows = -(-halo.shape[0] // (3 * own))
    halo = jnp.pad(halo, (0, halo_rows * 3 * own - halo.shape[0])).reshape(halo_rows, 3, own)
    moved, halo = exchange(chunk_for, devices, halo)
    halo = halo.reshape(-1)[: (TAPS - 1) * channels].reshape(TAPS - 1, channels)
    rows = moved[:, :row_count].reshape(tokens, 3, own)
    lib_all = moved[:, row_count:].reshape(devices, 3 * lib_rows, own)[:, : lib_here * BLK]
    lib_all = lib_all.reshape(devices * lib_here, BLK * own)

    gate_in = fresh[:, 0].astype(jnp.float32)
    gate_prev = jnp.where(seq_index > 0, halo.astype(jnp.float32), 0.0)
    gate_ext = jnp.concatenate([gate_prev, gate_in], axis=0)
    gating = jnp.zeros((row_count, channels), jnp.float32)
    for offset in range(TAPS):
        window_start = TAPS - 1 - offset
        gating = gating + short_taps[offset, 0][None] * gate_ext[
            window_start : window_start + row_count
        ]

    slot_ids = block_slot[prefix_blocks.reshape(-1)]
    prefix_len = slot_ids.shape[0] * BLK
    picker = (slot_ids[:, None] == jnp.arange(lib_all.shape[0], dtype=jnp.int32)[None, :]).astype(
        jnp.bfloat16
    )
    cached = jnp.dot(picker, lib_all, preferred_element_type=jnp.float32)
    cached = cached.reshape(prefix_len, own).astype(jnp.bfloat16)
    values = jnp.concatenate([cached, rows[prefix_len:, 1]], axis=0)
    stacked = jnp.stack([rows[:, 0], values], axis=1).astype(jnp.float32)

    taps = lax.dynamic_slice_in_dim(short_taps[:, 1:], seq_index * own, own, axis=2)
    gain = lax.dynamic_slice_in_dim(skip_gain, seq_index * own, own, axis=0)
    shortened = jnp.zeros((tokens, 2, own), jnp.float32)
    for offset in range(TAPS):
        shifted = jnp.pad(stacked[: tokens - offset], ((offset, 0), (0, 0), (0, 0)))
        shortened = shortened + taps[offset][None] * shifted
    signal = shortened[:, 0] * shortened[:, 1]

    table = dft_tables(tokens)
    operands = jnp.concatenate([signal.astype(jnp.bfloat16), rows[:, 2]], axis=1)
    spec = jnp.dot(table, operands, preferred_element_type=jnp.float32)
    bins = tokens + 1
    sig_c, tap_c = spec[:bins, :own], spec[:bins, own:]
    sig_s, tap_s = spec[bins:, :own], spec[bins:, own:]
    weight = jnp.where(
        (jnp.arange(bins) == 0) | (jnp.arange(bins) == tokens), 1.0, 2.0
    ).astype(jnp.float32)[:, None] / (2 * tokens)
    real = (sig_c * tap_c - sig_s * tap_s) * weight
    turned = (sig_c * tap_s + sig_s * tap_c) * weight
    back = jnp.concatenate([real, turned], axis=0).astype(jnp.bfloat16)
    convolved = lax.dot_general(
        table, back, (((0,), (0,)), ((), ())), preferred_element_type=jnp.float32
    )
    summed = (convolved + gain[None, :] * signal).astype(jnp.bfloat16)
    summed = exchange(
        lambda d: lax.dynamic_slice_in_dim(summed, d * row_count, row_count, axis=0), devices
    )
    summed = summed.transpose(1, 0, 2).reshape(row_count, channels)
    return (gating * summed.astype(jnp.float32)).astype(jnp.bfloat16)


def body(fresh, library, *rest):
    devices = lax.axis_size("seq")
    tokens = fresh.shape[0] * devices
    fits = tokens <= 4096 and fresh.shape[2] % devices == 0
    if fits:
        return local_body(fresh, library, *rest)
    return ring_body(fresh, library, *rest)


def solution(mesh):
    return jax.shard_map(
        body,
        mesh=mesh,
        in_specs=(
            P(("group", "seq"), None, "chan"),
            P("seq", None, "chan"),
            P(),
            P("group", None),
            P(None, None, "chan"),
            P("seq", "chan"),
            P("chan"),
        ),
        out_specs=P(("group", "seq"), "chan"),
        check_vma=False,
    )
```

```python
import math

import jax
import jax.numpy as jnp
from jax import lax
from jax.sharding import PartitionSpec as P

TAPS = 3
BLK = 8


def from_behind(shard, axis, by):
    count = lax.axis_size(axis)
    pairs = [(i, i + by) for i in range(count) if 0 <= i + by < count]
    return lax.ppermute(shard, axis, pairs)


def exact_dot(pattern, matrix, tensor):
    return jnp.einsum(pattern, matrix, tensor, precision=lax.Precision.HIGHEST)


def turn_angles(numbers, period):
    return (numbers % period).astype(jnp.float32) * (2.0 * math.pi / period)


def ring_body(fresh, library, block_slot, prefix_blocks, short_taps, long_filter, skip_gain):
    row_count = fresh.shape[0]
    channels = fresh.shape[2]
    devices = lax.axis_size("seq")
    seq_index = lax.axis_index("seq")
    group_rows = row_count // devices
    period = 2 * row_count * devices
    block_ids = jnp.arange(devices, dtype=jnp.int32)
    mode_ids = jnp.arange(2 * devices, dtype=jnp.int32)
    coarse = turn_angles(mode_ids[:, None] * block_ids[None, :], 2 * devices)
    cos_q = jnp.cos(coarse)
    sin_q = jnp.sin(coarse)
    local_rows = seq_index * group_rows + jnp.arange(group_rows, dtype=jnp.int32)
    twist = turn_angles(mode_ids[:, None] * local_rows[None, :], period)
    twist_cos = jnp.cos(twist)[:, :, None]
    twist_sin = jnp.sin(twist)[:, :, None]
    row_ids = jnp.arange(row_count, dtype=jnp.int32)
    fine_angles = turn_angles(row_ids[:, None] * row_ids[None, :], row_count)
    cos_m = jnp.cos(fine_angles)
    sin_m = jnp.sin(fine_angles)
    first_modes = 2 * seq_index + jnp.arange(2, dtype=jnp.int32)
    back_twist = turn_angles(first_modes[:, None] * row_ids[None, :], period)
    back_cos = jnp.cos(back_twist)[:, :, None]
    back_sin = jnp.sin(back_twist)[:, :, None]

    def to_modes(column):
        real_part = exact_dot("kq,qgc->kgc", cos_q, column)
        imag_part = -exact_dot("kq,qgc->kgc", sin_q, column)
        return jnp.stack(
            [
                real_part * twist_cos + imag_part * twist_sin,
                imag_part * twist_cos - real_part * twist_sin,
            ]
        )

    def to_spectrum(spread):
        real_part = exact_dot("ki,jic->jkc", cos_m, spread[0]) + exact_dot(
            "ki,jic->jkc", sin_m, spread[1]
        )
        imag_part = exact_dot("ki,jic->jkc", cos_m, spread[1]) - exact_dot(
            "ki,jic->jkc", sin_m, spread[0]
        )
        return (real_part, imag_part)

    blocks_here = row_count // BLK
    flat_ids = prefix_blocks.reshape(-1)
    first_block = jnp.minimum(seq_index * blocks_here, flat_ids.shape[0] - blocks_here)
    own_ids = lax.dynamic_slice_in_dim(flat_ids, first_block, blocks_here)
    matches = own_ids[:, None] == jnp.arange(block_slot.shape[0], dtype=jnp.int32)[None, :]
    wanted = jnp.sum(jnp.where(matches, block_slot[None, :], 0), axis=1)
    shards = lax.all_gather(library, "seq", axis=0, tiled=True)
    picker = (wanted[:, None] == jnp.arange(shards.shape[0], dtype=jnp.int32)[None, :]).astype(
        jnp.bfloat16
    )
    gathered = jnp.einsum("bn,nlc->blc", picker, shards, preferred_element_type=jnp.float32)
    cached = gathered.reshape(row_count, channels).astype(jnp.bfloat16)
    values = jnp.where(seq_index < devices // 4, cached, fresh[:, 2])
    stacked = jnp.concatenate([fresh[:, :2], values[:, None]], axis=1)
    previous = from_behind(stacked[row_count - (TAPS - 1) :], "seq", 1)
    extended = jnp.concatenate([previous, stacked], axis=0)
    shortened = jnp.zeros((row_count, 3, channels), jnp.float32)
    for offset in range(TAPS):
        window_start = TAPS - 1 - offset
        shortened = shortened + short_taps[offset][None] * extended[
            window_start : window_start + row_count
        ].astype(jnp.float32)
    gating = shortened[:, 0]
    signal = shortened[:, 1] * shortened[:, 2]
    spread_signal = to_modes(
        lax.all_to_all(signal[None], "seq", split_axis=1, concat_axis=0, tiled=True)
    )
    spread_taps = to_modes(
        lax.all_to_all(long_filter[None], "seq", split_axis=1, concat_axis=0, tiled=True)
    )
    moved_signal, moved_taps = (
        lax.all_to_all(
            spread_signal.astype(jnp.bfloat16), "seq", split_axis=1, concat_axis=2, tiled=True
        ).astype(spread_signal.dtype),
        lax.all_to_all(
            spread_taps.astype(jnp.bfloat16), "seq", split_axis=1, concat_axis=2, tiled=True
        ).astype(spread_taps.dtype),
    )
    sig_real, sig_imag = to_spectrum(moved_signal)
    tap_real, tap_imag = to_spectrum(moved_taps)
    prod_real = sig_real * tap_real - sig_imag * tap_imag
    prod_imag = sig_real * tap_imag + sig_imag * tap_real
    back_real = exact_dot("ki,jic->jkc", cos_m, prod_real) - exact_dot(
        "ki,jic->jkc", sin_m, prod_imag
    )
    back_imag = exact_dot("ki,jic->jkc", cos_m, prod_imag) + exact_dot(
        "ki,jic->jkc", sin_m, prod_real
    )
    turned = jnp.stack(
        [back_real * back_cos - back_imag * back_sin, back_imag * back_cos + back_real * back_sin]
    )
    spread = lax.all_to_all(turned, "seq", split_axis=2, concat_axis=1, tiled=True)
    positions = (
        exact_dot("kq,kgc->qgc", cos_q, spread[0]) - exact_dot("kq,kgc->qgc", sin_q, spread[1])
    ) / period
    convolved = lax.all_to_all(positions, "seq", split_axis=0, concat_axis=1, tiled=True)[0]
    output = gating * (convolved + skip_gain[None, :] * signal)
    return output.astype(jnp.bfloat16)


def exchange(chunk_of, devices, rider=None, finish=None):
    seq_index = lax.axis_index("seq")
    arrived = []
    carried = None
    for shift in range(devices):
        block = chunk_of(lax.rem(seq_index + shift, devices))
        if shift == 1 and rider is not None:
            size = block.shape[0]
            block = jnp.concatenate([block, rider], axis=0)
            block = lax.ppermute(
                block, "seq", [(i, (i + shift) % devices) for i in range(devices)]
            )
            carried = block[size:]
            arrived.append(block[:size])
            continue
        if shift:
            block = lax.ppermute(
                block, "seq", [(i, (i + shift) % devices) for i in range(devices)]
            )
        if finish is not None:
            block = finish(block, lax.rem(seq_index - shift + devices, devices))
        arrived.append(block)
    turned = jnp.stack(arrived[::-1] * 2)
    start = lax.rem(devices - 1 - seq_index + devices, devices)
    ordered = lax.dynamic_slice_in_dim(turned, start, devices, axis=0)
    if rider is None:
        return ordered
    return ordered, carried


def dft_tables(tokens):
    period = 2 * tokens
    width = 1
    while width * width < tokens:
        width *= 2
    outer = tokens // width
    freqs = jnp.arange(tokens + 1, dtype=jnp.int32)[:, None]
    coarse = turn_angles(freqs * (width * jnp.arange(outer, dtype=jnp.int32))[None, :], period)
    fine = turn_angles(freqs * jnp.arange(width, dtype=jnp.int32)[None, :], period)
    c1, s1 = jnp.cos(coarse)[:, :, None], jnp.sin(coarse)[:, :, None]
    c2, s2 = jnp.cos(fine)[:, None, :], jnp.sin(fine)[:, None, :]
    cos_t = (c1 * c2 - s1 * s2).reshape(tokens + 1, tokens)
    sin_t = (s1 * c2 + c1 * s2).reshape(tokens + 1, tokens)
    return cos_t, sin_t


def local_body(fresh, library, block_slot, prefix_blocks, short_taps, long_filter, skip_gain):
    row_count, _, channels = fresh.shape
    devices = lax.axis_size("seq")
    seq_index = lax.axis_index("seq")
    tokens = row_count * devices
    own = channels // devices
    lib_here = library.shape[0]
    lib_flat = library.reshape(lib_here * BLK, channels)
    lib_rows = -(-lib_here * BLK // 3)
    lib_flat = jnp.pad(lib_flat, ((0, 3 * lib_rows - lib_here * BLK), (0, 0)))
    lib_packed = lib_flat.reshape(lib_rows, 3, channels)

    def chunk_for(d):
        start = d * own
        streams = lax.dynamic_slice_in_dim(fresh[:, 1:], start, own, axis=2)
        taps_here = lax.dynamic_slice_in_dim(long_filter, start, own, axis=1)
        lib_here_rows = lax.dynamic_slice_in_dim(lib_packed, start, own, axis=2)
        block = jnp.concatenate([streams, taps_here.astype(jnp.bfloat16)[:, None, :]], axis=1)
        return jnp.concatenate([block, lib_here_rows], axis=0)

    halo = fresh[row_count - (TAPS - 1) :, 0].reshape(-1)
    halo_rows = -(-halo.shape[0] // (3 * own))
    halo = jnp.pad(halo, (0, halo_rows * 3 * own - halo.shape[0])).reshape(halo_rows, 3, own)
    moved, halo = exchange(chunk_for, devices, halo)
    halo = halo.reshape(-1)[: (TAPS - 1) * channels].reshape(TAPS - 1, channels)
    rows = moved[:, :row_count].reshape(tokens, 3, own)
    lib_all = moved[:, row_count:].reshape(devices, 3 * lib_rows, own)[:, : lib_here * BLK]
    lib_all = lib_all.reshape(devices * lib_here, BLK * own)

    gate_in = fresh[:, 0].astype(jnp.float32)
    gate_prev = jnp.where(seq_index > 0, halo.astype(jnp.float32), 0.0)
    gate_ext = jnp.concatenate([gate_prev, gate_in], axis=0)
    gating = jnp.zeros((row_count, channels), jnp.float32)
    for offset in range(TAPS):
        window_start = TAPS - 1 - offset
        gating = gating + short_taps[offset, 0][None] * gate_ext[
            window_start : window_start + row_count
        ]

    slot_ids = block_slot[prefix_blocks.reshape(-1)]
    prefix_len = slot_ids.shape[0] * BLK
    picker = (slot_ids[:, None] == jnp.arange(lib_all.shape[0], dtype=jnp.int32)[None, :]).astype(
        jnp.bfloat16
    )
    cached = jnp.dot(picker, lib_all, preferred_element_type=jnp.float32)
    cached = cached.reshape(prefix_len, own).astype(jnp.bfloat16)
    values = jnp.concatenate([cached, rows[prefix_len:, 1]], axis=0)
    stacked = jnp.stack([rows[:, 0], values], axis=1).astype(jnp.float32)

    taps = lax.dynamic_slice_in_dim(short_taps[:, 1:], seq_index * own, own, axis=2)
    gain = lax.dynamic_slice_in_dim(skip_gain, seq_index * own, own, axis=0)
    shortened = jnp.zeros((tokens, 2, own), jnp.float32)
    for offset in range(TAPS):
        shifted = jnp.pad(stacked[: tokens - offset], ((offset, 0), (0, 0), (0, 0)))
        shortened = shortened + taps[offset][None] * shifted
    signal = shortened[:, 0] * shortened[:, 1]

    cos_t, sin_t = dft_tables(tokens)
    table = jnp.concatenate([cos_t, sin_t], axis=0).astype(jnp.bfloat16)
    operands = jnp.concatenate([signal.astype(jnp.bfloat16), rows[:, 2]], axis=1)
    spec = jnp.dot(table, operands, preferred_element_type=jnp.float32)
    bins = tokens + 1
    sig_c, tap_c = spec[:bins, :own], spec[:bins, own:]
    sig_s, tap_s = spec[bins:, :own], spec[bins:, own:]
    weight = jnp.where(
        (jnp.arange(bins) == 0) | (jnp.arange(bins) == tokens), 1.0, 2.0
    ).astype(jnp.float32)[:, None] / (2 * tokens)
    real = (sig_c * tap_c - sig_s * tap_s) * weight
    turned = (sig_c * tap_s + sig_s * tap_c) * weight
    back = jnp.concatenate([real, turned], axis=0).astype(jnp.bfloat16)
    convolved = lax.dot_general(
        table, back, (((0,), (0,)), ((), ())), preferred_element_type=jnp.float32
    )
    summed = (convolved + gain[None, :] * signal).astype(jnp.bfloat16)
    def gated(block, source):
        gate = lax.dynamic_slice_in_dim(gating, source * own, own, axis=1)
        return (gate * block.astype(jnp.float32)).astype(jnp.bfloat16)

    summed = exchange(
        lambda d: lax.dynamic_slice_in_dim(summed, d * row_count, row_count, axis=0),
        devices,
        finish=gated,
    )
    return summed.transpose(1, 0, 2).reshape(row_count, channels)


def body(fresh, library, *rest):
    devices = lax.axis_size("seq")
    tokens = fresh.shape[0] * devices
    fits = tokens <= 4096 and fresh.shape[2] % devices == 0
    if fits:
        return local_body(fresh, library, *rest)
    return ring_body(fresh, library, *rest)


def solution(mesh):
    return jax.shard_map(
        body,
        mesh=mesh,
        in_specs=(
            P(("group", "seq"), None, "chan"),
            P("seq", None, "chan"),
            P(),
            P("group", None),
            P(None, None, "chan"),
            P("seq", "chan"),
            P("chan"),
        ),
        out_specs=P(("group", "seq"), "chan"),
        check_vma=False,
    )
```
